32 devices in a mesh: tm: 8 (over z, x), state: 4 (over y, core).
Axes of the slice: x: 2, y: 2, z: 4, core: 2. Of those that a mesh axis runs over, the one named last changes fastest.
Arguments:
- obs: bfloat16 [2048, 16, 256], P(('state', 'tm')), may hold values from -6 to 6
- mask: int32 [2048, 16], P(('state', 'tm')), may hold values 0 or 1
- loadings: bfloat16 [2048, 2048], P('state'), may hold values from -0.125 to 0.125
- decay: float32 [16, 2048], P('tm', 'state'), may hold values from 0 to 1, as said below
Outputs:
- smoothed: float32 [2048, 16, 256], P('state', 'tm')
- residual: float32 [2048, 16, 256], P('state', 'tm')
The draws below stay inside these ranges and needn't reach their ends.
Inputs may be any that keep to these rules, and one draw needn't show every extreme that they name: Every decay lies strictly between 0 and 1.
All inputs are finite; a program needn't handle non-finite values. No bound on the sum of `mask` on one device may be relied on, other than what follows from the above.
Results may differ from the reference program's by a relative error of at most 0.0021.
Values may be sent and summed in bfloat16 or wider, within the bound.
No kernel may reach another device: no remote copies, remote signals or barrier semaphores. Data moves between devices by JAX's collectives and lax.ppermute only.
A program may use at most 64 MiB of HBM per device.

```python
import jax
import jax.numpy as jnp
from jax import lax

S = 2048
NSTAT = 2048
R = 256
WINDOW_HOURS = 16


def draw_decay(key, part):
    random_key_list = jax.random.split(jax.random.fold_in(key, 17), 4)
    lowest = 4.0
    highest = 16.0 * WINDOW_HOURS
    lifetime = jnp.exp(jax.random.uniform(random_key_list[0], (S,), jnp.float32, jnp.log(lowest), jnp.log(highest)))
    baseline_rate = jnp.exp(-1.0 / lifetime)
    random_noise = jax.random.uniform(random_key_list[1], (WINDOW_HOURS, S), jnp.float32, 0.99, 1.0)
    spike_events = jax.random.uniform(random_key_list[2], (WINDOW_HOURS, 1), jnp.float32) < 0.06
    scale_multiplier = jax.random.uniform(random_key_list[3], (WINDOW_HOURS, 1), jnp.float32, 0.5, 0.8)
    spike_multiplier = jnp.where(spike_events, scale_multiplier, 1.0)
    return (baseline_rate[None, :] * random_noise * spike_multiplier).astype(jnp.float32)


def touch_ends(result, stream_key, least, high):
    spot = [jax.random.randint(jax.random.fold_in(stream_key, axis), (), 0, length) for axis, length in enumerate(result.shape)]
    main_axis = result.shape.index(max(result.shape))
    neighbour = spot[:main_axis] + [(spot[main_axis] + 1) % result.shape[main_axis]] + spot[main_axis + 1:]
    return result.at[tuple(spot)].set(least).at[tuple(neighbour)].set(high)


def steps_of(rng, extent, pieces, least, top_value):
    factor_of, own = 1.0, jax.random.fold_in(rng, 6)
    for dim, parts in pieces:
        heights = jnp.exp(jax.random.uniform(jax.random.fold_in(own, dim), (parts,), jnp.float32, least / len(pieces), top_value / len(pieces)))
        factor_of = factor_of * jnp.repeat(heights, extent[dim] // parts).reshape([-1 if axis == dim else 1 for axis in range(len(extent))])
    return factor_of


def gaussian(key, extent, width, limit, cuts=(), kind=jnp.bfloat16):
    gain = steps_of(key, extent, cuts, -0.22, 0.18) if cuts else 1.0
    array = jax.random.normal(key, extent, jnp.float32) * width * gain
    return jnp.minimum(jnp.maximum(array, -limit), limit).astype(kind)


def setup_inputs(seed: int = 0) -> dict:
    splits = jax.random.split(jax.random.key(seed), 5)
    obs = gaussian(splits[0], (NSTAT, WINDOW_HOURS, R), 1.0, 6.0, ((0, 32),))
    mask = touch_ends((jax.random.randint(splits[1], (NSTAT, WINDOW_HOURS), 0, 4) < 3).astype(jnp.int32), jax.random.fold_in(splits[1], 1), 0, 1)
    loadings = gaussian(splits[2], (NSTAT, S), NSTAT ** -0.5, 0.125, ((0, 4),))
    decay = draw_decay(jax.random.fold_in(splits[4], 71), 0)
    return dict(obs=obs, mask=mask, loadings=loadings, decay=decay)


def reference(obs, mask, loadings, decay):
    masked = obs * mask[:, :, None].astype(jnp.bfloat16)
    hours_first = jnp.transpose(masked, (1, 0, 2))
    zero_state = jnp.zeros((S, R), jnp.float32)

    def forward(carried, inputs):
        decay_row, reading = inputs
        information = jnp.dot(loadings.T, reading, preferred_element_type=jnp.float32)
        carried = decay_row[:, None] * carried + information
        return carried, carried

    _, filtered = lax.scan(forward, zero_state, (decay, hours_first))

    def backward(carried, inputs):
        decay_row, filtered_row, reading = inputs
        carried = decay_row[:, None] * carried + (1.0 - decay_row * decay_row)[:, None] * filtered_row
        rounded = carried.astype(jnp.bfloat16)
        predicted = jnp.dot(loadings, rounded, preferred_element_type=jnp.float32)
        return carried, (carried, reading.astype(jnp.float32) - predicted)

    _, (smoothed, residual) = lax.scan(backward, zero_state, (decay, filtered, hours_first), reverse=True)
    return jnp.transpose(smoothed, (1, 0, 2)), jnp.transpose(residual, (1, 0, 2))
```

```python
import jax
import jax.numpy as jnp
from jax import lax
from jax.sharding import PartitionSpec as P


def local(obs, mask, loadings, decay):
    tm_count = lax.axis_size("tm")
    _, hours, members = obs.shape
    members_here = members // tm_count
    masked = obs * mask[:, :, None].astype(obs.dtype)
    by_member = lax.all_to_all(masked, "tm", split_axis=2, concat_axis=0, tiled=True)
    by_hour = lax.all_to_all(masked, "tm", split_axis=1, concat_axis=0, tiled=True)
    stations_here = by_member.shape[0]
    partial = jnp.dot(
        loadings.T,
        by_member.reshape(stations_here, hours * members_here),
        preferred_element_type=jnp.float32,
    )
    information = lax.psum_scatter(partial, "state", scatter_dimension=0, tiled=True)
    comps = information.shape[0]
    information = information.reshape(comps, hours, members_here)
    decay_all = lax.all_gather(decay, "tm", axis=0, tiled=True)
    state = jnp.zeros((comps, members_here), jnp.float32)
    filtered = []
    for hour in range(hours):
        state = decay_all[hour][:, None] * state + information[:, hour, :]
        filtered.append(state)
    state = jnp.zeros((comps, members_here), jnp.float32)
    smoothed_rows = [None] * hours
    for hour in reversed(range(hours)):
        rate = decay_all[hour]
        state = rate[:, None] * state + (1.0 - rate * rate)[:, None] * filtered[hour]
        smoothed_rows[hour] = state
    smoothed_here = jnp.stack(smoothed_rows, axis=1)
    smoothed = lax.all_to_all(smoothed_here, "tm", split_axis=1, concat_axis=2, tiled=True)
    rounded = smoothed.astype(jnp.bfloat16)
    fitted = jnp.einsum(
        "so,ogy->sgy",
        loadings,
        lax.all_gather(rounded, "state", axis=0, tiled=True),
        preferred_element_type=jnp.float32,
    )
    residual = by_hour.astype(jnp.float32) - fitted
    return (smoothed, residual)


def solution(mesh):
    return jax.shard_map(
        local,
        mesh=mesh,
        in_specs=(
            P(("state", "tm"), None, None),
            P(("state", "tm"), None),
            P("state", None),
            P("tm", "state"),
        ),
        out_specs=(P("state", "tm", None), P("state", "tm", None)),
        check_vma=False,
    )
```

```python
import jax
import jax.numpy as jnp
from jax import lax
from jax.sharding import PartitionSpec as P

CHUNKS = 2


def smooth_chunk(information, decay_all):
    comps, hours, width = information.shape
    state = jnp.zeros((comps, width), jnp.float32)
    filtered = []
    for hour in range(hours):
        state = decay_all[hour][:, None] * state + information[:, hour, :]
        filtered.append(state)
    state = jnp.zeros((comps, width), jnp.float32)
    rows = [None] * hours
    for hour in reversed(range(hours)):
        rate = decay_all[hour]
        state = rate[:, None] * state + (1.0 - rate * rate)[:, None] * filtered[hour]
        rows[hour] = state
    return jnp.stack(rows, axis=1)


def local(obs, mask, loadings, decay):
    tm_count = lax.axis_size("tm")
    tm_index = lax.axis_index("tm")
    _, hours, members = obs.shape
    chunk_members = members // CHUNKS
    masked = obs * mask[:, :, None].astype(obs.dtype)
    by_hour = lax.all_to_all(masked, "tm", split_axis=1, concat_axis=0, tiled=True)
    slab_hours, comps = decay.shape
    padded = jnp.zeros((tm_count, slab_hours, comps), jnp.float32)
    padded = lax.dynamic_update_slice(padded, decay[None], (tm_index, 0, 0))
    decay_all = lax.psum(padded, "tm").reshape(tm_count * slab_hours, comps)
    smoothed_parts = []
    residual_parts = []
    for chunk in range(CHUNKS):
        low = chunk * chunk_members
        piece = masked[:, :, low:low + chunk_members]
        by_member = lax.all_to_all(piece, "tm", split_axis=2, concat_axis=0, tiled=True)
        stations_here, _, width = by_member.shape
        partial = jnp.dot(
            loadings.T,
            by_member.reshape(stations_here, hours * width),
            preferred_element_type=jnp.float32,
        )
        information = lax.psum_scatter(partial, "state", scatter_dimension=0, tiled=True)
        information = information.reshape(information.shape[0], hours, width)
        smoothed_here = smooth_chunk(information, decay_all)
        smoothed = lax.all_to_all(smoothed_here, "tm", split_axis=1, concat_axis=2, tiled=True)
        rounded = smoothed.astype(jnp.bfloat16)
        fitted = jnp.einsum(
            "so,ogy->sgy",
            loadings,
            lax.all_gather(rounded, "state", axis=0, tiled=True),
            preferred_element_type=jnp.float32,
        )
        residual = by_hour[:, :, low:low + chunk_members].astype(jnp.float32) - fitted
        smoothed_parts.append(smoothed)
        residual_parts.append(residual)
    return (
        jnp.concatenate(smoothed_parts, axis=2),
        jnp.concatenate(residual_parts, axis=2),
    )


def solution(mesh):
    return jax.shard_map(
        local,
        mesh=mesh,
        in_specs=(
            P(("state", "tm"), None, None),
            P(("state", "tm"), None),
            P("state", None),
            P("tm", "state"),
        ),
        out_specs=(P("state", "tm", None), P("state", "tm", None)),
        check_vma=False,
    )
```

```python
import jax
import jax.numpy as jnp
from jax import lax
from jax.experimental import pallas as pl
from jax.experimental.pallas import tpu as pltpu
from jax.sharding import PartitionSpec as P

CHUNKS = 2
LANES = 128


def recurrence_kernel(rate_ref, info_ref, out_ref):
    hours = info_ref.shape[0]
    state = jnp.zeros(info_ref.shape[1:], jnp.float32)
    for hour in range(hours):
        state = rate_ref[hour] * state + info_ref[hour]
        out_ref[hour] = state
    state = jnp.zeros(info_ref.shape[1:], jnp.float32)
    for hour in reversed(range(hours)):
        rate = rate_ref[hour]
        state = rate * state + (1.0 - rate * rate) * out_ref[hour]
        out_ref[hour] = state


def run_recurrence(rates, information):
    return pl.pallas_call(
        recurrence_kernel,
        out_shape=jax.ShapeDtypeStruct(information.shape, jnp.float32),
        in_specs=[pl.BlockSpec(memory_space=pltpu.VMEM)] * 2,
        out_specs=pl.BlockSpec(memory_space=pltpu.VMEM),
    )(rates, information)


def smooth_chunk(information, decay_all):
    comps, hours, width = information.shape
    hours_first = jnp.transpose(information, (1, 0, 2))
    rates = jnp.broadcast_to(decay_all[:, :, None], (hours, comps, width))
    if (comps * width) % LANES == 0:
        dense = (hours, comps * width // LANES, LANES)
        out = run_recurrence(rates.reshape(dense), hours_first.reshape(dense))
    else:
        out = run_recurrence(rates, hours_first)
    return jnp.transpose(out.reshape(hours, comps, width), (1, 0, 2))


def local(obs, mask, loadings, decay):
    tm_count = lax.axis_size("tm")
    _, hours, members = obs.shape
    chunk_members = members // CHUNKS
    masked = obs * mask[:, :, None].astype(obs.dtype)
    copies = jnp.broadcast_to(decay[None], (tm_count,) + decay.shape)
    decay_all = lax.all_to_all(copies, "tm", split_axis=0, concat_axis=0, tiled=True)
    decay_all = decay_all.reshape(hours, decay.shape[1])
    by_hour = lax.all_to_all(masked, "tm", split_axis=1, concat_axis=0, tiled=True)
    smoothed_parts = []
    residual_parts = []
    for chunk in range(CHUNKS):
        low = chunk * chunk_members
        piece = masked[:, :, low:low + chunk_members]
        by_member = lax.all_to_all(piece, "tm", split_axis=2, concat_axis=0, tiled=True)
        stations_here, _, width = by_member.shape
        partial = jnp.dot(
            loadings.T,
            by_member.reshape(stations_here, hours * width),
            preferred_element_type=jnp.float32,
        )
        information = lax.psum_scatter(partial, "state", scatter_dimension=0, tiled=True)
        information = information.reshape(information.shape[0], hours, width)
        smoothed_here = smooth_chunk(information, decay_all)
        smoothed = lax.all_to_all(smoothed_here, "tm", split_axis=1, concat_axis=2, tiled=True)
        rounded = smoothed.astype(jnp.bfloat16)
        fitted = jnp.einsum(
            "so,ogy->sgy",
            loadings,
            lax.all_gather(rounded, "state", axis=0, tiled=True),
            preferred_element_type=jnp.float32,
        )
        residual = by_hour[:, :, low:low + chunk_members].astype(jnp.float32) - fitted
        smoothed_parts.append(smoothed)
        residual_parts.append(residual)
    return (
        jnp.concatenate(smoothed_parts, axis=2),
        jnp.concatenate(residual_parts, axis=2),
    )


def solution(mesh):
    return jax.shard_map(
        local,
        mesh=mesh,
        in_specs=(
            P(("state", "tm"), None, None),
            P(("state", "tm"), None),
            P("state", None),
            P("tm", "state"),
        ),
        out_specs=(P("state", "tm", None), P("state", "tm", None)),
        check_vma=False,
    )
```

```python
import jax
import jax.numpy as jnp
from jax import lax
from jax.sharding import PartitionSpec as P


def local(obs, mask, loadings, decay):
    tm_count = lax.axis_size("tm")
    stations_local, hours, members = obs.shape
    members_here = members // tm_count
    hours_here = hours // tm_count
    masked = obs * mask[:, :, None].astype(obs.dtype)
    outgoing = jnp.transpose(
        masked.reshape(stations_local, hours, tm_count, members_here), (2, 0, 1, 3)
    )
    by_member = lax.all_to_all(outgoing, "tm", split_axis=0, concat_axis=0, tiled=True)
    stations_here = tm_count * stations_local
    by_member = by_member.reshape(stations_here, hours * members_here)
    outgoing = jnp.transpose(
        masked.reshape(stations_local, tm_count, hours_here, members), (1, 0, 2, 3)
    )
    by_hour = lax.all_to_all(outgoing, "tm", split_axis=0, concat_axis=0, tiled=True)
    by_hour = by_hour.reshape(stations_here, hours_here, members)
    copies = jnp.broadcast_to(decay[None], (tm_count,) + decay.shape)
    decay_all = lax.all_to_all(copies, "tm", split_axis=0, concat_axis=0, tiled=True)
    decay_all = decay_all.reshape(hours, decay.shape[1])
    partial = jnp.dot(loadings.T, by_member, preferred_element_type=jnp.float32)
    information = lax.psum_scatter(partial, "state", scatter_dimension=0, tiled=True)
    comps = information.shape[0]
    information = information.reshape(comps, hours, members_here)
    state = jnp.zeros((comps, members_here), jnp.float32)
    filtered = []
    for hour in range(hours):
        state = decay_all[hour][:, None] * state + information[:, hour, :]
        filtered.append(state)
    state = jnp.zeros((comps, members_here), jnp.float32)
    smoothed_rows = [None] * hours
    for hour in reversed(range(hours)):
        rate = decay_all[hour]
        state = rate[:, None] * state + (1.0 - rate * rate)[:, None] * filtered[hour]
        smoothed_rows[hour] = state
    smoothed_here = jnp.stack(smoothed_rows, axis=1)
    smoothed = lax.all_to_all(smoothed_here, "tm", split_axis=1, concat_axis=2, tiled=True)
    rounded = smoothed.astype(jnp.bfloat16)
    fitted = jnp.einsum(
        "so,ogy->sgy",
        loadings,
        lax.all_gather(rounded, "state", axis=0, tiled=True),
        preferred_element_type=jnp.float32,
    )
    residual = by_hour.astype(jnp.float32) - fitted
    return (smoothed, residual)


def solution(mesh):
    return jax.shard_map(
        local,
        mesh=mesh,
        in_specs=(
            P(("state", "tm"), None, None),
            P(("state", "tm"), None),
            P("state", None),
            P("tm", "state"),
        ),
        out_specs=(P("state", "tm", None), P("state", "tm", None)),
        check_vma=False,
    )
```

```python
import jax
import jax.numpy as jnp
from jax import lax
from jax.experimental import pallas as pl
from jax.experimental.pallas import tpu as pltpu
from jax.sharding import PartitionSpec as P


def information_kernel(x_ref, l_ref, out_ref):
    out_ref[...] = lax.dot_general(
        x_ref[...], l_ref[...], (((0,), (0,)), ((), ())),
        preferred_element_type=jnp.float32,
    )


def recurrence_kernel(rate_ref, info_ref, out_ref):
    hours = info_ref.shape[0]
    state = jnp.zeros(info_ref.shape[1:], jnp.float32)
    for hour in range(hours):
        state = rate_ref[pl.ds(hour, 1), :] * state + info_ref[hour]
        out_ref[hour] = state
    state = jnp.zeros(info_ref.shape[1:], jnp.float32)
    for hour in reversed(range(hours)):
        rate = rate_ref[pl.ds(hour, 1), :]
        state = rate * state + (1.0 - rate * rate) * out_ref[hour]
        out_ref[hour] = state


def vmem_call(kernel, out_shape, count, cost):
    return pl.pallas_call(
        kernel,
        out_shape=out_shape,
        in_specs=[pl.BlockSpec(memory_space=pltpu.VMEM)] * count,
        out_specs=pl.BlockSpec(memory_space=pltpu.VMEM),
        cost_estimate=cost,
    )


def local(obs, mask, loadings, decay):
    tm_count = lax.axis_size("tm")
    stations_local, hours, members = obs.shape
    members_here = members // tm_count
    masked = obs * mask[:, :, None].astype(obs.dtype)
    outgoing = jnp.transpose(
        masked.reshape(stations_local, hours, tm_count, members_here), (2, 0, 1, 3)
    ).reshape(tm_count, stations_local, hours * members_here)
    by_member = lax.all_to_all(outgoing, "tm", split_axis=0, concat_axis=0, tiled=True)
    stations_here = tm_count * stations_local
    by_member = by_member.reshape(stations_here, hours * members_here)
    by_hour = lax.all_to_all(masked, "tm", split_axis=1, concat_axis=0, tiled=True)
    copies = jnp.broadcast_to(decay[None], (tm_count,) + decay.shape)
    decay_all = lax.all_to_all(copies, "tm", split_axis=0, concat_axis=0, tiled=True)
    decay_all = decay_all.reshape(hours, decay.shape[1])
    all_comps = loadings.shape[1]
    columns = hours * members_here
    partial = vmem_call(
        information_kernel,
        jax.ShapeDtypeStruct((columns, all_comps), jnp.float32),
        2,
        pl.CostEstimate(
            flops=2 * stations_here * columns * all_comps,
            bytes_accessed=2 * stations_here * (columns + all_comps) + 4 * columns * all_comps,
            transcendentals=0,
        ),
    )(by_member, loadings)
    information = lax.psum_scatter(partial, "state", scatter_dimension=1, tiled=True)
    comps = information.shape[1]
    information = information.reshape(hours, members_here, comps)
    smoothed_here = vmem_call(
        recurrence_kernel,
        jax.ShapeDtypeStruct(information.shape, jnp.float32),
        2,
        pl.CostEstimate(
            flops=5 * hours * members_here * comps,
            bytes_accessed=8 * hours * members_here * comps,
            transcendentals=0,
        ),
    )(decay_all, information)
    gathered = lax.all_to_all(smoothed_here, "tm", split_axis=0, concat_axis=1, tiled=True)
    rounded = gathered.astype(jnp.bfloat16)
    full = lax.all_gather(rounded, "state", axis=2, tiled=True)
    fitted = jnp.einsum("so,gyo->sgy", loadings, full, preferred_element_type=jnp.float32)
    residual = by_hour.astype(jnp.float32) - fitted
    smoothed = jnp.transpose(gathered, (2, 0, 1))
    return (smoothed, residual)


def solution(mesh):
    return jax.shard_map(
        local,
        mesh=mesh,
        in_specs=(
            P(("state", "tm"), None, None),
            P(("state", "tm"), None),
            P("state", None),
            P("tm", "state"),
        ),
        out_specs=(P("state", "tm", None), P("state", "tm", None)),
        check_vma=False,
    )
```

```python
import jax
import jax.numpy as jnp
from jax import lax
from jax.experimental import pallas as pl
from jax.experimental.pallas import tpu as pltpu
from jax.sharding import PartitionSpec as P


def information_kernel(x_ref, l_ref, out_ref):
    total = lax.dot_general(
        x_ref[...], l_ref[...], (((0,), (0,)), ((), ())),
        preferred_element_type=jnp.float32,
    )
    levels = out_ref.ndim - 2
    width = out_ref.shape[-1]
    for block in range(2 ** levels):
        bits = tuple((block >> level) & 1 for level in range(levels))
        out_ref[bits] = total[:, block * width:(block + 1) * width]


def halving_reduce(blocks, axis):
    count = lax.axis_size(axis)
    me = lax.axis_index(axis)
    level = 0
    while blocks.ndim > 2:
        bit = (me >> level) & 1
        keep = jnp.where(bit == 0, blocks[0], blocks[1])
        send = jnp.where(bit == 0, blocks[1], blocks[0])
        pairs = [(i, i ^ (1 << level)) for i in range(count)]
        blocks = keep + lax.ppermute(send, axis, pairs)
        level += 1
    return blocks


def recurrence_kernel(rate_ref, info_ref, out_ref):
    hours = info_ref.shape[0]
    state = jnp.zeros(info_ref.shape[1:], jnp.float32)
    for hour in range(hours):
        state = rate_ref[pl.ds(hour, 1), :] * state + info_ref[hour]
        out_ref[hour] = state
    state = jnp.zeros(info_ref.shape[1:], jnp.float32)
    for hour in reversed(range(hours)):
        rate = rate_ref[pl.ds(hour, 1), :]
        state = rate * state + (1.0 - rate * rate) * out_ref[hour]
        out_ref[hour] = state


def vmem_call(kernel, out_shape, count, cost):
    return pl.pallas_call(
        kernel,
        out_shape=out_shape,
        in_specs=[pl.BlockSpec(memory_space=pltpu.VMEM)] * count,
        out_specs=pl.BlockSpec(memory_space=pltpu.VMEM),
        cost_estimate=cost,
    )


def local(obs, mask, loadings, decay):
    tm_count = lax.axis_size("tm")
    stations_local, hours, members = obs.shape
    members_here = members // tm_count
    masked = obs * mask[:, :, None].astype(obs.dtype)
    outgoing = jnp.transpose(
        masked.reshape(stations_local, hours, tm_count, members_here), (2, 0, 1, 3)
    ).reshape(tm_count, stations_local, hours * members_here)
    by_member = lax.all_to_all(outgoing, "tm", split_axis=0, concat_axis=0, tiled=True)
    stations_here = tm_count * stations_local
    by_member = by_member.reshape(stations_here, hours * members_here)
    by_hour = lax.all_to_all(masked, "tm", split_axis=1, concat_axis=0, tiled=True)
    copies = jnp.broadcast_to(decay[None], (tm_count,) + decay.shape)
    decay_all = lax.all_to_all(copies, "tm", split_axis=0, concat_axis=0, tiled=True)
    decay_all = decay_all.reshape(hours, decay.shape[1])
    all_comps = loadings.shape[1]
    columns = hours * members_here
    state_count = lax.axis_size("state")
    levels = state_count.bit_length() - 1
    partial = vmem_call(
        information_kernel,
        jax.ShapeDtypeStruct(
            (2,) * levels + (columns, all_comps // state_count), jnp.float32
        ),
        2,
        pl.CostEstimate(
            flops=2 * stations_here * columns * all_comps,
            bytes_accessed=2 * stations_here * (columns + all_comps) + 4 * columns * all_comps,
            transcendentals=0,
        ),
    )(by_member, loadings)
    information = halving_reduce(partial, "state")
    comps = information.shape[1]
    information = information.reshape(hours, members_here, comps)
    smoothed_here = vmem_call(
        recurrence_kernel,
        jax.ShapeDtypeStruct(information.shape, jnp.float32),
        2,
        pl.CostEstimate(
            flops=5 * hours * members_here * comps,
            bytes_accessed=8 * hours * members_here * comps,
            transcendentals=0,
        ),
    )(decay_all, information)
    gathered = lax.all_to_all(smoothed_here, "tm", split_axis=0, concat_axis=1, tiled=True)
    rounded = gathered.astype(jnp.bfloat16)
    full = lax.all_gather(rounded, "state", axis=2, tiled=True)
    fitted = jnp.einsum("so,gyo->sgy", loadings, full, preferred_element_type=jnp.float32)
    residual = by_hour.astype(jnp.float32) - fitted
    smoothed = jnp.transpose(gathered, (2, 0, 1))
    return (smoothed, residual)


def solution(mesh):
    return jax.shard_map(
        local,
        mesh=mesh,
        in_specs=(
            P(("state", "tm"), None, None),
            P(("state", "tm"), None),
            P("state", None),
            P("tm", "state"),
        ),
        out_specs=(P("state", "tm", None), P("state", "tm", None)),
        check_vma=False,
    )
```

```python
import jax
import jax.numpy as jnp
from jax import lax
from jax.experimental import pallas as pl
from jax.experimental.pallas import tpu as pltpu
from jax.sharding import PartitionSpec as P


def information_kernel(me_ref, x_ref, l_ref, send_ref, keep_ref):
    me = me_ref[0]
    levels = send_ref.ndim - 1
    width = send_ref.shape[-1]
    flipped = x_ref[...].T
    for slot in range(2 ** levels):
        relative = tuple((slot >> level) & 1 for level in range(levels))
        block = 0
        for level in range(levels):
            block = block + ((relative[level] ^ ((me >> level) & 1) ^ 1) << level)
        columns = l_ref[:, pl.ds(pl.multiple_of(block * width, width), width)]
        target = keep_ref if relative[0] else send_ref
        target[relative[1:]] = jnp.dot(flipped, columns, preferred_element_type=jnp.float32)


def halving_reduce(blocks, axis):
    count = lax.axis_size(axis)
    level = 0
    outgoing, keep = blocks
    received = lax.ppermute(outgoing, axis, [(i, i ^ 1) for i in range(count)])
    while keep.ndim > 2:
        level += 1
        outgoing = keep[0] + received[0]
        pairs = [(i, i ^ (1 << level)) for i in range(count)]
        arriving = lax.ppermute(outgoing, axis, pairs)
        keep = keep[1] + received[1]
        received = arriving
    return keep, received


def recurrence_kernel(rate_ref, keep_ref, received_ref, out_ref):
    hours = out_ref.shape[0]
    state = jnp.zeros(out_ref.shape[1:], jnp.float32)
    for hour in range(hours):
        state = rate_ref[pl.ds(hour, 1), :] * state + (keep_ref[hour] + received_ref[hour])
        out_ref[hour] = state
    state = jnp.zeros(out_ref.shape[1:], jnp.float32)
    for hour in reversed(range(hours)):
        rate = rate_ref[pl.ds(hour, 1), :]
        state = rate * state + (1.0 - rate * rate) * out_ref[hour]
        out_ref[hour] = state


def vmem_call(kernel, out_shape, count, cost, scalars=0):
    return pl.pallas_call(
        kernel,
        out_shape=out_shape,
        in_specs=[pl.BlockSpec(memory_space=pltpu.SMEM)] * scalars
        + [pl.BlockSpec(memory_space=pltpu.VMEM)] * count,
        out_specs=jax.tree.map(lambda _: pl.BlockSpec(memory_space=pltpu.VMEM), out_shape),
        cost_estimate=cost,
    )


def local(obs, mask, loadings, decay):
    tm_count = lax.axis_size("tm")
    stations_local, hours, members = obs.shape
    members_here = members // tm_count
    masked = obs * mask[:, :, None].astype(obs.dtype)
    outgoing = jnp.transpose(
        masked.reshape(stations_local, hours, tm_count, members_here), (2, 0, 1, 3)
    ).reshape(tm_count, stations_local, hours * members_here)
    by_member = lax.all_to_all(outgoing, "tm", split_axis=0, concat_axis=0, tiled=True)
    stations_here = tm_count * stations_local
    by_member = by_member.reshape(stations_here, hours * members_here)
    by_hour = lax.all_to_all(masked, "tm", split_axis=1, concat_axis=0, tiled=True)
    copies = jnp.broadcast_to(decay[None], (tm_count,) + decay.shape)
    decay_all = lax.all_to_all(copies, "tm", split_axis=0, concat_axis=0, tiled=True)
    decay_all = decay_all.reshape(hours, decay.shape[1])
    all_comps = loadings.shape[1]
    columns = hours * members_here
    state_count = lax.axis_size("state")
    levels = state_count.bit_length() - 1
    partial = vmem_call(
        information_kernel,
        (jax.ShapeDtypeStruct(
            (2,) * (levels - 1) + (columns, all_comps // state_count), jnp.float32
        ),) * 2,
        2,
        pl.CostEstimate(
            flops=2 * stations_here * columns * all_comps,
            bytes_accessed=2 * stations_here * (columns + all_comps) + 4 * columns * all_comps,
            transcendentals=0,
        ),
        scalars=1,
    )(lax.axis_index("state").reshape(1).astype(jnp.int32), by_member, loadings)
    keep, received = halving_reduce(partial, "state")
    comps = keep.shape[1]
    keep = keep.reshape(hours, members_here, comps)
    received = received.reshape(hours, members_here, comps)
    smoothed_here = vmem_call(
        recurrence_kernel,
        jax.ShapeDtypeStruct(keep.shape, jnp.float32),
        3,
        pl.CostEstimate(
            flops=5 * hours * members_here * comps,
            bytes_accessed=12 * hours * members_here * comps,
            transcendentals=0,
        ),
    )(decay_all, keep, received)
    gathered = lax.all_to_all(smoothed_here, "tm", split_axis=0, concat_axis=1, tiled=True)
    rounded = gathered.astype(jnp.bfloat16)
    full = lax.all_gather(rounded, "state", axis=2, tiled=True)
    fitted = jnp.einsum("so,gyo->sgy", loadings, full, preferred_element_type=jnp.float32)
    residual = by_hour.astype(jnp.float32) - fitted
    smoothed = jnp.transpose(gathered, (2, 0, 1))
    return (smoothed, residual)


def solution(mesh):
    return jax.shard_map(
        local,
        mesh=mesh,
        in_specs=(
            P(("state", "tm"), None, None),
            P(("state", "tm"), None),
            P("state", None),
            P("tm", "state"),
        ),
        out_specs=(P("state", "tm", None), P("state", "tm", None)),
        check_vma=False,
    )
```

```python
import functools

import jax
import jax.numpy as jnp
from jax import lax
from jax.experimental import pallas as pl
from jax.experimental.pallas import tpu as pltpu
from jax.sharding import PartitionSpec as P

CHUNKS = 2


def information_kernel(hours, me_ref, x_ref, l_ref, send_ref, keep_ref):
    me = me_ref[0]
    chunks = send_ref.shape[0]
    levels = send_ref.ndim - 2
    rows, width = send_ref.shape[-2:]
    flipped = x_ref[...].T
    for slot in range(2 ** levels):
        relative = tuple((slot >> level) & 1 for level in range(levels))
        block = 0
        for level in range(levels):
            block = block + ((relative[level] ^ ((me >> level) & 1) ^ 1) << level)
        columns = l_ref[:, pl.ds(pl.multiple_of(block * width, width), width)]
        total = jnp.dot(flipped, columns, preferred_element_type=jnp.float32)
        total = total.reshape(hours, chunks, rows // hours, width)
        target = keep_ref if relative[0] else send_ref
        for chunk in range(chunks):
            target[(chunk,) + relative[1:]] = total[:, chunk].reshape(rows, width)


def halving_reduce(outgoing, keep, axis):
    count = lax.axis_size(axis)
    level = 0
    received = lax.ppermute(outgoing, axis, [(i, i ^ 1) for i in range(count)])
    while keep.ndim > 2:
        level += 1
        outgoing = keep[0] + received[0]
        pairs = [(i, i ^ (1 << level)) for i in range(count)]
        arriving = lax.ppermute(outgoing, axis, pairs)
        keep = keep[1] + received[1]
        received = arriving
    return keep, received


def recurrence_kernel(rate_ref, keep_ref, received_ref, out_ref):
    hours = out_ref.shape[0]
    state = jnp.zeros(out_ref.shape[1:], jnp.float32)
    for hour in range(hours):
        state = rate_ref[pl.ds(hour, 1), :] * state + (keep_ref[hour] + received_ref[hour])
        out_ref[hour] = state
    state = jnp.zeros(out_ref.shape[1:], jnp.float32)
    for hour in reversed(range(hours)):
        rate = rate_ref[pl.ds(hour, 1), :]
        state = rate * state + (1.0 - rate * rate) * out_ref[hour]
        out_ref[hour] = state


def vmem_call(kernel, out_shape, count, cost, scalars=0):
    return pl.pallas_call(
        kernel,
        out_shape=out_shape,
        in_specs=[pl.BlockSpec(memory_space=pltpu.SMEM)] * scalars
        + [pl.BlockSpec(memory_space=pltpu.VMEM)] * count,
        out_specs=jax.tree.map(lambda _: pl.BlockSpec(memory_space=pltpu.VMEM), out_shape),
        cost_estimate=cost,
    )


def local(obs, mask, loadings, decay):
    tm_count = lax.axis_size("tm")
    state_count = lax.axis_size("state")
    levels = state_count.bit_length() - 1
    stations_local, hours, members = obs.shape
    members_here = members // tm_count
    chunk_members = members_here // CHUNKS
    masked = obs * mask[:, :, None].astype(obs.dtype)
    outgoing = jnp.transpose(
        masked.reshape(stations_local, hours, CHUNKS, tm_count, chunk_members),
        (3, 0, 1, 2, 4),
    ).reshape(tm_count, stations_local, hours * members_here)
    by_member = lax.all_to_all(outgoing, "tm", split_axis=0, concat_axis=0, tiled=True)
    stations_here = tm_count * stations_local
    by_member = by_member.reshape(stations_here, hours * members_here)
    by_hour = lax.all_to_all(masked, "tm", split_axis=1, concat_axis=0, tiled=True)
    copies = jnp.broadcast_to(decay[None], (tm_count,) + decay.shape)
    decay_all = lax.all_to_all(copies, "tm", split_axis=0, concat_axis=0, tiled=True)
    decay_all = decay_all.reshape(hours, decay.shape[1])
    all_comps = loadings.shape[1]
    comps = all_comps // state_count
    rows = hours * chunk_members
    half = jax.ShapeDtypeStruct((CHUNKS,) + (2,) * (levels - 1) + (rows, comps), jnp.float32)
    outgoing, keep = vmem_call(
        functools.partial(information_kernel, hours),
        (half, half),
        2,
        pl.CostEstimate(
            flops=2 * stations_here * hours * members_here * all_comps,
            bytes_accessed=2 * stations_here * (hours * members_here + all_comps)
            + 4 * hours * members_here * all_comps,
            transcendentals=0,
        ),
        scalars=1,
    )(lax.axis_index("state").reshape(1).astype(jnp.int32), by_member, loadings)
    smoothed_parts = []
    residual_parts = []
    for chunk in range(CHUNKS):
        kept, received = halving_reduce(outgoing[chunk], keep[chunk], "state")
        kept = kept.reshape(hours, chunk_members, comps)
        received = received.reshape(hours, chunk_members, comps)
        smoothed_here = vmem_call(
            recurrence_kernel,
            jax.ShapeDtypeStruct(kept.shape, jnp.float32),
            3,
            pl.CostEstimate(
                flops=6 * hours * chunk_members * comps,
                bytes_accessed=12 * hours * chunk_members * comps,
                transcendentals=0,
            ),
        )(decay_all, kept, received)
        gathered = lax.all_to_all(smoothed_here, "tm", split_axis=0, concat_axis=1, tiled=True)
        rounded = gathered.astype(jnp.bfloat16)
        full = lax.all_gather(rounded, "state", axis=2, tiled=True)
        fitted = jnp.einsum("so,gyo->sgy", loadings, full, preferred_element_type=jnp.float32)
        low = chunk * members // CHUNKS
        picked = by_hour[:, :, low:low + members // CHUNKS]
        residual_parts.append(picked.astype(jnp.float32) - fitted)
        smoothed_parts.append(jnp.transpose(gathered, (2, 0, 1)))
    return (
        jnp.concatenate(smoothed_parts, axis=2),
        jnp.concatenate(residual_parts, axis=2),
    )


def solution(mesh):
    return jax.shard_map(
        local,
        mesh=mesh,
        in_specs=(
            P(("state", "tm"), None, None),
            P(("state", "tm"), None),
            P("state", None),
            P("tm", "state"),
        ),
        out_specs=(P("state", "tm", None), P("state", "tm", None)),
        check_vma=False,
    )
```

```python
import functools

import jax
import jax.numpy as jnp
from jax import lax
from jax.experimental import pallas as pl
from jax.experimental.pallas import tpu as pltpu
from jax.sharding import PartitionSpec as P

CHUNKS = 2


def information_kernel(hours, me_ref, x_ref, l_ref, *out_refs):
    me = me_ref[0]
    chunks = len(out_refs) // 2
    levels = out_refs[0].ndim - 1
    rows, width = out_refs[0].shape[-2:]
    flipped = x_ref[...].T
    for slot in range(2 ** levels):
        relative = tuple((slot >> level) & 1 for level in range(levels))
        block = 0
        for level in range(levels):
            block = block + ((relative[level] ^ ((me >> level) & 1) ^ 1) << level)
        columns = l_ref[:, pl.ds(pl.multiple_of(block * width, width), width)]
        total = jnp.dot(flipped, columns, preferred_element_type=jnp.float32)
        total = total.reshape(hours, chunks, rows // hours, width)
        for chunk in range(chunks):
            target = out_refs[2 * chunk + relative[0]]
            target[relative[1:]] = total[:, chunk].reshape(rows, width)


def halving_reduce(outgoing, keep, axis):
    count = lax.axis_size(axis)
    level = 0
    received = lax.ppermute(outgoing, axis, [(i, i ^ 1) for i in range(count)])
    while keep.ndim > 2:
        level += 1
        outgoing = keep[0] + received[0]
        pairs = [(i, i ^ (1 << level)) for i in range(count)]
        arriving = lax.ppermute(outgoing, axis, pairs)
        keep = keep[1] + received[1]
        received = arriving
    return keep, received


def recurrence_kernel(rate_ref, keep_ref, received_ref, out_ref):
    hours = out_ref.shape[0]
    state = jnp.zeros(out_ref.shape[1:], jnp.float32)
    for hour in range(hours):
        state = rate_ref[pl.ds(hour, 1), :] * state + (keep_ref[hour] + received_ref[hour])
        out_ref[hour] = state
    state = jnp.zeros(out_ref.shape[1:], jnp.float32)
    for hour in reversed(range(hours)):
        rate = rate_ref[pl.ds(hour, 1), :]
        state = rate * state + (1.0 - rate * rate) * out_ref[hour]
        out_ref[hour] = state


def vmem_call(kernel, out_shape, count, cost, scalars=0):
    return pl.pallas_call(
        kernel,
        out_shape=out_shape,
        in_specs=[pl.BlockSpec(memory_space=pltpu.SMEM)] * scalars
        + [pl.BlockSpec(memory_space=pltpu.VMEM)] * count,
        out_specs=jax.tree.map(lambda _: pl.BlockSpec(memory_space=pltpu.VMEM), out_shape),
        cost_estimate=cost,
    )


def local(obs, mask, loadings, decay):
    tm_count = lax.axis_size("tm")
    state_count = lax.axis_size("state")
    levels = state_count.bit_length() - 1
    stations_local, hours, members = obs.shape
    members_here = members // tm_count
    chunk_members = members_here // CHUNKS
    masked = obs * mask[:, :, None].astype(obs.dtype)
    outgoing = jnp.transpose(
        masked.reshape(stations_local, hours, CHUNKS, tm_count, chunk_members),
        (3, 0, 1, 2, 4),
    ).reshape(tm_count, stations_local, hours * members_here)
    by_member = lax.all_to_all(outgoing, "tm", split_axis=0, concat_axis=0, tiled=True)
    stations_here = tm_count * stations_local
    by_member = by_member.reshape(stations_here, hours * members_here)
    by_hour = lax.all_to_all(masked, "tm", split_axis=1, concat_axis=0, tiled=True)
    copies = jnp.broadcast_to(decay[None], (tm_count,) + decay.shape)
    decay_all = lax.all_to_all(copies, "tm", split_axis=0, concat_axis=0, tiled=True)
    decay_all = decay_all.reshape(hours, decay.shape[1])
    all_comps = loadings.shape[1]
    comps = all_comps // state_count
    rows = hours * chunk_members
    half = jax.ShapeDtypeStruct((2,) * (levels - 1) + (rows, comps), jnp.float32)
    halves = vmem_call(
        functools.partial(information_kernel, hours),
        (half,) * (2 * CHUNKS),
        2,
        pl.CostEstimate(
            flops=2 * stations_here * hours * members_here * all_comps,
            bytes_accessed=2 * stations_here * (hours * members_here + all_comps)
            + 4 * hours * members_here * all_comps,
            transcendentals=0,
        ),
        scalars=1,
    )(lax.axis_index("state").reshape(1).astype(jnp.int32), by_member, loadings)
    smoothed_parts = []
    residual_parts = []
    for chunk in range(CHUNKS):
        kept, received = halving_reduce(halves[2 * chunk], halves[2 * chunk + 1], "state")
        kept = kept.reshape(hours, chunk_members, comps)
        received = received.reshape(hours, chunk_members, comps)
        smoothed_here = vmem_call(
            recurrence_kernel,
            jax.ShapeDtypeStruct(kept.shape, jnp.float32),
            3,
            pl.CostEstimate(
                flops=6 * hours * chunk_members * comps,
                bytes_accessed=12 * hours * chunk_members * comps,
                transcendentals=0,
            ),
        )(decay_all, kept, received)
        gathered = lax.all_to_all(smoothed_here, "tm", split_axis=0, concat_axis=1, tiled=True)
        rounded = gathered.astype(jnp.bfloat16)
        full = lax.all_gather(rounded, "state", axis=2, tiled=True)
        fitted = jnp.einsum("so,gyo->sgy", loadings, full, preferred_element_type=jnp.float32)
        low = chunk * members // CHUNKS
        picked = by_hour[:, :, low:low + members // CHUNKS]
        residual_parts.append(picked.astype(jnp.float32) - fitted)
        smoothed_parts.append(jnp.transpose(gathered, (2, 0, 1)))
    return (
        jnp.concatenate(smoothed_parts, axis=2),
        jnp.concatenate(residual_parts, axis=2),
    )


def solution(mesh):
    return jax.shard_map(
        local,
        mesh=mesh,
        in_specs=(
            P(("state", "tm"), None, None),
            P(("state", "tm"), None),
            P("state", None),
            P("tm", "state"),
        ),
        out_specs=(P("state", "tm", None), P("state", "tm", None)),
        check_vma=False,
    )
```

```python
import functools

import jax
import jax.numpy as jnp
from jax import lax
from jax.experimental import pallas as pl
from jax.experimental.pallas import tpu as pltpu
from jax.sharding import PartitionSpec as P

CHUNKS = 2


def information_kernel(hours, stations, me_ref, x_ref, l_ref, *out_refs):
    me = me_ref[0]
    chunks = len(out_refs) // 2
    levels = out_refs[0].ndim - 1
    rows, width = out_refs[0].shape[-2:]
    senders = x_ref.shape[0]
    flipped = x_ref[:, :stations, :].reshape(senders * stations, x_ref.shape[2]).T
    for slot in range(2 ** levels):
        relative = tuple((slot >> level) & 1 for level in range(levels))
        block = 0
        for level in range(levels):
            block = block + ((relative[level] ^ ((me >> level) & 1) ^ 1) << level)
        columns = l_ref[:, pl.ds(pl.multiple_of(block * width, width), width)]
        total = jnp.dot(flipped, columns, preferred_element_type=jnp.float32)
        total = total.reshape(hours, chunks, rows // hours, width)
        for chunk in range(chunks):
            target = out_refs[2 * chunk + relative[0]]
            target[relative[1:]] = total[:, chunk].reshape(rows, width)


def halving_reduce(outgoing, keep, axis):
    count = lax.axis_size(axis)
    level = 0
    received = lax.ppermute(outgoing, axis, [(i, i ^ 1) for i in range(count)])
    while keep.ndim > 2:
        level += 1
        outgoing = keep[0] + received[0]
        pairs = [(i, i ^ (1 << level)) for i in range(count)]
        arriving = lax.ppermute(outgoing, axis, pairs)
        keep = keep[1] + received[1]
        received = arriving
    return keep, received


def recurrence_kernel(rate_ref, keep_ref, received_ref, out_ref):
    hours = out_ref.shape[0]
    state = jnp.zeros(out_ref.shape[1:], jnp.float32)
    for hour in range(hours):
        state = rate_ref[pl.ds(hour, 1), :] * state + (keep_ref[hour] + received_ref[hour])
        out_ref[hour] = state
    state = jnp.zeros(out_ref.shape[1:], jnp.float32)
    for hour in reversed(range(hours)):
        rate = rate_ref[pl.ds(hour, 1), :]
        state = rate * state + (1.0 - rate * rate) * out_ref[hour]
        out_ref[hour] = state


def vmem_call(kernel, out_shape, count, cost, scalars=0):
    return pl.pallas_call(
        kernel,
        out_shape=out_shape,
        in_specs=[pl.BlockSpec(memory_space=pltpu.SMEM)] * scalars
        + [pl.BlockSpec(memory_space=pltpu.VMEM)] * count,
        out_specs=jax.tree.map(lambda _: pl.BlockSpec(memory_space=pltpu.VMEM), out_shape),
        cost_estimate=cost,
    )


def local(obs, mask, loadings, decay):
    tm_count = lax.axis_size("tm")
    state_count = lax.axis_size("state")
    levels = state_count.bit_length() - 1
    stations_local, hours, members = obs.shape
    members_here = members // tm_count
    chunk_members = members_here // CHUNKS
    masked = obs * mask[:, :, None].astype(obs.dtype)
    outgoing = jnp.transpose(
        masked.reshape(stations_local, hours, CHUNKS, tm_count, chunk_members),
        (3, 0, 1, 2, 4),
    ).reshape(tm_count, stations_local, hours * members_here)
    high = lax.reduce_precision(decay, exponent_bits=8, mantissa_bits=7)
    middle = lax.reduce_precision(decay - high, exponent_bits=8, mantissa_bits=7)
    low = decay - high - middle
    pieces = jnp.stack([high, middle, low]).astype(obs.dtype).reshape(-1, hours * members_here)
    spare = (-(stations_local + pieces.shape[0])) % 16
    pieces = jnp.pad(pieces, ((0, spare), (0, 0)))
    pieces = jnp.broadcast_to(pieces[None], (tm_count,) + pieces.shape)
    outgoing = jnp.concatenate([outgoing, pieces], axis=1)
    by_member = lax.all_to_all(outgoing, "tm", split_axis=0, concat_axis=0, tiled=True)
    stations_here = tm_count * stations_local
    slab_hours, comps_here = decay.shape
    arrived = by_member[:, stations_local:stations_local + 3 * slab_hours * comps_here // (hours * members_here)]
    arrived = arrived.reshape(tm_count, 3, slab_hours, comps_here).astype(jnp.float32)
    decay_all = (arrived[:, 0] + arrived[:, 1] + arrived[:, 2]).reshape(hours, comps_here)
    masked_later, by_member = lax.optimization_barrier((masked, by_member))
    by_hour = lax.all_to_all(masked_later, "tm", split_axis=1, concat_axis=0, tiled=True)
    all_comps = loadings.shape[1]
    comps = all_comps // state_count
    rows = hours * chunk_members
    half = jax.ShapeDtypeStruct((2,) * (levels - 1) + (rows, comps), jnp.float32)
    halves = vmem_call(
        functools.partial(information_kernel, hours, stations_local),
        (half,) * (2 * CHUNKS),
        2,
        pl.CostEstimate(
            flops=2 * stations_here * hours * members_here * all_comps,
            bytes_accessed=2 * stations_here * (hours * members_here + all_comps)
            + 4 * hours * members_here * all_comps,
            transcendentals=0,
        ),
        scalars=1,
    )(lax.axis_index("state").reshape(1).astype(jnp.int32), by_member, loadings)
    smoothed_parts = []
    residual_parts = []
    for chunk in range(CHUNKS):
        kept, received = halving_reduce(halves[2 * chunk], halves[2 * chunk + 1], "state")
        if chunk == 0:
            by_hour, kept, received = lax.optimization_barrier((by_hour, kept, received))
        kept = kept.reshape(hours, chunk_members, comps)
        received = received.reshape(hours, chunk_members, comps)
        smoothed_here = vmem_call(
            recurrence_kernel,
            jax.ShapeDtypeStruct(kept.shape, jnp.float32),
            3,
            pl.CostEstimate(
                flops=6 * hours * chunk_members * comps,
                bytes_accessed=12 * hours * chunk_members * comps,
                transcendentals=0,
            ),
        )(decay_all, kept, received)
        gathered = lax.all_to_all(smoothed_here, "tm", split_axis=0, concat_axis=1, tiled=True)
        rounded = gathered.astype(jnp.bfloat16)
        full = lax.all_gather(rounded, "state", axis=2, tiled=True)
        fitted = jnp.einsum("so,gyo->sgy", loadings, full, preferred_element_type=jnp.float32)
        low = chunk * members // CHUNKS
        picked = by_hour[:, :, low:low + members // CHUNKS]
        residual_parts.append(picked.astype(jnp.float32) - fitted)
        smoothed_parts.append(jnp.transpose(gathered, (2, 0, 1)))
    return (
        jnp.concatenate(smoothed_parts, axis=2),
        jnp.concatenate(residual_parts, axis=2),
    )


def solution(mesh):
    return jax.shard_map(
        local,
        mesh=mesh,
        in_specs=(
            P(("state", "tm"), None, None),
            P(("state", "tm"), None),
            P("state", None),
            P("tm", "state"),
        ),
        out_specs=(P("state", "tm", None), P("state", "tm", None)),
        check_vma=False,
    )
```

```python
import functools

import jax
import jax.numpy as jnp
from jax import lax
from jax.experimental import pallas as pl
from jax.experimental.pallas import tpu as pltpu
from jax.sharding import PartitionSpec as P

CHUNKS = 2


def information_kernel(hours, stations, me_ref, x_ref, l_ref, *out_refs):
    me = me_ref[0]
    chunks = len(out_refs) // 2
    levels = out_refs[0].ndim - 1
    rows, width = out_refs[0].shape[-2:]
    senders = x_ref.shape[0]
    flipped = x_ref[:, :stations, :].reshape(senders * stations, x_ref.shape[2]).T
    for slot in range(2 ** levels):
        relative = tuple((slot >> level) & 1 for level in range(levels))
        block = 0
        for level in range(levels):
            block = block + ((relative[level] ^ ((me >> level) & 1) ^ 1) << level)
        columns = l_ref[:, pl.ds(pl.multiple_of(block * width, width), width)]
        total = jnp.dot(flipped, columns, preferred_element_type=jnp.float32)
        total = total.reshape(hours, chunks, rows // hours, width)
        for chunk in range(chunks):
            target = out_refs[2 * chunk + relative[0]]
            target[relative[1:]] = total[:, chunk].reshape(rows, width)


def halving_reduce(outgoing, keep, axis):
    count = lax.axis_size(axis)
    level = 0
    received = lax.ppermute(outgoing, axis, [(i, i ^ 1) for i in range(count)])
    while keep.ndim > 2:
        level += 1
        outgoing = keep[0] + received[0]
        pairs = [(i, i ^ (1 << level)) for i in range(count)]
        arriving = lax.ppermute(outgoing, axis, pairs)
        keep = keep[1] + received[1]
        received = arriving
    return keep, received


def doubling_gather(block, axis):
    count = lax.axis_size(axis)
    me = lax.axis_index(axis)
    levels = count.bit_length() - 1
    held = block[None]
    for level in reversed(range(levels)):
        pairs = [(i, i ^ (1 << level)) for i in range(count)]
        held = jnp.concatenate([held, lax.ppermute(held, axis, pairs)], axis=0)
    order = jnp.arange(count) ^ me
    flipped = jnp.zeros_like(order)
    for level in range(levels):
        flipped = flipped | (((order >> level) & 1) << (levels - 1 - level))
    return jnp.take(held, flipped, axis=0)


def recurrence_kernel(rate_ref, keep_ref, received_ref, out_ref):
    hours = out_ref.shape[0]
    state = jnp.zeros(out_ref.shape[1:], jnp.float32)
    for hour in range(hours):
        state = rate_ref[pl.ds(hour, 1), :] * state + (keep_ref[hour] + received_ref[hour])
        out_ref[hour] = state
    state = jnp.zeros(out_ref.shape[1:], jnp.float32)
    for hour in reversed(range(hours)):
        rate = rate_ref[pl.ds(hour, 1), :]
        state = rate * state + (1.0 - rate * rate) * out_ref[hour]
        out_ref[hour] = state


def vmem_call(kernel, out_shape, count, cost, scalars=0):
    return pl.pallas_call(
        kernel,
        out_shape=out_shape,
        in_specs=[pl.BlockSpec(memory_space=pltpu.SMEM)] * scalars
        + [pl.BlockSpec(memory_space=pltpu.VMEM)] * count,
        out_specs=jax.tree.map(lambda _: pl.BlockSpec(memory_space=pltpu.VMEM), out_shape),
        cost_estimate=cost,
    )


def local(obs, mask, loadings, decay):
    tm_count = lax.axis_size("tm")
    state_count = lax.axis_size("state")
    levels = state_count.bit_length() - 1
    stations_local, hours, members = obs.shape
    members_here = members // tm_count
    chunk_members = members_here // CHUNKS
    masked = obs * mask[:, :, None].astype(obs.dtype)
    outgoing = jnp.transpose(
        masked.reshape(stations_local, hours, CHUNKS, tm_count, chunk_members),
        (3, 0, 1, 2, 4),
    ).reshape(tm_count, stations_local, hours * members_here)
    high = lax.reduce_precision(decay, exponent_bits=8, mantissa_bits=7)
    middle = lax.reduce_precision(decay - high, exponent_bits=8, mantissa_bits=7)
    low = decay - high - middle
    pieces = jnp.stack([high, middle, low]).astype(obs.dtype).reshape(-1, hours * members_here)
    spare = (-(stations_local + pieces.shape[0])) % 16
    pieces = jnp.pad(pieces, ((0, spare), (0, 0)))
    pieces = jnp.broadcast_to(pieces[None], (tm_count,) + pieces.shape)
    outgoing = jnp.concatenate([outgoing, pieces], axis=1)
    by_member = lax.all_to_all(outgoing, "tm", split_axis=0, concat_axis=0, tiled=True)
    stations_here = tm_count * stations_local
    slab_hours, comps_here = decay.shape
    arrived = by_member[:, stations_local:stations_local + 3 * slab_hours * comps_here // (hours * members_here)]
    arrived = arrived.reshape(tm_count, 3, slab_hours, comps_here).astype(jnp.float32)
    decay_all = (arrived[:, 0] + arrived[:, 1] + arrived[:, 2]).reshape(hours, comps_here)
    masked_later, by_member = lax.optimization_barrier((masked, by_member))
    by_hour = lax.all_to_all(masked_later, "tm", split_axis=1, concat_axis=0, tiled=True)
    all_comps = loadings.shape[1]
    comps = all_comps // state_count
    rows = hours * chunk_members
    half = jax.ShapeDtypeStruct((2,) * (levels - 1) + (rows, comps), jnp.float32)
    halves = vmem_call(
        functools.partial(information_kernel, hours, stations_local),
        (half,) * (2 * CHUNKS),
        2,
        pl.CostEstimate(
            flops=2 * stations_here * hours * members_here * all_comps,
            bytes_accessed=2 * stations_here * (hours * members_here + all_comps)
            + 4 * hours * members_here * all_comps,
            transcendentals=0,
        ),
        scalars=1,
    )(lax.axis_index("state").reshape(1).astype(jnp.int32), by_member, loadings)
    smoothed_parts = []
    residual_parts = []
    for chunk in range(CHUNKS):
        kept, received = halving_reduce(halves[2 * chunk], halves[2 * chunk + 1], "state")
        if chunk == 0:
            by_hour, kept, received = lax.optimization_barrier((by_hour, kept, received))
        kept = kept.reshape(hours, chunk_members, comps)
        received = received.reshape(hours, chunk_members, comps)
        smoothed_here = vmem_call(
            recurrence_kernel,
            jax.ShapeDtypeStruct(kept.shape, jnp.float32),
            3,
            pl.CostEstimate(
                flops=6 * hours * chunk_members * comps,
                bytes_accessed=12 * hours * chunk_members * comps,
                transcendentals=0,
            ),
        )(decay_all, kept, received)
        gathered = lax.all_to_all(smoothed_here, "tm", split_axis=0, concat_axis=1, tiled=True)
        rounded = gathered.astype(jnp.bfloat16)
        if chunk == CHUNKS - 1:
            every = doubling_gather(rounded, "state")
            full = jnp.transpose(every, (1, 2, 0, 3)).reshape(
                rounded.shape[:2] + (every.shape[0] * rounded.shape[2],)
            )
        else:
            full = lax.all_gather(rounded, "state", axis=2, tiled=True)
        fitted = jnp.einsum("so,gyo->sgy", loadings, full, preferred_element_type=jnp.float32)
        low = chunk * members // CHUNKS
        picked = by_hour[:, :, low:low + members // CHUNKS]
        residual_parts.append(picked.astype(jnp.float32) - fitted)
        smoothed_parts.append(jnp.transpose(gathered, (2, 0, 1)))
    return (
        jnp.concatenate(smoothed_parts, axis=2),
        jnp.concatenate(residual_parts, axis=2),
    )


def solution(mesh):
    return jax.shard_map(
        local,
        mesh=mesh,
        in_specs=(
            P(("state", "tm"), None, None),
            P(("state", "tm"), None),
            P("state", None),
            P("tm", "state"),
        ),
        out_specs=(P("state", "tm", None), P("state", "tm", None)),
        check_vma=False,
    )
```

```python
import functools

import jax
import jax.numpy as jnp
from jax import lax
from jax.experimental import pallas as pl
from jax.experimental.pallas import tpu as pltpu
from jax.sharding import PartitionSpec as P

CHUNKS = 2


def information_kernel(hours, stations, me_ref, x_ref, l_ref, *out_refs):
    me = me_ref[0]
    chunks = len(out_refs) // 2
    levels = out_refs[0].ndim - 1
    rows, width = out_refs[0].shape[-2:]
    senders = x_ref.shape[0]
    flipped = x_ref[:, :stations, :].reshape(senders * stations, x_ref.shape[2]).T
    for slot in range(2 ** levels):
        relative = tuple((slot >> level) & 1 for level in range(levels))
        block = 0
        for level in range(levels):
            block = block + ((relative[level] ^ ((me >> level) & 1) ^ 1) << level)
        columns = l_ref[:, pl.ds(pl.multiple_of(block * width, width), width)]
        total = jnp.dot(flipped, columns, preferred_element_type=jnp.float32)
        total = total.reshape(hours, chunks, rows // hours, width)
        for chunk in range(chunks):
            target = out_refs[2 * chunk + relative[0]]
            target[relative[1:]] = total[:, chunk].reshape(rows, width)


def halving_stages(outgoing, keep, axis):
    count = lax.axis_size(axis)
    level = 0
    pairs = [(i, i ^ 1) for i in range(count)]
    while keep.ndim > 2:
        received = lax.ppermute(outgoing, axis, pairs)
        level += 1
        outgoing = keep[0] + received[0]
        keep = keep[1] + received[1]
        pairs = [(i, i ^ (1 << level)) for i in range(count)]
    return keep, outgoing, pairs


def doubling_gather(block, axis):
    count = lax.axis_size(axis)
    me = lax.axis_index(axis)
    levels = count.bit_length() - 1
    held = block[None]
    for level in reversed(range(levels)):
        pairs = [(i, i ^ (1 << level)) for i in range(count)]
        held = jnp.concatenate([held, lax.ppermute(held, axis, pairs)], axis=0)
    order = jnp.arange(count) ^ me
    flipped = jnp.zeros_like(order)
    for level in range(levels):
        flipped = flipped | (((order >> level) & 1) << (levels - 1 - level))
    return jnp.take(held, flipped, axis=0)


def recurrence_kernel(rate_ref, keep_ref, received_ref, out_ref):
    hours = out_ref.shape[0]
    state = jnp.zeros(out_ref.shape[1:], jnp.float32)
    for hour in range(hours):
        state = rate_ref[pl.ds(hour, 1), :] * state + (keep_ref[hour] + received_ref[hour])
        out_ref[hour] = state
    state = jnp.zeros(out_ref.shape[1:], jnp.float32)
    for hour in reversed(range(hours)):
        rate = rate_ref[pl.ds(hour, 1), :]
        state = rate * state + (1.0 - rate * rate) * out_ref[hour]
        out_ref[hour] = state


def vmem_call(kernel, out_shape, count, cost, scalars=0):
    return pl.pallas_call(
        kernel,
        out_shape=out_shape,
        in_specs=[pl.BlockSpec(memory_space=pltpu.SMEM)] * scalars
        + [pl.BlockSpec(memory_space=pltpu.VMEM)] * count,
        out_specs=jax.tree.map(lambda _: pl.BlockSpec(memory_space=pltpu.VMEM), out_shape),
        cost_estimate=cost,
    )


def local(obs, mask, loadings, decay):
    tm_count = lax.axis_size("tm")
    state_count = lax.axis_size("state")
    levels = state_count.bit_length() - 1
    stations_local, hours, members = obs.shape
    members_here = members // tm_count
    chunk_members = members_here // CHUNKS
    masked = obs * mask[:, :, None].astype(obs.dtype)
    outgoing = jnp.transpose(
        masked.reshape(stations_local, hours, CHUNKS, tm_count, chunk_members),
        (3, 0, 1, 2, 4),
    ).reshape(tm_count, stations_local, hours * members_here)
    high = lax.reduce_precision(decay, exponent_bits=8, mantissa_bits=7)
    middle = lax.reduce_precision(decay - high, exponent_bits=8, mantissa_bits=7)
    low = decay - high - middle
    pieces = jnp.stack([high, middle, low]).astype(obs.dtype).reshape(-1, hours * members_here)
    spare = (-(stations_local + pieces.shape[0])) % 16
    pieces = jnp.pad(pieces, ((0, spare), (0, 0)))
    pieces = jnp.broadcast_to(pieces[None], (tm_count,) + pieces.shape)
    outgoing = jnp.concatenate([outgoing, pieces], axis=1)
    by_member = lax.all_to_all(outgoing, "tm", split_axis=0, concat_axis=0, tiled=True)
    stations_here = tm_count * stations_local
    slab_hours, comps_here = decay.shape
    arrived = by_member[:, stations_local:stations_local + 3 * slab_hours * comps_here // (hours * members_here)]
    arrived = arrived.reshape(tm_count, 3, slab_hours, comps_here).astype(jnp.float32)
    decay_all = (arrived[:, 0] + arrived[:, 1] + arrived[:, 2]).reshape(hours, comps_here)
    masked_later, by_member = lax.optimization_barrier((masked, by_member))
    by_hour = lax.all_to_all(masked_later, "tm", split_axis=1, concat_axis=0, tiled=True)
    all_comps = loadings.shape[1]
    comps = all_comps // state_count
    rows = hours * chunk_members
    half = jax.ShapeDtypeStruct((2,) * (levels - 1) + (rows, comps), jnp.float32)
    halves = vmem_call(
        functools.partial(information_kernel, hours, stations_local),
        (half,) * (2 * CHUNKS),
        2,
        pl.CostEstimate(
            flops=2 * stations_here * hours * members_here * all_comps,
            bytes_accessed=2 * stations_here * (hours * members_here + all_comps)
            + 4 * hours * members_here * all_comps,
            transcendentals=0,
        ),
        scalars=1,
    )(lax.axis_index("state").reshape(1).astype(jnp.int32), by_member, loadings)
    smoothed_parts = []
    residual_parts = []
    last = [halving_stages(halves[2 * c], halves[2 * c + 1], "state") for c in range(CHUNKS)]
    kept, outgoing, pairs = last[0]
    received = lax.ppermute(outgoing, "state", pairs)
    later = [(k, o) for k, o, _ in last[1:]]
    by_hour, kept, received, later = lax.optimization_barrier((by_hour, kept, received, later))
    addends = [(kept, received)] + [
        (k, lax.ppermute(o, "state", last[c + 1][2])) for c, (k, o) in enumerate(later)
    ]
    for chunk in range(CHUNKS):
        kept, received = addends[chunk]
        kept = kept.reshape(hours, chunk_members, comps)
        received = received.reshape(hours, chunk_members, comps)
        smoothed_here = vmem_call(
            recurrence_kernel,
            jax.ShapeDtypeStruct(kept.shape, jnp.float32),
            3,
            pl.CostEstimate(
                flops=6 * hours * chunk_members * comps,
                bytes_accessed=12 * hours * chunk_members * comps,
                transcendentals=0,
            ),
        )(decay_all, kept, received)
        gathered = lax.all_to_all(smoothed_here, "tm", split_axis=0, concat_axis=1, tiled=True)
        rounded = gathered.astype(jnp.bfloat16)
        if chunk == CHUNKS - 1:
            every = doubling_gather(rounded, "state")
            full = jnp.transpose(every, (1, 2, 0, 3)).reshape(
                rounded.shape[:2] + (every.shape[0] * rounded.shape[2],)
            )
        else:
            full = lax.all_gather(rounded, "state", axis=2, tiled=True)
        fitted = jnp.einsum("so,gyo->sgy", loadings, full, preferred_element_type=jnp.float32)
        low = chunk * members // CHUNKS
        picked = by_hour[:, :, low:low + members // CHUNKS]
        residual_parts.append(picked.astype(jnp.float32) - fitted)
        smoothed_parts.append(jnp.transpose(gathered, (2, 0, 1)))
    return (
        jnp.concatenate(smoothed_parts, axis=2),
        jnp.concatenate(residual_parts, axis=2),
    )


def solution(mesh):
    return jax.shard_map(
        local,
        mesh=mesh,
        in_specs=(
            P(("state", "tm"), None, None),
            P(("state", "tm"), None),
            P("state", None),
            P("tm", "state"),
        ),
        out_specs=(P("state", "tm", None), P("state", "tm", None)),
        check_vma=False,
    )
```

```python
import functools

import jax
import jax.numpy as jnp
from jax import lax
from jax.experimental import pallas as pl
from jax.experimental.pallas import tpu as pltpu
from jax.sharding import PartitionSpec as P

CHUNKS = 2


def information_kernel(hours, stations, me_ref, x_ref, l_ref, *out_refs):
    me = me_ref[0]
    chunks = len(out_refs) // 2
    levels = out_refs[0].ndim - 1
    rows, width = out_refs[0].shape[-2:]
    senders = x_ref.shape[0]
    flipped = x_ref[:, :stations, :].reshape(senders * stations, x_ref.shape[2]).T
    for slot in range(2 ** levels):
        relative = tuple((slot >> level) & 1 for level in range(levels))
        block = 0
        for level in range(levels):
            block = block + ((relative[level] ^ ((me >> level) & 1) ^ 1) << level)
        columns = l_ref[:, pl.ds(pl.multiple_of(block * width, width), width)]
        total = jnp.dot(flipped, columns, preferred_element_type=jnp.float32)
        total = total.reshape(hours, chunks, rows // hours, width)
        for chunk in range(chunks):
            target = out_refs[2 * chunk + relative[0]]
            target[relative[1:]] = total[:, chunk].reshape(rows, width)


def halving_stages(outgoing, keep, axis):
    count = lax.axis_size(axis)
    level = 0
    pairs = [(i, i ^ 1) for i in range(count)]
    while keep.ndim > 2:
        received = lax.ppermute(outgoing, axis, pairs)
        level += 1
        outgoing = keep[0] + received[0]
        keep = keep[1] + received[1]
        pairs = [(i, i ^ (1 << level)) for i in range(count)]
    return keep, outgoing, pairs


def doubling_gather(block, axis):
    count = lax.axis_size(axis)
    levels = count.bit_length() - 1
    pieces = [block]
    for level in reversed(range(levels)):
        pairs = [(i, i ^ (1 << level)) for i in range(count)]
        pieces = pieces + [lax.ppermute(piece, axis, pairs) for piece in pieces]
    return pieces


def fitted_kernel(me_ref, l_ref, *refs):
    *piece_refs, out_ref = refs
    me = me_ref[0]
    levels = len(piece_refs).bit_length() - 1
    width = piece_refs[0].shape[-1]
    for hour in range(out_ref.shape[0]):
        total = None
        for position, piece_ref in enumerate(piece_refs):
            flipped = 0
            for level in range(levels):
                flipped |= ((position >> level) & 1) << (levels - 1 - level)
            block = me ^ flipped
            columns = l_ref[:, pl.ds(pl.multiple_of(block * width, width), width)]
            part = lax.dot_general(
                columns, piece_ref[hour], (((1,), (1,)), ((), ())),
                preferred_element_type=jnp.float32,
            )
            total = part if total is None else total + part
        out_ref[hour] = total


def recurrence_kernel(rate_ref, keep_ref, received_ref, out_ref):
    hours = out_ref.shape[0]
    state = jnp.zeros(out_ref.shape[1:], jnp.float32)
    for hour in range(hours):
        state = rate_ref[pl.ds(hour, 1), :] * state + (keep_ref[hour] + received_ref[hour])
        out_ref[hour] = state
    state = jnp.zeros(out_ref.shape[1:], jnp.float32)
    for hour in reversed(range(hours)):
        rate = rate_ref[pl.ds(hour, 1), :]
        state = rate * state + (1.0 - rate * rate) * out_ref[hour]
        out_ref[hour] = state


def vmem_call(kernel, out_shape, count, cost, scalars=0):
    return pl.pallas_call(
        kernel,
        out_shape=out_shape,
        in_specs=[pl.BlockSpec(memory_space=pltpu.SMEM)] * scalars
        + [pl.BlockSpec(memory_space=pltpu.VMEM)] * count,
        out_specs=jax.tree.map(lambda _: pl.BlockSpec(memory_space=pltpu.VMEM), out_shape),
        cost_estimate=cost,
    )


def local(obs, mask, loadings, decay):
    tm_count = lax.axis_size("tm")
    state_count = lax.axis_size("state")
    levels = state_count.bit_length() - 1
    stations_local, hours, members = obs.shape
    members_here = members // tm_count
    chunk_members = members_here // CHUNKS
    masked = obs * mask[:, :, None].astype(obs.dtype)
    outgoing = jnp.transpose(
        masked.reshape(stations_local, hours, CHUNKS, tm_count, chunk_members),
        (3, 0, 1, 2, 4),
    ).reshape(tm_count, stations_local, hours * members_here)
    high = lax.reduce_precision(decay, exponent_bits=8, mantissa_bits=7)
    middle = lax.reduce_precision(decay - high, exponent_bits=8, mantissa_bits=7)
    low = decay - high - middle
    pieces = jnp.stack([high, middle, low]).astype(obs.dtype).reshape(-1, hours * members_here)
    spare = (-(stations_local + pieces.shape[0])) % 16
    pieces = jnp.pad(pieces, ((0, spare), (0, 0)))
    pieces = jnp.broadcast_to(pieces[None], (tm_count,) + pieces.shape)
    outgoing = jnp.concatenate([outgoing, pieces], axis=1)
    by_member = lax.all_to_all(outgoing, "tm", split_axis=0, concat_axis=0, tiled=True)
    stations_here = tm_count * stations_local
    slab_hours, comps_here = decay.shape
    arrived = by_member[:, stations_local:stations_local + 3 * slab_hours * comps_here // (hours * members_here)]
    arrived = arrived.reshape(tm_count, 3, slab_hours, comps_here).astype(jnp.float32)
    decay_all = (arrived[:, 0] + arrived[:, 1] + arrived[:, 2]).reshape(hours, comps_here)
    masked_later, by_member = lax.optimization_barrier((masked, by_member))
    by_hour = lax.all_to_all(masked_later, "tm", split_axis=1, concat_axis=0, tiled=True)
    all_comps = loadings.shape[1]
    comps = all_comps // state_count
    rows = hours * chunk_members
    half = jax.ShapeDtypeStruct((2,) * (levels - 1) + (rows, comps), jnp.float32)
    halves = vmem_call(
        functools.partial(information_kernel, hours, stations_local),
        (half,) * (2 * CHUNKS),
        2,
        pl.CostEstimate(
            flops=2 * stations_here * hours * members_here * all_comps,
            bytes_accessed=2 * stations_here * (hours * members_here + all_comps)
            + 4 * hours * members_here * all_comps,
            transcendentals=0,
        ),
        scalars=1,
    )(lax.axis_index("state").reshape(1).astype(jnp.int32), by_member, loadings)
    smoothed_parts = []
    residual_parts = []
    last = [halving_stages(halves[2 * c], halves[2 * c + 1], "state") for c in range(CHUNKS)]
    kept, outgoing, pairs = last[0]
    received = lax.ppermute(outgoing, "state", pairs)
    later = [(k, o) for k, o, _ in last[1:]]
    by_hour, kept, received, later = lax.optimization_barrier((by_hour, kept, received, later))
    addends = [(kept, received)] + [
        (k, lax.ppermute(o, "state", last[c + 1][2])) for c, (k, o) in enumerate(later)
    ]
    for chunk in range(CHUNKS):
        kept, received = addends[chunk]
        kept = kept.reshape(hours, chunk_members, comps)
        received = received.reshape(hours, chunk_members, comps)
        smoothed_here = vmem_call(
            recurrence_kernel,
            jax.ShapeDtypeStruct(kept.shape, jnp.float32),
            3,
            pl.CostEstimate(
                flops=6 * hours * chunk_members * comps,
                bytes_accessed=12 * hours * chunk_members * comps,
                transcendentals=0,
            ),
        )(decay_all, kept, received)
        gathered = lax.all_to_all(smoothed_here, "tm", split_axis=0, concat_axis=1, tiled=True)
        rounded = gathered.astype(jnp.bfloat16)
        if chunk == CHUNKS - 1:
            pieces = doubling_gather(rounded, "state")
            slab_hours, width, _ = rounded.shape
            fitted = vmem_call(
                fitted_kernel,
                jax.ShapeDtypeStruct((slab_hours, stations_here, width), jnp.float32),
                1 + len(pieces),
                pl.CostEstimate(
                    flops=2 * stations_here * slab_hours * width * all_comps,
                    bytes_accessed=2 * stations_here * all_comps
                    + 2 * slab_hours * width * all_comps
                    + 4 * slab_hours * stations_here * width,
                    transcendentals=0,
                ),
                scalars=1,
            )(lax.axis_index("state").reshape(1).astype(jnp.int32), loadings, *pieces)
            fitted = jnp.transpose(fitted, (1, 0, 2))
        else:
            full = lax.all_gather(rounded, "state", axis=2, tiled=True)
            fitted = jnp.einsum(
                "so,gyo->sgy", loadings, full, preferred_element_type=jnp.float32
            )
        low = chunk * members // CHUNKS
        picked = by_hour[:, :, low:low + members // CHUNKS]
        residual_parts.append(picked.astype(jnp.float32) - fitted)
        smoothed_parts.append(jnp.transpose(gathered, (2, 0, 1)))
    return (
        jnp.concatenate(smoothed_parts, axis=2),
        jnp.concatenate(residual_parts, axis=2),
    )


def solution(mesh):
    return jax.shard_map(
        local,
        mesh=mesh,
        in_specs=(
            P(("state", "tm"), None, None),
            P(("state", "tm"), None),
            P("state", None),
            P("tm", "state"),
        ),
        out_specs=(P("state", "tm", None), P("state", "tm", None)),
        check_vma=False,
    )
```

```python
import functools

import jax
import jax.numpy as jnp
from jax import lax
from jax.experimental import pallas as pl
from jax.experimental.pallas import tpu as pltpu
from jax.sharding import PartitionSpec as P

CHUNKS = 2


def information_kernel(hours, stations, me_ref, x_ref, l_ref, *out_refs):
    me = me_ref[0]
    chunks = len(out_refs) // 2
    levels = out_refs[0].ndim - 1
    rows, width = out_refs[0].shape[-2:]
    senders = x_ref.shape[0]
    flipped = x_ref[:, :stations, :].reshape(senders * stations, x_ref.shape[2]).T
    for slot in range(2 ** levels):
        relative = tuple((slot >> level) & 1 for level in range(levels))
        block = 0
        for level in range(levels):
            block = block + ((relative[level] ^ ((me >> level) & 1) ^ 1) << level)
        columns = l_ref[:, pl.ds(pl.multiple_of(block * width, width), width)]
        total = jnp.dot(flipped, columns, preferred_element_type=jnp.float32)
        total = total.reshape(hours, chunks, rows // hours, width)
        for chunk in range(chunks):
            target = out_refs[2 * chunk + relative[0]]
            target[relative[1:]] = total[:, chunk].reshape(rows, width)


def halving_stages(outgoing, keep, axis):
    count = lax.axis_size(axis)
    level = 0
    pairs = [(i, i ^ 1) for i in range(count)]
    while keep.ndim > 2:
        received = lax.ppermute(outgoing, axis, pairs)
        level += 1
        outgoing = keep[0] + received[0]
        keep = keep[1] + received[1]
        pairs = [(i, i ^ (1 << level)) for i in range(count)]
    return keep, outgoing, pairs


def doubling_gather(block, axis):
    count = lax.axis_size(axis)
    levels = count.bit_length() - 1
    pieces = [block]
    for level in reversed(range(levels)):
        pairs = [(i, i ^ (1 << level)) for i in range(count)]
        pieces = pieces + [lax.ppermute(piece, axis, pairs) for piece in pieces]
    return pieces


def fitted_kernel(me_ref, l_ref, *refs):
    *piece_refs, out_ref = refs
    me = me_ref[0]
    levels = len(piece_refs).bit_length() - 1
    width = piece_refs[0].shape[-1]
    hours, members, _ = piece_refs[0].shape
    total = None
    for position, piece_ref in enumerate(piece_refs):
        flipped = 0
        for level in range(levels):
            flipped |= ((position >> level) & 1) << (levels - 1 - level)
        block = me ^ flipped
        columns = l_ref[:, pl.ds(pl.multiple_of(block * width, width), width)]
        piece = piece_ref[...].reshape(hours * members, width)
        part = lax.dot_general(
            columns, piece, (((1,), (1,)), ((), ())),
            preferred_element_type=jnp.float32,
        )
        total = part if total is None else total + part
    for hour in range(hours):
        out_ref[hour] = total[:, hour * members:(hour + 1) * members]


def recurrence_kernel(rate_ref, keep_ref, received_ref, out_ref):
    hours = out_ref.shape[0]
    state = jnp.zeros(out_ref.shape[1:], jnp.float32)
    for hour in range(hours):
        state = rate_ref[pl.ds(hour, 1), :] * state + (keep_ref[hour] + received_ref[hour])
        out_ref[hour] = state
    state = jnp.zeros(out_ref.shape[1:], jnp.float32)
    for hour in reversed(range(hours)):
        rate = rate_ref[pl.ds(hour, 1), :]
        state = rate * state + (1.0 - rate * rate) * out_ref[hour]
        out_ref[hour] = state


def vmem_call(kernel, out_shape, count, cost, scalars=0):
    return pl.pallas_call(
        kernel,
        out_shape=out_shape,
        in_specs=[pl.BlockSpec(memory_space=pltpu.SMEM)] * scalars
        + [pl.BlockSpec(memory_space=pltpu.VMEM)] * count,
        out_specs=jax.tree.map(lambda _: pl.BlockSpec(memory_space=pltpu.VMEM), out_shape),
        cost_estimate=cost,
    )


def local(obs, mask, loadings, decay):
    tm_count = lax.axis_size("tm")
    state_count = lax.axis_size("state")
    levels = state_count.bit_length() - 1
    stations_local, hours, members = obs.shape
    members_here = members // tm_count
    chunk_members = members_here // CHUNKS
    masked = obs * mask[:, :, None].astype(obs.dtype)
    outgoing = jnp.transpose(
        masked.reshape(stations_local, hours, CHUNKS, tm_count, chunk_members),
        (3, 0, 1, 2, 4),
    ).reshape(tm_count, stations_local, hours * members_here)
    high = lax.reduce_precision(decay, exponent_bits=8, mantissa_bits=7)
    middle = lax.reduce_precision(decay - high, exponent_bits=8, mantissa_bits=7)
    low = decay - high - middle
    pieces = jnp.stack([high, middle, low]).astype(obs.dtype).reshape(-1, hours * members_here)
    spare = (-(stations_local + pieces.shape[0])) % 16
    pieces = jnp.pad(pieces, ((0, spare), (0, 0)))
    pieces = jnp.broadcast_to(pieces[None], (tm_count,) + pieces.shape)
    outgoing = jnp.concatenate([outgoing, pieces], axis=1)
    by_member = lax.all_to_all(outgoing, "tm", split_axis=0, concat_axis=0, tiled=True)
    stations_here = tm_count * stations_local
    slab_hours, comps_here = decay.shape
    arrived = by_member[:, stations_local:stations_local + 3 * slab_hours * comps_here // (hours * members_here)]
    arrived = arrived.reshape(tm_count, 3, slab_hours, comps_here).astype(jnp.float32)
    decay_all = (arrived[:, 0] + arrived[:, 1] + arrived[:, 2]).reshape(hours, comps_here)
    masked_later, by_member = lax.optimization_barrier((masked, by_member))
    by_hour = lax.all_to_all(masked_later, "tm", split_axis=1, concat_axis=0, tiled=True)
    all_comps = loadings.shape[1]
    comps = all_comps // state_count
    rows = hours * chunk_members
    half = jax.ShapeDtypeStruct((2,) * (levels - 1) + (rows, comps), jnp.float32)
    halves = vmem_call(
        functools.partial(information_kernel, hours, stations_local),
        (half,) * (2 * CHUNKS),
        2,
        pl.CostEstimate(
            flops=2 * stations_here * hours * members_here * all_comps,
            bytes_accessed=2 * stations_here * (hours * members_here + all_comps)
            + 4 * hours * members_here * all_comps,
            transcendentals=0,
        ),
        scalars=1,
    )(lax.axis_index("state").reshape(1).astype(jnp.int32), by_member, loadings)
    smoothed_parts = []
    residual_parts = []
    last = [halving_stages(halves[2 * c], halves[2 * c + 1], "state") for c in range(CHUNKS)]
    kept, outgoing, pairs = last[0]
    received = lax.ppermute(outgoing, "state", pairs)
    later = [(k, o) for k, o, _ in last[1:]]
    by_hour, kept, received, later = lax.optimization_barrier((by_hour, kept, received, later))
    addends = [(kept, received)] + [
        (k, lax.ppermute(o, "state", last[c + 1][2])) for c, (k, o) in enumerate(later)
    ]
    for chunk in range(CHUNKS):
        kept, received = addends[chunk]
        kept = kept.reshape(hours, chunk_members, comps)
        received = received.reshape(hours, chunk_members, comps)
        smoothed_here = vmem_call(
            recurrence_kernel,
            jax.ShapeDtypeStruct(kept.shape, jnp.float32),
            3,
            pl.CostEstimate(
                flops=6 * hours * chunk_members * comps,
                bytes_accessed=12 * hours * chunk_members * comps,
                transcendentals=0,
            ),
        )(decay_all, kept, received)
        gathered = lax.all_to_all(smoothed_here, "tm", split_axis=0, concat_axis=1, tiled=True)
        rounded = gathered.astype(jnp.bfloat16)
        if chunk == CHUNKS - 1:
            pieces = doubling_gather(rounded, "state")
            smoothed_parts.append(jnp.transpose(gathered, (2, 0, 1)))
            smoothed = jnp.concatenate(smoothed_parts, axis=2)
            smoothed, pieces = lax.optimization_barrier((smoothed, pieces))
            slab_hours, width, _ = rounded.shape
            fitted = vmem_call(
                fitted_kernel,
                jax.ShapeDtypeStruct((slab_hours, stations_here, width), jnp.float32),
                1 + len(pieces),
                pl.CostEstimate(
                    flops=2 * stations_here * slab_hours * width * all_comps,
                    bytes_accessed=2 * stations_here * all_comps
                    + 2 * slab_hours * width * all_comps
                    + 4 * slab_hours * stations_here * width,
                    transcendentals=0,
                ),
                scalars=1,
            )(lax.axis_index("state").reshape(1).astype(jnp.int32), loadings, *pieces)
            fitted = jnp.transpose(fitted, (1, 0, 2))
        else:
            full = lax.all_gather(rounded, "state", axis=2, tiled=True)
            fitted = jnp.einsum(
                "so,gyo->sgy", loadings, full, preferred_element_type=jnp.float32
            )
        low = chunk * members // CHUNKS
        picked = by_hour[:, :, low:low + members // CHUNKS]
        residual_parts.append(picked.astype(jnp.float32) - fitted)
        if chunk < CHUNKS - 1:
            smoothed_parts.append(jnp.transpose(gathered, (2, 0, 1)))
    return (smoothed, jnp.concatenate(residual_parts, axis=2))


def solution(mesh):
    return jax.shard_map(
        local,
        mesh=mesh,
        in_specs=(
            P(("state", "tm"), None, None),
            P(("state", "tm"), None),
            P("state", None),
            P("tm", "state"),
        ),
        out_specs=(P("state", "tm", None), P("state", "tm", None)),
        check_vma=False,
    )
```

```python
import functools

import jax
import jax.numpy as jnp
from jax import lax
from jax.experimental import pallas as pl
from jax.experimental.pallas import tpu as pltpu
from jax.sharding import PartitionSpec as P

CHUNKS = 2


def information_kernel(hours, stations, me_ref, x_ref, l_ref, *out_refs):
    me = me_ref[0]
    chunks = len(out_refs) // 2
    levels = out_refs[0].ndim - 1
    rows, width = out_refs[0].shape[-2:]
    senders = x_ref.shape[0]
    flipped = x_ref[:, :stations, :].reshape(senders * stations, x_ref.shape[2]).T
    for slot in range(2 ** levels):
        relative = tuple((slot >> level) & 1 for level in range(levels))
        block = 0
        for level in range(levels):
            block = block + ((relative[level] ^ ((me >> level) & 1) ^ 1) << level)
        columns = l_ref[:, pl.ds(pl.multiple_of(block * width, width), width)]
        total = jnp.dot(flipped, columns, preferred_element_type=jnp.float32)
        total = total.reshape(hours, chunks, rows // hours, width)
        for chunk in range(chunks):
            target = out_refs[2 * chunk + relative[0]]
            target[relative[1:]] = total[:, chunk].reshape(rows, width)


def halving_stages(outgoing, keep, axis):
    count = lax.axis_size(axis)
    level = 0
    pairs = [(i, i ^ 1) for i in range(count)]
    while keep.ndim > 2:
        received = lax.ppermute(outgoing, axis, pairs)
        level += 1
        outgoing = keep[0] + received[0]
        keep = keep[1] + received[1]
        pairs = [(i, i ^ (1 << level)) for i in range(count)]
    return keep, outgoing, pairs


def doubling_gather(block, axis):
    count = lax.axis_size(axis)
    levels = count.bit_length() - 1
    pieces = [block]
    for level in reversed(range(levels)):
        pairs = [(i, i ^ (1 << level)) for i in range(count)]
        pieces = pieces + [lax.ppermute(piece, axis, pairs) for piece in pieces]
    return pieces


def fitted_kernel(me_ref, l_ref, *refs):
    *piece_refs, out_ref = refs
    me = me_ref[0]
    levels = len(piece_refs).bit_length() - 1
    width = piece_refs[0].shape[-1]
    for hour in range(out_ref.shape[0]):
        total = None
        for position, piece_ref in enumerate(piece_refs):
            flipped = 0
            for level in range(levels):
                flipped |= ((position >> level) & 1) << (levels - 1 - level)
            block = me ^ flipped
            columns = l_ref[:, pl.ds(pl.multiple_of(block * width, width), width)]
            part = lax.dot_general(
                columns, piece_ref[hour], (((1,), (1,)), ((), ())),
                preferred_element_type=jnp.float32,
            )
            total = part if total is None else total + part
        out_ref[hour] = total


def recurrence_kernel(rate_ref, keep_ref, received_ref, out_ref):
    hours = out_ref.shape[0]
    state = jnp.zeros(out_ref.shape[1:], jnp.float32)
    for hour in range(hours):
        state = rate_ref[pl.ds(hour, 1), :] * state + (keep_ref[hour] + received_ref[hour])
        out_ref[hour] = state
    state = jnp.zeros(out_ref.shape[1:], jnp.float32)
    for hour in reversed(range(hours)):
        rate = rate_ref[pl.ds(hour, 1), :]
        state = rate * state + (1.0 - rate * rate) * out_ref[hour]
        out_ref[hour] = state


def vmem_call(kernel, out_shape, count, cost, scalars=0):
    return pl.pallas_call(
        kernel,
        out_shape=out_shape,
        in_specs=[pl.BlockSpec(memory_space=pltpu.SMEM)] * scalars
        + [pl.BlockSpec(memory_space=pltpu.VMEM)] * count,
        out_specs=jax.tree.map(lambda _: pl.BlockSpec(memory_space=pltpu.VMEM), out_shape),
        cost_estimate=cost,
    )


def local(obs, mask, loadings, decay):
    tm_count = lax.axis_size("tm")
    state_count = lax.axis_size("state")
    levels = state_count.bit_length() - 1
    stations_local, hours, members = obs.shape
    members_here = members // tm_count
    chunk_members = members_here // CHUNKS
    masked = obs * mask[:, :, None].astype(obs.dtype)
    outgoing = jnp.transpose(
        masked.reshape(stations_local, hours, CHUNKS, tm_count, chunk_members),
        (3, 0, 1, 2, 4),
    ).reshape(tm_count, stations_local, hours * members_here)
    high = lax.reduce_precision(decay, exponent_bits=8, mantissa_bits=7)
    middle = lax.reduce_precision(decay - high, exponent_bits=8, mantissa_bits=7)
    low = decay - high - middle
    pieces = jnp.stack([high, middle, low]).astype(obs.dtype).reshape(-1, hours * members_here)
    spare = (-(stations_local + pieces.shape[0])) % 16
    pieces = jnp.pad(pieces, ((0, spare), (0, 0)))
    pieces = jnp.broadcast_to(pieces[None], (tm_count,) + pieces.shape)
    outgoing = jnp.concatenate([outgoing, pieces], axis=1)
    by_member = lax.all_to_all(outgoing, "tm", split_axis=0, concat_axis=0, tiled=True)
    stations_here = tm_count * stations_local
    slab_hours, comps_here = decay.shape
    arrived = by_member[:, stations_local:stations_local + 3 * slab_hours * comps_here // (hours * members_here)]
    arrived = arrived.reshape(tm_count, 3, slab_hours, comps_here).astype(jnp.float32)
    decay_all = (arrived[:, 0] + arrived[:, 1] + arrived[:, 2]).reshape(hours, comps_here)
    masked_later, by_member = lax.optimization_barrier((masked, by_member))
    by_hour = lax.all_to_all(masked_later, "tm", split_axis=1, concat_axis=0, tiled=True)
    all_comps = loadings.shape[1]
    comps = all_comps // state_count
    rows = hours * chunk_members
    half = jax.ShapeDtypeStruct((2,) * (levels - 1) + (rows, comps), jnp.float32)
    halves = vmem_call(
        functools.partial(information_kernel, hours, stations_local),
        (half,) * (2 * CHUNKS),
        2,
        pl.CostEstimate(
            flops=2 * stations_here * hours * members_here * all_comps,
            bytes_accessed=2 * stations_here * (hours * members_here + all_comps)
            + 4 * hours * members_here * all_comps,
            transcendentals=0,
        ),
        scalars=1,
    )(lax.axis_index("state").reshape(1).astype(jnp.int32), by_member, loadings)
    smoothed_parts = []
    residual_parts = []
    last = [halving_stages(halves[2 * c], halves[2 * c + 1], "state") for c in range(CHUNKS)]
    kept, outgoing, pairs = last[0]
    received = lax.ppermute(outgoing, "state", pairs)
    later = [(k, o) for k, o, _ in last[1:]]
    by_hour, kept, received, later = lax.optimization_barrier((by_hour, kept, received, later))
    addends = [(kept, received)] + [
        (k, lax.ppermute(o, "state", last[c + 1][2])) for c, (k, o) in enumerate(later)
    ]
    for chunk in range(CHUNKS):
        kept, received = addends[chunk]
        kept = kept.reshape(hours, chunk_members, comps)
        received = received.reshape(hours, chunk_members, comps)
        smoothed_here = vmem_call(
            recurrence_kernel,
            jax.ShapeDtypeStruct(kept.shape, jnp.float32),
            3,
            pl.CostEstimate(
                flops=6 * hours * chunk_members * comps,
                bytes_accessed=12 * hours * chunk_members * comps,
                transcendentals=0,
            ),
        )(decay_all, kept, received)
        gathered = lax.all_to_all(smoothed_here, "tm", split_axis=0, concat_axis=1, tiled=True)
        rounded = gathered.astype(jnp.bfloat16)
        pieces = doubling_gather(rounded, "state")
        slab_hours, width, _ = rounded.shape
        fitted = vmem_call(
            fitted_kernel,
            jax.ShapeDtypeStruct((slab_hours, stations_here, width), jnp.float32),
            1 + len(pieces),
            pl.CostEstimate(
                flops=2 * stations_here * slab_hours * width * all_comps,
                bytes_accessed=2 * stations_here * all_comps
                + 2 * slab_hours * width * all_comps
                + 4 * slab_hours * stations_here * width,
                transcendentals=0,
            ),
            scalars=1,
        )(lax.axis_index("state").reshape(1).astype(jnp.int32), loadings, *pieces)
        fitted = jnp.transpose(fitted, (1, 0, 2))
        low = chunk * members // CHUNKS
        picked = by_hour[:, :, low:low + members // CHUNKS]
        residual_parts.append(picked.astype(jnp.float32) - fitted)
        smoothed_parts.append(jnp.transpose(gathered, (2, 0, 1)))
    return (
        jnp.concatenate(smoothed_parts, axis=2),
        jnp.concatenate(residual_parts, axis=2),
    )


def solution(mesh):
    return jax.shard_map(
        local,
        mesh=mesh,
        in_specs=(
            P(("state", "tm"), None, None),
            P(("state", "tm"), None),
            P("state", None),
            P("tm", "state"),
        ),
        out_specs=(P("state", "tm", None), P("state", "tm", None)),
        check_vma=False,
    )
```

```python
import functools

import jax
import jax.numpy as jnp
from jax import lax
from jax.experimental import pallas as pl
from jax.experimental.pallas import tpu as pltpu
from jax.sharding import PartitionSpec as P

CHUNKS = 2


def information_kernel(hours, stations, me_ref, x_ref, l_ref, *out_refs):
    me = me_ref[0]
    chunks = len(out_refs) // 2
    levels = out_refs[0].ndim - 1
    rows, width = out_refs[0].shape[-2:]
    senders = x_ref.shape[0]
    flipped = x_ref[:, :stations, :].reshape(senders * stations, x_ref.shape[2]).T
    for slot in range(2 ** levels):
        relative = tuple((slot >> level) & 1 for level in range(levels))
        block = 0
        for level in range(levels):
            block = block + ((relative[level] ^ ((me >> level) & 1) ^ 1) << level)
        columns = l_ref[:, pl.ds(pl.multiple_of(block * width, width), width)]
        total = jnp.dot(flipped, columns, preferred_element_type=jnp.float32)
        total = total.reshape(hours, chunks, rows // hours, width)
        for chunk in range(chunks):
            target = out_refs[2 * chunk + relative[0]]
            target[relative[1:]] = total[:, chunk].reshape(rows, width)


def halving_stages(outgoing, keep, axis):
    count = lax.axis_size(axis)
    level = 0
    pairs = [(i, i ^ 1) for i in range(count)]
    while keep.ndim > 2:
        received = lax.ppermute(outgoing, axis, pairs)
        level += 1
        outgoing = keep[0] + received[0]
        keep = keep[1] + received[1]
        pairs = [(i, i ^ (1 << level)) for i in range(count)]
    return keep, outgoing, pairs


def doubling_gather(block, axis):
    count = lax.axis_size(axis)
    levels = count.bit_length() - 1
    pieces = [block]
    for level in reversed(range(levels)):
        pairs = [(i, i ^ (1 << level)) for i in range(count)]
        pieces = pieces + [lax.ppermute(piece, axis, pairs) for piece in pieces]
    return pieces


def fitted_kernel(me_ref, l_ref, *refs):
    *piece_refs, out_ref = refs
    me = me_ref[0]
    levels = len(piece_refs).bit_length() - 1
    width = piece_refs[0].shape[-1]
    for hour in range(out_ref.shape[0]):
        total = None
        for position, piece_ref in enumerate(piece_refs):
            flipped = 0
            for level in range(levels):
                flipped |= ((position >> level) & 1) << (levels - 1 - level)
            block = me ^ flipped
            columns = l_ref[:, pl.ds(pl.multiple_of(block * width, width), width)]
            part = lax.dot_general(
                columns, piece_ref[hour], (((1,), (1,)), ((), ())),
                preferred_element_type=jnp.float32,
            )
            total = part if total is None else total + part
        out_ref[hour] = total


def recurrence_kernel(rate_ref, keep_ref, received_ref, out_ref):
    hours = out_ref.shape[0]
    state = jnp.zeros(out_ref.shape[1:], jnp.float32)
    for hour in range(hours):
        state = rate_ref[pl.ds(hour, 1), :] * state + (keep_ref[hour] + received_ref[hour])
        out_ref[hour] = state
    state = jnp.zeros(out_ref.shape[1:], jnp.float32)
    for hour in reversed(range(hours)):
        rate = rate_ref[pl.ds(hour, 1), :]
        state = rate * state + (1.0 - rate * rate) * out_ref[hour]
        out_ref[hour] = state


def vmem_call(kernel, out_shape, count, cost, scalars=0):
    return pl.pallas_call(
        kernel,
        out_shape=out_shape,
        in_specs=[pl.BlockSpec(memory_space=pltpu.SMEM)] * scalars
        + [pl.BlockSpec(memory_space=pltpu.VMEM)] * count,
        out_specs=jax.tree.map(lambda _: pl.BlockSpec(memory_space=pltpu.VMEM), out_shape),
        cost_estimate=cost,
    )


def local(obs, mask, loadings, decay):
    tm_count = lax.axis_size("tm")
    state_count = lax.axis_size("state")
    levels = state_count.bit_length() - 1
    stations_local, hours, members = obs.shape
    members_here = members // tm_count
    chunk_members = members_here // CHUNKS
    masked = obs * mask[:, :, None].astype(obs.dtype)
    outgoing = jnp.transpose(
        masked.reshape(stations_local, hours, CHUNKS, tm_count, chunk_members),
        (3, 0, 1, 2, 4),
    ).reshape(tm_count, stations_local, hours * members_here)
    high = lax.reduce_precision(decay, exponent_bits=8, mantissa_bits=7)
    middle = lax.reduce_precision(decay - high, exponent_bits=8, mantissa_bits=7)
    low = decay - high - middle
    pieces = jnp.stack([high, middle, low]).astype(obs.dtype).reshape(-1, hours * members_here)
    spare = (-(stations_local + pieces.shape[0])) % 16
    pieces = jnp.pad(pieces, ((0, spare), (0, 0)))
    pieces = jnp.broadcast_to(pieces[None], (tm_count,) + pieces.shape)
    outgoing = jnp.concatenate([outgoing, pieces], axis=1)
    by_member = lax.all_to_all(outgoing, "tm", split_axis=0, concat_axis=0, tiled=True)
    stations_here = tm_count * stations_local
    slab_hours, comps_here = decay.shape
    arrived = by_member[:, stations_local:stations_local + 3 * slab_hours * comps_here // (hours * members_here)]
    arrived = arrived.reshape(tm_count, 3, slab_hours, comps_here).astype(jnp.float32)
    decay_all = (arrived[:, 0] + arrived[:, 1] + arrived[:, 2]).reshape(hours, comps_here)
    masked_later, by_member = lax.optimization_barrier((masked, by_member))
    by_hour = lax.all_to_all(masked_later, "tm", split_axis=1, concat_axis=0, tiled=True)
    all_comps = loadings.shape[1]
    comps = all_comps // state_count
    rows = hours * chunk_members
    half = jax.ShapeDtypeStruct((2,) * (levels - 1) + (rows, comps), jnp.float32)
    halves = vmem_call(
        functools.partial(information_kernel, hours, stations_local),
        (half,) * (2 * CHUNKS),
        2,
        pl.CostEstimate(
            flops=2 * stations_here * hours * members_here * all_comps,
            bytes_accessed=2 * stations_here * (hours * members_here + all_comps)
            + 4 * hours * members_here * all_comps,
            transcendentals=0,
        ),
        scalars=1,
    )(lax.axis_index("state").reshape(1).astype(jnp.int32), by_member, loadings)
    smoothed_parts = []
    residual_parts = []
    fitted_parts = []
    last = [halving_stages(halves[2 * c], halves[2 * c + 1], "state") for c in range(CHUNKS)]
    kept, outgoing, pairs = last[0]
    received = lax.ppermute(outgoing, "state", pairs)
    later = [(k, o) for k, o, _ in last[1:]]
    by_hour, kept, received, later = lax.optimization_barrier((by_hour, kept, received, later))
    addends = [(kept, received)] + [
        (k, lax.ppermute(o, "state", last[c + 1][2])) for c, (k, o) in enumerate(later)
    ]
    for chunk in range(CHUNKS):
        kept, received = addends[chunk]
        kept = kept.reshape(hours, chunk_members, comps)
        received = received.reshape(hours, chunk_members, comps)
        smoothed_here = vmem_call(
            recurrence_kernel,
            jax.ShapeDtypeStruct(kept.shape, jnp.float32),
            3,
            pl.CostEstimate(
                flops=6 * hours * chunk_members * comps,
                bytes_accessed=12 * hours * chunk_members * comps,
                transcendentals=0,
            ),
        )(decay_all, kept, received)
        gathered = lax.all_to_all(smoothed_here, "tm", split_axis=0, concat_axis=1, tiled=True)
        if fitted_parts:
            gathered, fitted_parts[-1] = lax.optimization_barrier((gathered, fitted_parts[-1]))
        rounded = gathered.astype(jnp.bfloat16)
        pieces = doubling_gather(rounded, "state")
        slab_hours, width, _ = rounded.shape
        fitted = vmem_call(
            fitted_kernel,
            jax.ShapeDtypeStruct((slab_hours, stations_here, width), jnp.float32),
            1 + len(pieces),
            pl.CostEstimate(
                flops=2 * stations_here * slab_hours * width * all_comps,
                bytes_accessed=2 * stations_here * all_comps
                + 2 * slab_hours * width * all_comps
                + 4 * slab_hours * stations_here * width,
                transcendentals=0,
            ),
            scalars=1,
        )(lax.axis_index("state").reshape(1).astype(jnp.int32), loadings, *pieces)
        fitted_parts.append(fitted)
        smoothed_parts.append(jnp.transpose(gathered, (2, 0, 1)))
    for chunk, fitted in enumerate(fitted_parts):
        low = chunk * members // CHUNKS
        picked = by_hour[:, :, low:low + members // CHUNKS]
        residual_parts.append(picked.astype(jnp.float32) - jnp.transpose(fitted, (1, 0, 2)))
    return (
        jnp.concatenate(smoothed_parts, axis=2),
        jnp.concatenate(residual_parts, axis=2),
    )


def solution(mesh):
    return jax.shard_map(
        local,
        mesh=mesh,
        in_specs=(
            P(("state", "tm"), None, None),
            P(("state", "tm"), None),
            P("state", None),
            P("tm", "state"),
        ),
        out_specs=(P("state", "tm", None), P("state", "tm", None)),
        check_vma=False,
    )
```

```python
import functools

import jax
import jax.numpy as jnp
from jax import lax
from jax.experimental import pallas as pl
from jax.experimental.pallas import tpu as pltpu
from jax.sharding import PartitionSpec as P

CHUNKS = 2


def information_kernel(hours, stations, me_ref, x_ref, l_ref, *out_refs):
    me = me_ref[0]
    chunks = len(out_refs) // 2
    levels = out_refs[0].ndim - 1
    rows, width = out_refs[0].shape[-2:]
    senders = x_ref.shape[0]
    flipped = x_ref[:, :stations, :].reshape(senders * stations, x_ref.shape[2]).T
    for slot in range(2 ** levels):
        relative = tuple((slot >> level) & 1 for level in range(levels))
        block = 0
        for level in range(levels):
            block = block + ((relative[level] ^ ((me >> level) & 1) ^ 1) << level)
        columns = l_ref[:, pl.ds(pl.multiple_of(block * width, width), width)]
        total = jnp.dot(flipped, columns, preferred_element_type=jnp.float32)
        total = total.reshape(hours, chunks, rows // hours, width)
        for chunk in range(chunks):
            target = out_refs[2 * chunk + relative[0]]
            target[relative[1:]] = total[:, chunk].reshape(rows, width)


def halving_stages(outgoing, keep, axis):
    count = lax.axis_size(axis)
    level = 0
    pairs = [(i, i ^ 1) for i in range(count)]
    while keep.ndim > 2:
        received = lax.ppermute(outgoing, axis, pairs)
        level += 1
        outgoing = keep[0] + received[0]
        keep = keep[1] + received[1]
        pairs = [(i, i ^ (1 << level)) for i in range(count)]
    return keep, outgoing, pairs


def doubling_gather(block, axis, companion):
    count = lax.axis_size(axis)
    levels = count.bit_length() - 1
    pieces = [block]
    for level in reversed(range(levels)):
        pairs = [(i, i ^ (1 << level)) for i in range(count)]
        pieces = pieces + [lax.ppermute(piece, axis, pairs) for piece in pieces]
        if level == levels - 1:
            pieces, companion = lax.optimization_barrier((pieces, companion))
    return pieces, companion


def fitted_kernel(me_ref, l_ref, *refs):
    *piece_refs, out_ref = refs
    me = me_ref[0]
    levels = len(piece_refs).bit_length() - 1
    width = piece_refs[0].shape[-1]
    for hour in range(out_ref.shape[0]):
        total = None
        for position, piece_ref in enumerate(piece_refs):
            flipped = 0
            for level in range(levels):
                flipped |= ((position >> level) & 1) << (levels - 1 - level)
            block = me ^ flipped
            columns = l_ref[:, pl.ds(pl.multiple_of(block * width, width), width)]
            part = lax.dot_general(
                columns, piece_ref[hour], (((1,), (1,)), ((), ())),
                preferred_element_type=jnp.float32,
            )
            total = part if total is None else total + part
        out_ref[hour] = total


def recurrence_kernel(rate_ref, keep_ref, received_ref, out_ref):
    hours = out_ref.shape[0]
    state = jnp.zeros(out_ref.shape[1:], jnp.float32)
    for hour in range(hours):
        state = rate_ref[pl.ds(hour, 1), :] * state + (keep_ref[hour] + received_ref[hour])
        out_ref[hour] = state
    state = jnp.zeros(out_ref.shape[1:], jnp.float32)
    for hour in reversed(range(hours)):
        rate = rate_ref[pl.ds(hour, 1), :]
        state = rate * state + (1.0 - rate * rate) * out_ref[hour]
        out_ref[hour] = state


def vmem_call(kernel, out_shape, count, cost, scalars=0):
    return pl.pallas_call(
        kernel,
        out_shape=out_shape,
        in_specs=[pl.BlockSpec(memory_space=pltpu.SMEM)] * scalars
        + [pl.BlockSpec(memory_space=pltpu.VMEM)] * count,
        out_specs=jax.tree.map(lambda _: pl.BlockSpec(memory_space=pltpu.VMEM), out_shape),
        cost_estimate=cost,
    )


def local(obs, mask, loadings, decay):
    tm_count = lax.axis_size("tm")
    state_count = lax.axis_size("state")
    levels = state_count.bit_length() - 1
    stations_local, hours, members = obs.shape
    members_here = members // tm_count
    chunk_members = members_here // CHUNKS
    masked = obs * mask[:, :, None].astype(obs.dtype)
    outgoing = jnp.transpose(
        masked.reshape(stations_local, hours, CHUNKS, tm_count, chunk_members),
        (3, 0, 1, 2, 4),
    ).reshape(tm_count, stations_local, hours * members_here)
    high = lax.reduce_precision(decay, exponent_bits=8, mantissa_bits=7)
    middle = lax.reduce_precision(decay - high, exponent_bits=8, mantissa_bits=7)
    low = decay - high - middle
    pieces = jnp.stack([high, middle, low]).astype(obs.dtype).reshape(-1, hours * members_here)
    spare = (-(stations_local + pieces.shape[0])) % 16
    pieces = jnp.pad(pieces, ((0, spare), (0, 0)))
    pieces = jnp.broadcast_to(pieces[None], (tm_count,) + pieces.shape)
    outgoing = jnp.concatenate([outgoing, pieces], axis=1)
    by_member = lax.all_to_all(outgoing, "tm", split_axis=0, concat_axis=0, tiled=True)
    stations_here = tm_count * stations_local
    slab_hours, comps_here = decay.shape
    arrived = by_member[:, stations_local:stations_local + 3 * slab_hours * comps_here // (hours * members_here)]
    arrived = arrived.reshape(tm_count, 3, slab_hours, comps_here).astype(jnp.float32)
    decay_all = (arrived[:, 0] + arrived[:, 1] + arrived[:, 2]).reshape(hours, comps_here)
    masked_later, by_member = lax.optimization_barrier((masked, by_member))
    by_hour = lax.all_to_all(masked_later, "tm", split_axis=1, concat_axis=0, tiled=True)
    all_comps = loadings.shape[1]
    comps = all_comps // state_count
    rows = hours * chunk_members
    half = jax.ShapeDtypeStruct((2,) * (levels - 1) + (rows, comps), jnp.float32)
    halves = vmem_call(
        functools.partial(information_kernel, hours, stations_local),
        (half,) * (2 * CHUNKS),
        2,
        pl.CostEstimate(
            flops=2 * stations_here * hours * members_here * all_comps,
            bytes_accessed=2 * stations_here * (hours * members_here + all_comps)
            + 4 * hours * members_here * all_comps,
            transcendentals=0,
        ),
        scalars=1,
    )(lax.axis_index("state").reshape(1).astype(jnp.int32), by_member, loadings)
    smoothed_parts = []
    residual_parts = []
    fitted_parts = []
    last = [halving_stages(halves[2 * c], halves[2 * c + 1], "state") for c in range(CHUNKS)]
    kept, outgoing, pairs = last[0]
    received = lax.ppermute(outgoing, "state", pairs)
    later = [(k, o) for k, o, _ in last[1:]]
    by_hour, kept, received, later = lax.optimization_barrier((by_hour, kept, received, later))
    addends = [(kept, received)] + [
        (k, lax.ppermute(o, "state", last[c + 1][2])) for c, (k, o) in enumerate(later)
    ]
    for chunk in range(CHUNKS):
        kept, received = addends[chunk]
        kept = kept.reshape(hours, chunk_members, comps)
        received = received.reshape(hours, chunk_members, comps)
        smoothed_here = vmem_call(
            recurrence_kernel,
            jax.ShapeDtypeStruct(kept.shape, jnp.float32),
            3,
            pl.CostEstimate(
                flops=6 * hours * chunk_members * comps,
                bytes_accessed=12 * hours * chunk_members * comps,
                transcendentals=0,
            ),
        )(decay_all, kept, received)
        gathered = lax.all_to_all(smoothed_here, "tm", split_axis=0, concat_axis=1, tiled=True)
        rounded = gathered.astype(jnp.bfloat16)
        pieces, earlier = doubling_gather(rounded, "state", fitted_parts[-1:])
        fitted_parts[-1:] = earlier
        slab_hours, width, _ = rounded.shape
        fitted = vmem_call(
            fitted_kernel,
            jax.ShapeDtypeStruct((slab_hours, stations_here, width), jnp.float32),
            1 + len(pieces),
            pl.CostEstimate(
                flops=2 * stations_here * slab_hours * width * all_comps,
                bytes_accessed=2 * stations_here * all_comps
                + 2 * slab_hours * width * all_comps
                + 4 * slab_hours * stations_here * width,
                transcendentals=0,
            ),
            scalars=1,
        )(lax.axis_index("state").reshape(1).astype(jnp.int32), loadings, *pieces)
        fitted_parts.append(fitted)
        smoothed_parts.append(jnp.transpose(gathered, (2, 0, 1)))
    for chunk, fitted in enumerate(fitted_parts):
        low = chunk * members // CHUNKS
        picked = by_hour[:, :, low:low + members // CHUNKS]
        residual_parts.append(picked.astype(jnp.float32) - jnp.transpose(fitted, (1, 0, 2)))
    return (
        jnp.concatenate(smoothed_parts, axis=2),
        jnp.concatenate(residual_parts, axis=2),
    )


def solution(mesh):
    return jax.shard_map(
        local,
        mesh=mesh,
        in_specs=(
            P(("state", "tm"), None, None),
            P(("state", "tm"), None),
            P("state", None),
            P("tm", "state"),
        ),
        out_specs=(P("state", "tm", None), P("state", "tm", None)),
        check_vma=False,
    )
```

```python
import functools

import jax
import jax.numpy as jnp
from jax import lax
from jax.experimental import pallas as pl
from jax.experimental.pallas import tpu as pltpu
from jax.sharding import PartitionSpec as P

CHUNKS = 2


def information_kernel(hours, stations, me_ref, x_ref, l_ref, *out_refs):
    me = me_ref[0]
    chunks = len(out_refs) // 2
    levels = out_refs[0].ndim - 1
    rows, width = out_refs[0].shape[-2:]
    senders = x_ref.shape[0]
    flipped = x_ref[...].reshape(senders * stations, x_ref.shape[2]).T
    for slot in range(2 ** levels):
        relative = tuple((slot >> level) & 1 for level in range(levels))
        block = 0
        for level in range(levels):
            block = block + ((relative[level] ^ ((me >> level) & 1) ^ 1) << level)
        columns = l_ref[:, pl.ds(pl.multiple_of(block * width, width), width)]
        total = jnp.dot(flipped, columns, preferred_element_type=jnp.float32)
        total = total.reshape(hours, chunks, rows // hours, width)
        for chunk in range(chunks):
            target = out_refs[2 * chunk + relative[0]]
            target[relative[1:]] = total[:, chunk].reshape(rows, width)


def halving_stages(outgoing, keep, axis):
    count = lax.axis_size(axis)
    level = 0
    pairs = [(i, i ^ 1) for i in range(count)]
    while keep.ndim > 2:
        received = lax.ppermute(outgoing, axis, pairs)
        level += 1
        outgoing = keep[0] + received[0]
        keep = keep[1] + received[1]
        pairs = [(i, i ^ (1 << level)) for i in range(count)]
    return keep, outgoing, pairs


def doubling_gather(block, axis, companion):
    count = lax.axis_size(axis)
    levels = count.bit_length() - 1
    pieces = [block]
    for level in reversed(range(levels)):
        pairs = [(i, i ^ (1 << level)) for i in range(count)]
        pieces = pieces + [lax.ppermute(piece, axis, pairs) for piece in pieces]
        if level == levels - 1:
            pieces, companion = lax.optimization_barrier((pieces, companion))
    return pieces, companion


def fitted_kernel(me_ref, l_ref, *refs):
    *piece_refs, out_ref = refs
    me = me_ref[0]
    levels = len(piece_refs).bit_length() - 1
    width = piece_refs[0].shape[-1]
    for hour in range(out_ref.shape[0]):
        total = None
        for position, piece_ref in enumerate(piece_refs):
            flipped = 0
            for level in range(levels):
                flipped |= ((position >> level) & 1) << (levels - 1 - level)
            block = me ^ flipped
            columns = l_ref[:, pl.ds(pl.multiple_of(block * width, width), width)]
            part = lax.dot_general(
                columns, piece_ref[hour], (((1,), (1,)), ((), ())),
                preferred_element_type=jnp.float32,
            )
            total = part if total is None else total + part
        out_ref[hour] = total


def recurrence_kernel(rate_ref, keep_ref, received_ref, out_ref):
    hours = out_ref.shape[0]
    state = jnp.zeros(out_ref.shape[1:], jnp.float32)
    for hour in range(hours):
        state = rate_ref[pl.ds(hour, 1), :] * state + (keep_ref[hour] + received_ref[hour])
        out_ref[hour] = state
    state = jnp.zeros(out_ref.shape[1:], jnp.float32)
    for hour in reversed(range(hours)):
        rate = rate_ref[pl.ds(hour, 1), :]
        state = rate * state + (1.0 - rate * rate) * out_ref[hour]
        out_ref[hour] = state


def vmem_call(kernel, out_shape, count, cost, scalars=0):
    return pl.pallas_call(
        kernel,
        out_shape=out_shape,
        in_specs=[pl.BlockSpec(memory_space=pltpu.SMEM)] * scalars
        + [pl.BlockSpec(memory_space=pltpu.VMEM)] * count,
        out_specs=jax.tree.map(lambda _: pl.BlockSpec(memory_space=pltpu.VMEM), out_shape),
        cost_estimate=cost,
    )


def local(obs, mask, loadings, decay):
    tm_count = lax.axis_size("tm")
    state_count = lax.axis_size("state")
    levels = state_count.bit_length() - 1
    stations_local, hours, members = obs.shape
    members_here = members // tm_count
    chunk_members = members_here // CHUNKS
    masked = obs * mask[:, :, None].astype(obs.dtype)
    outgoing = jnp.transpose(
        masked.reshape(stations_local, hours, CHUNKS, tm_count, chunk_members),
        (3, 0, 1, 2, 4),
    ).reshape(tm_count, stations_local, hours * members_here)
    by_member = lax.all_to_all(outgoing, "tm", split_axis=0, concat_axis=0, tiled=True)
    stations_here = tm_count * stations_local
    masked_later, by_member = lax.optimization_barrier((masked, by_member))
    slab_hours, comps_here = decay.shape
    high = lax.reduce_precision(decay, exponent_bits=8, mantissa_bits=7)
    middle = lax.reduce_precision(decay - high, exponent_bits=8, mantissa_bits=7)
    low = decay - high - middle
    pieces = jnp.stack([high, middle, low]).astype(obs.dtype).reshape(-1, slab_hours, members)
    piece_rows = pieces.shape[0]
    spare = (-(stations_local + piece_rows)) % 8
    pieces = jnp.pad(pieces, ((0, spare), (0, 0), (0, 0)))
    pieces = jnp.broadcast_to(pieces[None], (tm_count,) + pieces.shape)
    outgoing_hours = jnp.transpose(
        masked_later.reshape(stations_local, tm_count, slab_hours, members), (1, 0, 2, 3)
    )
    outgoing_hours = jnp.concatenate([outgoing_hours, pieces], axis=1)
    by_hour = lax.all_to_all(outgoing_hours, "tm", split_axis=0, concat_axis=0, tiled=True)
    arrived = by_hour[:, stations_local:stations_local + piece_rows]
    arrived = arrived.reshape(tm_count, 3, slab_hours, comps_here).astype(jnp.float32)
    decay_all = (arrived[:, 0] + arrived[:, 1] + arrived[:, 2]).reshape(hours, comps_here)
    by_hour = by_hour[:, :stations_local].reshape(stations_here, slab_hours, members)
    all_comps = loadings.shape[1]
    comps = all_comps // state_count
    rows = hours * chunk_members
    half = jax.ShapeDtypeStruct((2,) * (levels - 1) + (rows, comps), jnp.float32)
    halves = vmem_call(
        functools.partial(information_kernel, hours, stations_local),
        (half,) * (2 * CHUNKS),
        2,
        pl.CostEstimate(
            flops=2 * stations_here * hours * members_here * all_comps,
            bytes_accessed=2 * stations_here * (hours * members_here + all_comps)
            + 4 * hours * members_here * all_comps,
            transcendentals=0,
        ),
        scalars=1,
    )(lax.axis_index("state").reshape(1).astype(jnp.int32), by_member, loadings)
    smoothed_parts = []
    residual_parts = []
    fitted_parts = []
    last = [halving_stages(halves[2 * c], halves[2 * c + 1], "state") for c in range(CHUNKS)]
    kept, outgoing, pairs = last[0]
    received = lax.ppermute(outgoing, "state", pairs)
    later = [(k, o) for k, o, _ in last[1:]]
    by_hour, kept, received, later = lax.optimization_barrier((by_hour, kept, received, later))
    addends = [(kept, received)] + [
        (k, lax.ppermute(o, "state", last[c + 1][2])) for c, (k, o) in enumerate(later)
    ]
    for chunk in range(CHUNKS):
        kept, received = addends[chunk]
        kept = kept.reshape(hours, chunk_members, comps)
        received = received.reshape(hours, chunk_members, comps)
        smoothed_here = vmem_call(
            recurrence_kernel,
            jax.ShapeDtypeStruct(kept.shape, jnp.float32),
            3,
            pl.CostEstimate(
                flops=6 * hours * chunk_members * comps,
                bytes_accessed=12 * hours * chunk_members * comps,
                transcendentals=0,
            ),
        )(decay_all, kept, received)
        gathered = lax.all_to_all(smoothed_here, "tm", split_axis=0, concat_axis=1, tiled=True)
        rounded = gathered.astype(jnp.bfloat16)
        pieces, earlier = doubling_gather(rounded, "state", fitted_parts[-1:])
        fitted_parts[-1:] = earlier
        slab_hours, width, _ = rounded.shape
        fitted = vmem_call(
            fitted_kernel,
            jax.ShapeDtypeStruct((slab_hours, stations_here, width), jnp.float32),
            1 + len(pieces),
            pl.CostEstimate(
                flops=2 * stations_here * slab_hours * width * all_comps,
                bytes_accessed=2 * stations_here * all_comps
                + 2 * slab_hours * width * all_comps
                + 4 * slab_hours * stations_here * width,
                transcendentals=0,
            ),
            scalars=1,
        )(lax.axis_index("state").reshape(1).astype(jnp.int32), loadings, *pieces)
        fitted_parts.append(fitted)
        smoothed_parts.append(jnp.transpose(gathered, (2, 0, 1)))
    for chunk, fitted in enumerate(fitted_parts):
        low = chunk * members // CHUNKS
        picked = by_hour[:, :, low:low + members // CHUNKS]
        residual_parts.append(picked.astype(jnp.float32) - jnp.transpose(fitted, (1, 0, 2)))
    return (
        jnp.concatenate(smoothed_parts, axis=2),
        jnp.concatenate(residual_parts, axis=2),
    )


def solution(mesh):
    return jax.shard_map(
        local,
        mesh=mesh,
        in_specs=(
            P(("state", "tm"), None, None),
            P(("state", "tm"), None),
            P("state", None),
            P("tm", "state"),
        ),
        out_specs=(P("state", "tm", None), P("state", "tm", None)),
        check_vma=False,
    )
```

```python
import functools

import jax
import jax.numpy as jnp
from jax import lax
from jax.experimental import pallas as pl
from jax.experimental.pallas import tpu as pltpu
from jax.sharding import PartitionSpec as P

CHUNKS = 2


def information_kernel(hours, stations, me_ref, x_ref, l_ref, *out_refs):
    me = me_ref[0]
    chunks = len(out_refs) // 2
    levels = out_refs[0].ndim - 1
    rows, width = out_refs[0].shape[-2:]
    senders = x_ref.shape[0]
    flipped = x_ref[:, :stations, :].reshape(senders * stations, x_ref.shape[2]).T
    for slot in range(2 ** levels):
        relative = tuple((slot >> level) & 1 for level in range(levels))
        block = 0
        for level in range(levels):
            block = block + ((relative[level] ^ ((me >> level) & 1) ^ 1) << level)
        columns = l_ref[:, pl.ds(pl.multiple_of(block * width, width), width)]
        total = jnp.dot(flipped, columns, preferred_element_type=jnp.float32)
        total = total.reshape(hours, chunks, rows // hours, width)
        for chunk in range(chunks):
            target = out_refs[2 * chunk + relative[0]]
            target[relative[1:]] = total[:, chunk].reshape(rows, width)


def halving_stages(outgoing, keep, axis):
    count = lax.axis_size(axis)
    level = 0
    pairs = [(i, i ^ 1) for i in range(count)]
    while keep.ndim > 2:
        received = lax.ppermute(outgoing, axis, pairs)
        level += 1
        outgoing = keep[0] + received[0]
        keep = keep[1] + received[1]
        pairs = [(i, i ^ (1 << level)) for i in range(count)]
    return keep, outgoing, pairs


def doubling_gather(block, axis, companion):
    count = lax.axis_size(axis)
    levels = count.bit_length() - 1
    pieces = [block]
    for level in reversed(range(levels)):
        pairs = [(i, i ^ (1 << level)) for i in range(count)]
        pieces = pieces + [lax.ppermute(piece, axis, pairs) for piece in pieces]
        if level == levels - 1:
            pieces, companion = lax.optimization_barrier((pieces, companion))
    return pieces, companion


def fitted_kernel(me_ref, l_ref, *refs):
    *piece_refs, out_ref = refs
    me = me_ref[0]
    levels = len(piece_refs).bit_length() - 1
    width = piece_refs[0].shape[-1]
    for hour in range(out_ref.shape[0]):
        total = None
        for position, piece_ref in enumerate(piece_refs):
            flipped = 0
            for level in range(levels):
                flipped |= ((position >> level) & 1) << (levels - 1 - level)
            block = me ^ flipped
            columns = l_ref[:, pl.ds(pl.multiple_of(block * width, width), width)]
            part = lax.dot_general(
                columns, piece_ref[hour], (((1,), (1,)), ((), ())),
                preferred_element_type=jnp.float32,
            )
            total = part if total is None else total + part
        out_ref[hour] = total


def recurrence_kernel(rate_ref, keep_ref, received_ref, out_ref):
    hours = out_ref.shape[0]
    state = jnp.zeros(out_ref.shape[1:], jnp.float32)
    for hour in range(hours):
        state = rate_ref[pl.ds(hour, 1), :] * state + (keep_ref[hour] + received_ref[hour])
        out_ref[hour] = state
    state = jnp.zeros(out_ref.shape[1:], jnp.float32)
    for hour in reversed(range(hours)):
        rate = rate_ref[pl.ds(hour, 1), :]
        state = rate * state + (1.0 - rate * rate) * out_ref[hour]
        out_ref[hour] = state


def vmem_call(kernel, out_shape, count, cost, scalars=0):
    return pl.pallas_call(
        kernel,
        out_shape=out_shape,
        in_specs=[pl.BlockSpec(memory_space=pltpu.SMEM)] * scalars
        + [pl.BlockSpec(memory_space=pltpu.VMEM)] * count,
        out_specs=jax.tree.map(lambda _: pl.BlockSpec(memory_space=pltpu.VMEM), out_shape),
        cost_estimate=cost,
    )


def local(obs, mask, loadings, decay):
    tm_count = lax.axis_size("tm")
    state_count = lax.axis_size("state")
    levels = state_count.bit_length() - 1
    stations_local, hours, members = obs.shape
    members_here = members // tm_count
    chunk_members = members_here // CHUNKS
    masked = obs * mask[:, :, None].astype(obs.dtype)
    outgoing = jnp.transpose(
        masked.reshape(stations_local, hours, CHUNKS, tm_count, chunk_members),
        (3, 0, 1, 2, 4),
    ).reshape(tm_count, stations_local, hours * members_here)
    by_member = lax.all_to_all(outgoing, "tm", split_axis=0, concat_axis=0, tiled=True)
    stations_here = tm_count * stations_local
    slabs, _ = doubling_gather(decay, "tm", [])
    tm_levels = tm_count.bit_length() - 1
    wanted = jnp.arange(tm_count) ^ lax.axis_index("tm")
    position = jnp.zeros_like(wanted)
    for level in range(tm_levels):
        position = position | (((wanted >> level) & 1) << (tm_levels - 1 - level))
    decay_all = jnp.take(jnp.stack(slabs), position, axis=0).reshape(hours, decay.shape[1])
    masked_later, by_member = lax.optimization_barrier((masked, by_member))
    by_hour = lax.all_to_all(masked_later, "tm", split_axis=1, concat_axis=0, tiled=True)
    all_comps = loadings.shape[1]
    comps = all_comps // state_count
    rows = hours * chunk_members
    half = jax.ShapeDtypeStruct((2,) * (levels - 1) + (rows, comps), jnp.float32)
    halves = vmem_call(
        functools.partial(information_kernel, hours, stations_local),
        (half,) * (2 * CHUNKS),
        2,
        pl.CostEstimate(
            flops=2 * stations_here * hours * members_here * all_comps,
            bytes_accessed=2 * stations_here * (hours * members_here + all_comps)
            + 4 * hours * members_here * all_comps,
            transcendentals=0,
        ),
        scalars=1,
    )(lax.axis_index("state").reshape(1).astype(jnp.int32), by_member, loadings)
    smoothed_parts = []
    residual_parts = []
    fitted_parts = []
    last = [halving_stages(halves[2 * c], halves[2 * c + 1], "state") for c in range(CHUNKS)]
    kept, outgoing, pairs = last[0]
    received = lax.ppermute(outgoing, "state", pairs)
    later = [(k, o) for k, o, _ in last[1:]]
    by_hour, kept, received, later = lax.optimization_barrier((by_hour, kept, received, later))
    addends = [(kept, received)] + [
        (k, lax.ppermute(o, "state", last[c + 1][2])) for c, (k, o) in enumerate(later)
    ]
    for chunk in range(CHUNKS):
        kept, received = addends[chunk]
        kept = kept.reshape(hours, chunk_members, comps)
        received = received.reshape(hours, chunk_members, comps)
        smoothed_here = vmem_call(
            recurrence_kernel,
            jax.ShapeDtypeStruct(kept.shape, jnp.float32),
            3,
            pl.CostEstimate(
                flops=6 * hours * chunk_members * comps,
                bytes_accessed=12 * hours * chunk_members * comps,
                transcendentals=0,
            ),
        )(decay_all, kept, received)
        gathered = lax.all_to_all(smoothed_here, "tm", split_axis=0, concat_axis=1, tiled=True)
        rounded = gathered.astype(jnp.bfloat16)
        pieces, earlier = doubling_gather(rounded, "state", fitted_parts[-1:])
        fitted_parts[-1:] = earlier
        slab_hours, width, _ = rounded.shape
        fitted = vmem_call(
            fitted_kernel,
            jax.ShapeDtypeStruct((slab_hours, stations_here, width), jnp.float32),
            1 + len(pieces),
            pl.CostEstimate(
                flops=2 * stations_here * slab_hours * width * all_comps,
                bytes_accessed=2 * stations_here * all_comps
                + 2 * slab_hours * width * all_comps
                + 4 * slab_hours * stations_here * width,
                transcendentals=0,
            ),
            scalars=1,
        )(lax.axis_index("state").reshape(1).astype(jnp.int32), loadings, *pieces)
        fitted_parts.append(fitted)
        smoothed_parts.append(jnp.transpose(gathered, (2, 0, 1)))
    for chunk, fitted in enumerate(fitted_parts):
        low = chunk * members // CHUNKS
        picked = by_hour[:, :, low:low + members // CHUNKS]
        residual_parts.append(picked.astype(jnp.float32) - jnp.transpose(fitted, (1, 0, 2)))
    return (
        jnp.concatenate(smoothed_parts, axis=2),
        jnp.concatenate(residual_parts, axis=2),
    )


def solution(mesh):
    return jax.shard_map(
        local,
        mesh=mesh,
        in_specs=(
            P(("state", "tm"), None, None),
            P(("state", "tm"), None),
            P("state", None),
            P("tm", "state"),
        ),
        out_specs=(P("state", "tm", None), P("state", "tm", None)),
        check_vma=False,
    )
```

```python
import functools

import jax
import jax.numpy as jnp
from jax import lax
from jax.experimental import pallas as pl
from jax.experimental.pallas import tpu as pltpu
from jax.sharding import PartitionSpec as P

CHUNKS = 2


def information_kernel(hours, stations, me_ref, x_ref, l_ref, *out_refs):
    me = me_ref[0]
    chunks = len(out_refs) // 2
    levels = out_refs[0].ndim - 1
    rows, width = out_refs[0].shape[-2:]
    senders = x_ref.shape[0]
    flipped = x_ref[:, :stations, :].reshape(senders * stations, x_ref.shape[2]).T
    for slot in range(2 ** levels):
        relative = tuple((slot >> level) & 1 for level in range(levels))
        block = 0
        for level in range(levels):
            block = block + ((relative[level] ^ ((me >> level) & 1) ^ 1) << level)
        columns = l_ref[:, pl.ds(pl.multiple_of(block * width, width), width)]
        total = jnp.dot(flipped, columns, preferred_element_type=jnp.float32)
        total = total.reshape(hours, chunks, rows // hours, width)
        for chunk in range(chunks):
            target = out_refs[2 * chunk + relative[0]]
            target[relative[1:]] = total[:, chunk].reshape(rows, width)


def halving_stages(outgoing, keep, axis):
    count = lax.axis_size(axis)
    level = 0
    pairs = [(i, i ^ 1) for i in range(count)]
    while keep.ndim > 2:
        received = lax.ppermute(outgoing, axis, pairs)
        level += 1
        outgoing = keep[0] + received[0]
        keep = keep[1] + received[1]
        pairs = [(i, i ^ (1 << level)) for i in range(count)]
    return keep, outgoing, pairs


def doubling_gather(block, axis, companion):
    count = lax.axis_size(axis)
    levels = count.bit_length() - 1
    pieces = [block]
    for level in reversed(range(levels)):
        pairs = [(i, i ^ (1 << level)) for i in range(count)]
        pieces = pieces + [lax.ppermute(piece, axis, pairs) for piece in pieces]
        if level == levels - 1:
            pieces, companion = lax.optimization_barrier((pieces, companion))
    return pieces, companion


def fitted_kernel(me_ref, l_ref, *refs):
    *piece_refs, observed_ref, out_ref = refs
    me = me_ref[0]
    levels = len(piece_refs).bit_length() - 1
    hours, members, width = piece_refs[0].shape
    total = None
    for position, piece_ref in enumerate(piece_refs):
        flipped = 0
        for level in range(levels):
            flipped |= ((position >> level) & 1) << (levels - 1 - level)
        block = me ^ flipped
        columns = l_ref[:, pl.ds(pl.multiple_of(block * width, width), width)]
        piece = piece_ref[...].reshape(hours * members, width)
        part = lax.dot_general(
            columns, piece, (((1,), (1,)), ((), ())),
            preferred_element_type=jnp.float32,
        )
        total = part if total is None else total + part
    for hour in range(hours):
        observed = observed_ref[hour].astype(jnp.float32)
        out_ref[hour] = observed - total[:, hour * members:(hour + 1) * members]


def recurrence_kernel(rate_ref, keep_ref, received_ref, out_ref):
    hours = out_ref.shape[0]
    state = jnp.zeros(out_ref.shape[1:], jnp.float32)
    for hour in range(hours):
        state = rate_ref[pl.ds(hour, 1), :] * state + (keep_ref[hour] + received_ref[hour])
        out_ref[hour] = state
    state = jnp.zeros(out_ref.shape[1:], jnp.float32)
    for hour in reversed(range(hours)):
        rate = rate_ref[pl.ds(hour, 1), :]
        state = rate * state + (1.0 - rate * rate) * out_ref[hour]
        out_ref[hour] = state


def vmem_call(kernel, out_shape, count, cost, scalars=0):
    return pl.pallas_call(
        kernel,
        out_shape=out_shape,
        in_specs=[pl.BlockSpec(memory_space=pltpu.SMEM)] * scalars
        + [pl.BlockSpec(memory_space=pltpu.VMEM)] * count,
        out_specs=jax.tree.map(lambda _: pl.BlockSpec(memory_space=pltpu.VMEM), out_shape),
        cost_estimate=cost,
    )


def local(obs, mask, loadings, decay):
    tm_count = lax.axis_size("tm")
    state_count = lax.axis_size("state")
    levels = state_count.bit_length() - 1
    stations_local, hours, members = obs.shape
    members_here = members // tm_count
    chunk_members = members_here // CHUNKS
    masked = obs * mask[:, :, None].astype(obs.dtype)
    outgoing = jnp.transpose(
        masked.reshape(stations_local, hours, CHUNKS, tm_count, chunk_members),
        (3, 0, 1, 2, 4),
    ).reshape(tm_count, stations_local, hours * members_here)
    high = lax.reduce_precision(decay, exponent_bits=8, mantissa_bits=7)
    middle = lax.reduce_precision(decay - high, exponent_bits=8, mantissa_bits=7)
    low = decay - high - middle
    pieces = jnp.stack([high, middle, low]).astype(obs.dtype).reshape(-1, hours * members_here)
    spare = (-(stations_local + pieces.shape[0])) % 16
    pieces = jnp.pad(pieces, ((0, spare), (0, 0)))
    pieces = jnp.broadcast_to(pieces[None], (tm_count,) + pieces.shape)
    outgoing = jnp.concatenate([outgoing, pieces], axis=1)
    by_member = lax.all_to_all(outgoing, "tm", split_axis=0, concat_axis=0, tiled=True)
    stations_here = tm_count * stations_local
    slab_hours, comps_here = decay.shape
    arrived = by_member[:, stations_local:stations_local + 3 * slab_hours * comps_here // (hours * members_here)]
    arrived = arrived.reshape(tm_count, 3, slab_hours, comps_here).astype(jnp.float32)
    decay_all = (arrived[:, 0] + arrived[:, 1] + arrived[:, 2]).reshape(hours, comps_here)
    masked_later, by_member = lax.optimization_barrier((masked, by_member))
    by_hour = lax.all_to_all(masked_later, "tm", split_axis=1, concat_axis=0, tiled=True)
    all_comps = loadings.shape[1]
    comps = all_comps // state_count
    rows = hours * chunk_members
    half = jax.ShapeDtypeStruct((2,) * (levels - 1) + (rows, comps), jnp.float32)
    halves = vmem_call(
        functools.partial(information_kernel, hours, stations_local),
        (half,) * (2 * CHUNKS),
        2,
        pl.CostEstimate(
            flops=2 * stations_here * hours * members_here * all_comps,
            bytes_accessed=2 * stations_here * (hours * members_here + all_comps)
            + 4 * hours * members_here * all_comps,
            transcendentals=0,
        ),
        scalars=1,
    )(lax.axis_index("state").reshape(1).astype(jnp.int32), by_member, loadings)
    smoothed_parts = []
    residual_parts = []
    fitted_parts = []
    last = [halving_stages(halves[2 * c], halves[2 * c + 1], "state") for c in range(CHUNKS)]
    kept, outgoing, pairs = last[0]
    received = lax.ppermute(outgoing, "state", pairs)
    later = [(k, o) for k, o, _ in last[1:]]
    by_hour, kept, received, later = lax.optimization_barrier((by_hour, kept, received, later))
    addends = [(kept, received)] + [
        (k, lax.ppermute(o, "state", last[c + 1][2])) for c, (k, o) in enumerate(later)
    ]
    for chunk in range(CHUNKS):
        kept, received = addends[chunk]
        kept = kept.reshape(hours, chunk_members, comps)
        received = received.reshape(hours, chunk_members, comps)
        smoothed_here = vmem_call(
            recurrence_kernel,
            jax.ShapeDtypeStruct(kept.shape, jnp.float32),
            3,
            pl.CostEstimate(
                flops=6 * hours * chunk_members * comps,
                bytes_accessed=12 * hours * chunk_members * comps,
                transcendentals=0,
            ),
        )(decay_all, kept, received)
        gathered = lax.all_to_all(smoothed_here, "tm", split_axis=0, concat_axis=1, tiled=True)
        rounded = gathered.astype(jnp.bfloat16)
        pieces, earlier = doubling_gather(rounded, "state", fitted_parts[-1:])
        fitted_parts[-1:] = earlier
        slab_hours, width, _ = rounded.shape
        low = chunk * members // CHUNKS
        observed = jnp.transpose(by_hour[:, :, low:low + members // CHUNKS], (1, 0, 2))
        fitted = vmem_call(
            fitted_kernel,
            jax.ShapeDtypeStruct((slab_hours, stations_here, width), jnp.float32),
            2 + len(pieces),
            pl.CostEstimate(
                flops=2 * stations_here * slab_hours * width * all_comps,
                bytes_accessed=2 * stations_here * all_comps
                + 2 * slab_hours * width * all_comps
                + 4 * slab_hours * stations_here * width,
                transcendentals=0,
            ),
            scalars=1,
        )(lax.axis_index("state").reshape(1).astype(jnp.int32), loadings, *pieces, observed)
        fitted_parts.append(fitted)
        smoothed_parts.append(jnp.transpose(gathered, (2, 0, 1)))
    for residual in fitted_parts:
        residual_parts.append(jnp.transpose(residual, (1, 0, 2)))
    return (
        jnp.concatenate(smoothed_parts, axis=2),
        jnp.concatenate(residual_parts, axis=2),
    )


def solution(mesh):
    return jax.shard_map(
        local,
        mesh=mesh,
        in_specs=(
            P(("state", "tm"), None, None),
            P(("state", "tm"), None),
            P("state", None),
            P("tm", "state"),
        ),
        out_specs=(P("state", "tm", None), P("state", "tm", None)),
        check_vma=False,
    )
```

```python
import functools

import jax
import jax.numpy as jnp
from jax import lax
from jax.experimental import pallas as pl
from jax.experimental.pallas import tpu as pltpu
from jax.sharding import PartitionSpec as P

CHUNKS = 4


def information_kernel(hours, stations, me_ref, x_ref, l_ref, *out_refs):
    me = me_ref[0]
    chunks = len(out_refs) // 2
    levels = out_refs[0].ndim - 1
    rows, width = out_refs[0].shape[-2:]
    senders = x_ref.shape[0]
    flipped = x_ref[:, :stations, :].reshape(senders * stations, x_ref.shape[2]).T
    for slot in range(2 ** levels):
        relative = tuple((slot >> level) & 1 for level in range(levels))
        block = 0
        for level in range(levels):
            block = block + ((relative[level] ^ ((me >> level) & 1) ^ 1) << level)
        columns = l_ref[:, pl.ds(pl.multiple_of(block * width, width), width)]
        total = jnp.dot(flipped, columns, preferred_element_type=jnp.float32)
        total = total.reshape(hours, chunks, rows // hours, width)
        for chunk in range(chunks):
            target = out_refs[2 * chunk + relative[0]]
            target[relative[1:]] = total[:, chunk].reshape(rows, width)


def halving_stages(outgoing, keep, axis):
    count = lax.axis_size(axis)
    level = 0
    pairs = [(i, i ^ 1) for i in range(count)]
    while keep.ndim > 2:
        received = lax.ppermute(outgoing, axis, pairs)
        level += 1
        outgoing = keep[0] + received[0]
        keep = keep[1] + received[1]
        pairs = [(i, i ^ (1 << level)) for i in range(count)]
    return keep, outgoing, pairs


def doubling_gather(block, axis, companion):
    count = lax.axis_size(axis)
    levels = count.bit_length() - 1
    pieces = [block]
    for level in reversed(range(levels)):
        pairs = [(i, i ^ (1 << level)) for i in range(count)]
        pieces = pieces + [lax.ppermute(piece, axis, pairs) for piece in pieces]
        if level == levels - 1:
            pieces, companion = lax.optimization_barrier((pieces, companion))
    return pieces, companion


def fitted_kernel(me_ref, l_ref, *refs):
    *piece_refs, out_ref = refs
    me = me_ref[0]
    levels = len(piece_refs).bit_length() - 1
    width = piece_refs[0].shape[-1]
    for hour in range(out_ref.shape[0]):
        total = None
        for position, piece_ref in enumerate(piece_refs):
            flipped = 0
            for level in range(levels):
                flipped |= ((position >> level) & 1) << (levels - 1 - level)
            block = me ^ flipped
            columns = l_ref[:, pl.ds(pl.multiple_of(block * width, width), width)]
            part = lax.dot_general(
                columns, piece_ref[hour], (((1,), (1,)), ((), ())),
                preferred_element_type=jnp.float32,
            )
            total = part if total is None else total + part
        out_ref[hour] = total


def recurrence_kernel(rate_ref, keep_ref, received_ref, out_ref):
    hours = out_ref.shape[0]
    state = jnp.zeros(out_ref.shape[1:], jnp.float32)
    for hour in range(hours):
        state = rate_ref[pl.ds(hour, 1), :] * state + (keep_ref[hour] + received_ref[hour])
        out_ref[hour] = state
    state = jnp.zeros(out_ref.shape[1:], jnp.float32)
    for hour in reversed(range(hours)):
        rate = rate_ref[pl.ds(hour, 1), :]
        state = rate * state + (1.0 - rate * rate) * out_ref[hour]
        out_ref[hour] = state


def vmem_call(kernel, out_shape, count, cost, scalars=0):
    return pl.pallas_call(
        kernel,
        out_shape=out_shape,
        in_specs=[pl.BlockSpec(memory_space=pltpu.SMEM)] * scalars
        + [pl.BlockSpec(memory_space=pltpu.VMEM)] * count,
        out_specs=jax.tree.map(lambda _: pl.BlockSpec(memory_space=pltpu.VMEM), out_shape),
        cost_estimate=cost,
    )


def local(obs, mask, loadings, decay):
    tm_count = lax.axis_size("tm")
    state_count = lax.axis_size("state")
    levels = state_count.bit_length() - 1
    stations_local, hours, members = obs.shape
    members_here = members // tm_count
    chunk_members = members_here // CHUNKS
    masked = obs * mask[:, :, None].astype(obs.dtype)
    outgoing = jnp.transpose(
        masked.reshape(stations_local, hours, CHUNKS, tm_count, chunk_members),
        (3, 0, 1, 2, 4),
    ).reshape(tm_count, stations_local, hours * members_here)
    high = lax.reduce_precision(decay, exponent_bits=8, mantissa_bits=7)
    middle = lax.reduce_precision(decay - high, exponent_bits=8, mantissa_bits=7)
    low = decay - high - middle
    pieces = jnp.stack([high, middle, low]).astype(obs.dtype).reshape(-1, hours * members_here)
    spare = (-(stations_local + pieces.shape[0])) % 16
    pieces = jnp.pad(pieces, ((0, spare), (0, 0)))
    pieces = jnp.broadcast_to(pieces[None], (tm_count,) + pieces.shape)
    outgoing = jnp.concatenate([outgoing, pieces], axis=1)
    by_member = lax.all_to_all(outgoing, "tm", split_axis=0, concat_axis=0, tiled=True)
    stations_here = tm_count * stations_local
    slab_hours, comps_here = decay.shape
    arrived = by_member[:, stations_local:stations_local + 3 * slab_hours * comps_here // (hours * members_here)]
    arrived = arrived.reshape(tm_count, 3, slab_hours, comps_here).astype(jnp.float32)
    decay_all = (arrived[:, 0] + arrived[:, 1] + arrived[:, 2]).reshape(hours, comps_here)
    masked_later, by_member = lax.optimization_barrier((masked, by_member))
    by_hour = lax.all_to_all(masked_later, "tm", split_axis=1, concat_axis=0, tiled=True)
    all_comps = loadings.shape[1]
    comps = all_comps // state_count
    rows = hours * chunk_members
    half = jax.ShapeDtypeStruct((2,) * (levels - 1) + (rows, comps), jnp.float32)
    halves = vmem_call(
        functools.partial(information_kernel, hours, stations_local),
        (half,) * (2 * CHUNKS),
        2,
        pl.CostEstimate(
            flops=2 * stations_here * hours * members_here * all_comps,
            bytes_accessed=2 * stations_here * (hours * members_here + all_comps)
            + 4 * hours * members_here * all_comps,
            transcendentals=0,
        ),
        scalars=1,
    )(lax.axis_index("state").reshape(1).astype(jnp.int32), by_member, loadings)
    smoothed_parts = []
    residual_parts = []
    fitted_parts = []
    last = [halving_stages(halves[2 * c], halves[2 * c + 1], "state") for c in range(CHUNKS)]
    kept, outgoing, pairs = last[0]
    received = lax.ppermute(outgoing, "state", pairs)
    later = [(k, o) for k, o, _ in last[1:]]
    by_hour, kept, received, later = lax.optimization_barrier((by_hour, kept, received, later))
    addends = [(kept, received)] + [
        (k, lax.ppermute(o, "state", last[c + 1][2])) for c, (k, o) in enumerate(later)
    ]
    for chunk in range(CHUNKS):
        kept, received = addends[chunk]
        kept = kept.reshape(hours, chunk_members, comps)
        received = received.reshape(hours, chunk_members, comps)
        smoothed_here = vmem_call(
            recurrence_kernel,
            jax.ShapeDtypeStruct(kept.shape, jnp.float32),
            3,
            pl.CostEstimate(
                flops=6 * hours * chunk_members * comps,
                bytes_accessed=12 * hours * chunk_members * comps,
                transcendentals=0,
            ),
        )(decay_all, kept, received)
        gathered = lax.all_to_all(smoothed_here, "tm", split_axis=0, concat_axis=1, tiled=True)
        rounded = gathered.astype(jnp.bfloat16)
        pieces, earlier = doubling_gather(rounded, "state", fitted_parts[-1:])
        fitted_parts[-1:] = earlier
        slab_hours, width, _ = rounded.shape
        fitted = vmem_call(
            fitted_kernel,
            jax.ShapeDtypeStruct((slab_hours, stations_here, width), jnp.float32),
            1 + len(pieces),
            pl.CostEstimate(
                flops=2 * stations_here * slab_hours * width * all_comps,
                bytes_accessed=2 * stations_here * all_comps
                + 2 * slab_hours * width * all_comps
                + 4 * slab_hours * stations_here * width,
                transcendentals=0,
            ),
            scalars=1,
        )(lax.axis_index("state").reshape(1).astype(jnp.int32), loadings, *pieces)
        fitted_parts.append(fitted)
        smoothed_parts.append(jnp.transpose(gathered, (2, 0, 1)))
    for chunk, fitted in enumerate(fitted_parts):
        low = chunk * members // CHUNKS
        picked = by_hour[:, :, low:low + members // CHUNKS]
        residual_parts.append(picked.astype(jnp.float32) - jnp.transpose(fitted, (1, 0, 2)))
    return (
        jnp.concatenate(smoothed_parts, axis=2),
        jnp.concatenate(residual_parts, axis=2),
    )


def solution(mesh):
    return jax.shard_map(
        local,
        mesh=mesh,
        in_specs=(
            P(("state", "tm"), None, None),
            P(("state", "tm"), None),
            P("state", None),
            P("tm", "state"),
        ),
        out_specs=(P("state", "tm", None), P("state", "tm", None)),
        check_vma=False,
    )
```

```python
import functools

import jax
import jax.numpy as jnp
from jax import lax
from jax.experimental import pallas as pl
from jax.experimental.pallas import tpu as pltpu
from jax.sharding import PartitionSpec as P

CHUNKS = 2


def information_kernel(hours, stations, me_ref, x_ref, l_ref, *refs):
    *out_refs, total_ref = refs
    me = me_ref[0]
    chunks = len(out_refs) // 2
    levels = out_refs[0].ndim - 1
    rows, width = out_refs[0].shape[-2:]
    senders = x_ref.shape[0]
    flipped = x_ref[:, :stations, :].reshape(senders * stations, x_ref.shape[2]).T
    total_ref[...] = jnp.dot(flipped, l_ref[...], preferred_element_type=jnp.float32)
    for slot in range(2 ** levels):
        relative = tuple((slot >> level) & 1 for level in range(levels))
        block = 0
        for level in range(levels):
            block = block + ((relative[level] ^ ((me >> level) & 1) ^ 1) << level)
        total = total_ref[:, pl.ds(pl.multiple_of(block * width, width), width)]
        total = total.reshape(hours, chunks, rows // hours, width)
        for chunk in range(chunks):
            target = out_refs[2 * chunk + relative[0]]
            target[relative[1:]] = total[:, chunk].reshape(rows, width)


def halving_stages(outgoing, keep, axis):
    count = lax.axis_size(axis)
    level = 0
    pairs = [(i, i ^ 1) for i in range(count)]
    while keep.ndim > 2:
        received = lax.ppermute(outgoing, axis, pairs)
        level += 1
        outgoing = keep[0] + received[0]
        keep = keep[1] + received[1]
        pairs = [(i, i ^ (1 << level)) for i in range(count)]
    return keep, outgoing, pairs


def doubling_gather(block, axis, companion):
    count = lax.axis_size(axis)
    levels = count.bit_length() - 1
    pieces = [block]
    for level in reversed(range(levels)):
        pairs = [(i, i ^ (1 << level)) for i in range(count)]
        pieces = pieces + [lax.ppermute(piece, axis, pairs) for piece in pieces]
        if level == levels - 1:
            pieces, companion = lax.optimization_barrier((pieces, companion))
    return pieces, companion


def fitted_kernel(me_ref, l_ref, *refs):
    *piece_refs, out_ref = refs
    me = me_ref[0]
    levels = len(piece_refs).bit_length() - 1
    width = piece_refs[0].shape[-1]
    for hour in range(out_ref.shape[0]):
        total = None
        for position, piece_ref in enumerate(piece_refs):
            flipped = 0
            for level in range(levels):
                flipped |= ((position >> level) & 1) << (levels - 1 - level)
            block = me ^ flipped
            columns = l_ref[:, pl.ds(pl.multiple_of(block * width, width), width)]
            part = lax.dot_general(
                columns, piece_ref[hour], (((1,), (1,)), ((), ())),
                preferred_element_type=jnp.float32,
            )
            total = part if total is None else total + part
        out_ref[hour] = total


def recurrence_kernel(rate_ref, keep_ref, received_ref, out_ref):
    hours = out_ref.shape[0]
    state = jnp.zeros(out_ref.shape[1:], jnp.float32)
    for hour in range(hours):
        state = rate_ref[pl.ds(hour, 1), :] * state + (keep_ref[hour] + received_ref[hour])
        out_ref[hour] = state
    state = jnp.zeros(out_ref.shape[1:], jnp.float32)
    for hour in reversed(range(hours)):
        rate = rate_ref[pl.ds(hour, 1), :]
        state = rate * state + (1.0 - rate * rate) * out_ref[hour]
        out_ref[hour] = state


def vmem_call(kernel, out_shape, count, cost, scalars=0, scratch=()):
    return pl.pallas_call(
        kernel,
        out_shape=out_shape,
        scratch_shapes=list(scratch),
        in_specs=[pl.BlockSpec(memory_space=pltpu.SMEM)] * scalars
        + [pl.BlockSpec(memory_space=pltpu.VMEM)] * count,
        out_specs=jax.tree.map(lambda _: pl.BlockSpec(memory_space=pltpu.VMEM), out_shape),
        cost_estimate=cost,
    )


def local(obs, mask, loadings, decay):
    tm_count = lax.axis_size("tm")
    state_count = lax.axis_size("state")
    levels = state_count.bit_length() - 1
    stations_local, hours, members = obs.shape
    members_here = members // tm_count
    chunk_members = members_here // CHUNKS
    masked = obs * mask[:, :, None].astype(obs.dtype)
    outgoing = jnp.transpose(
        masked.reshape(stations_local, hours, CHUNKS, tm_count, chunk_members),
        (3, 0, 1, 2, 4),
    ).reshape(tm_count, stations_local, hours * members_here)
    high = lax.reduce_precision(decay, exponent_bits=8, mantissa_bits=7)
    middle = lax.reduce_precision(decay - high, exponent_bits=8, mantissa_bits=7)
    low = decay - high - middle
    pieces = jnp.stack([high, middle, low]).astype(obs.dtype).reshape(-1, hours * members_here)
    spare = (-(stations_local + pieces.shape[0])) % 16
    pieces = jnp.pad(pieces, ((0, spare), (0, 0)))
    pieces = jnp.broadcast_to(pieces[None], (tm_count,) + pieces.shape)
    outgoing = jnp.concatenate([outgoing, pieces], axis=1)
    by_member = lax.all_to_all(outgoing, "tm", split_axis=0, concat_axis=0, tiled=True)
    stations_here = tm_count * stations_local
    slab_hours, comps_here = decay.shape
    arrived = by_member[:, stations_local:stations_local + 3 * slab_hours * comps_here // (hours * members_here)]
    arrived = arrived.reshape(tm_count, 3, slab_hours, comps_here).astype(jnp.float32)
    decay_all = (arrived[:, 0] + arrived[:, 1] + arrived[:, 2]).reshape(hours, comps_here)
    masked_later, by_member = lax.optimization_barrier((masked, by_member))
    by_hour = lax.all_to_all(masked_later, "tm", split_axis=1, concat_axis=0, tiled=True)
    all_comps = loadings.shape[1]
    comps = all_comps // state_count
    rows = hours * chunk_members
    half = jax.ShapeDtypeStruct((2,) * (levels - 1) + (rows, comps), jnp.float32)
    halves = vmem_call(
        functools.partial(information_kernel, hours, stations_local),
        (half,) * (2 * CHUNKS),
        2,
        pl.CostEstimate(
            flops=2 * stations_here * hours * members_here * all_comps,
            bytes_accessed=2 * stations_here * (hours * members_here + all_comps)
            + 4 * hours * members_here * all_comps,
            transcendentals=0,
        ),
        scalars=1,
        scratch=[pltpu.VMEM((hours * members_here, all_comps), jnp.float32)],
    )(lax.axis_index("state").reshape(1).astype(jnp.int32), by_member, loadings)
    smoothed_parts = []
    residual_parts = []
    fitted_parts = []
    last = [halving_stages(halves[2 * c], halves[2 * c + 1], "state") for c in range(CHUNKS)]
    kept, outgoing, pairs = last[0]
    received = lax.ppermute(outgoing, "state", pairs)
    later = [(k, o) for k, o, _ in last[1:]]
    by_hour, kept, received, later = lax.optimization_barrier((by_hour, kept, received, later))
    addends = [(kept, received)] + [
        (k, lax.ppermute(o, "state", last[c + 1][2])) for c, (k, o) in enumerate(later)
    ]
    for chunk in range(CHUNKS):
        kept, received = addends[chunk]
        kept = kept.reshape(hours, chunk_members, comps)
        received = received.reshape(hours, chunk_members, comps)
        smoothed_here = vmem_call(
            recurrence_kernel,
            jax.ShapeDtypeStruct(kept.shape, jnp.float32),
            3,
            pl.CostEstimate(
                flops=6 * hours * chunk_members * comps,
                bytes_accessed=12 * hours * chunk_members * comps,
                transcendentals=0,
            ),
        )(decay_all, kept, received)
        gathered = lax.all_to_all(smoothed_here, "tm", split_axis=0, concat_axis=1, tiled=True)
        rounded = gathered.astype(jnp.bfloat16)
        pieces, earlier = doubling_gather(rounded, "state", fitted_parts[-1:])
        fitted_parts[-1:] = earlier
        slab_hours, width, _ = rounded.shape
        fitted = vmem_call(
            fitted_kernel,
            jax.ShapeDtypeStruct((slab_hours, stations_here, width), jnp.float32),
            1 + len(pieces),
            pl.CostEstimate(
                flops=2 * stations_here * slab_hours * width * all_comps,
                bytes_accessed=2 * stations_here * all_comps
                + 2 * slab_hours * width * all_comps
                + 4 * slab_hours * stations_here * width,
                transcendentals=0,
            ),
            scalars=1,
        )(lax.axis_index("state").reshape(1).astype(jnp.int32), loadings, *pieces)
        fitted_parts.append(fitted)
        smoothed_parts.append(jnp.transpose(gathered, (2, 0, 1)))
    for chunk, fitted in enumerate(fitted_parts):
        low = chunk * members // CHUNKS
        picked = by_hour[:, :, low:low + members // CHUNKS]
        residual_parts.append(picked.astype(jnp.float32) - jnp.transpose(fitted, (1, 0, 2)))
    return (
        jnp.concatenate(smoothed_parts, axis=2),
        jnp.concatenate(residual_parts, axis=2),
    )


def solution(mesh):
    return jax.shard_map(
        local,
        mesh=mesh,
        in_specs=(
            P(("state", "tm"), None, None),
            P(("state", "tm"), None),
            P("state", None),
            P("tm", "state"),
        ),
        out_specs=(P("state", "tm", None), P("state", "tm", None)),
        check_vma=False,
    )
```

```python
import functools

import jax
import jax.numpy as jnp
from jax import lax
from jax.experimental import pallas as pl
from jax.experimental.pallas import tpu as pltpu
from jax.sharding import PartitionSpec as P

CHUNKS = 2


def information_kernel(hours, stations, me_ref, x_ref, l_ref, *out_refs):
    me = me_ref[0]
    chunks = len(out_refs) // 2
    levels = out_refs[0].ndim - 1
    rows, width = out_refs[0].shape[-2:]
    senders = x_ref.shape[0]
    flipped = x_ref[:, :stations, :].reshape(senders * stations, x_ref.shape[2]).T
    for slot in range(2 ** levels):
        relative = tuple((slot >> level) & 1 for level in range(levels))
        block = 0
        for level in range(levels):
            block = block + ((relative[level] ^ ((me >> level) & 1) ^ 1) << level)
        columns = l_ref[:, pl.ds(pl.multiple_of(block * width, width), width)]
        total = jnp.dot(flipped, columns, preferred_element_type=jnp.float32)
        total = total.reshape(hours, chunks, rows // hours, width)
        for chunk in range(chunks):
            target = out_refs[2 * chunk + relative[0]]
            target[relative[1:]] = total[:, chunk].reshape(rows, width)


def halving_stages(outgoing, keep, axis):
    count = lax.axis_size(axis)
    level = 0
    pairs = [(i, i ^ 1) for i in range(count)]
    while keep.ndim > 2:
        received = lax.ppermute(outgoing, axis, pairs)
        level += 1
        outgoing = keep[0] + received[0]
        keep = keep[1] + received[1]
        pairs = [(i, i ^ (1 << level)) for i in range(count)]
    return keep, outgoing, pairs


def doubling_gather(block, axis, companion):
    count = lax.axis_size(axis)
    levels = count.bit_length() - 1
    pieces = [block]
    for level in reversed(range(levels)):
        pairs = [(i, i ^ (1 << level)) for i in range(count)]
        pieces = pieces + [lax.ppermute(piece, axis, pairs) for piece in pieces]
        if level == levels - 1:
            pieces, companion = lax.optimization_barrier((pieces, companion))
    return pieces, companion


def fitted_kernel(me_ref, l_ref, *refs):
    *piece_refs, out_ref = refs
    me = me_ref[0]
    levels = len(piece_refs).bit_length() - 1
    width = piece_refs[0].shape[-1]
    for hour in range(out_ref.shape[0]):
        total = None
        for position, piece_ref in enumerate(piece_refs):
            flipped = 0
            for level in range(levels):
                flipped |= ((position >> level) & 1) << (levels - 1 - level)
            block = me ^ flipped
            columns = l_ref[:, pl.ds(pl.multiple_of(block * width, width), width)]
            part = lax.dot_general(
                columns, piece_ref[hour], (((1,), (1,)), ((), ())),
                preferred_element_type=jnp.float32,
            )
            total = part if total is None else total + part
        out_ref[hour] = total


def recurrence_kernel(rate_ref, keep_ref, received_ref, out_ref):
    hours = out_ref.shape[0]
    state = jnp.zeros(out_ref.shape[1:], jnp.float32)
    for hour in range(hours):
        state = rate_ref[pl.ds(hour, 1), :] * state + (keep_ref[hour] + received_ref[hour])
        out_ref[hour] = state
    state = jnp.zeros(out_ref.shape[1:], jnp.float32)
    for hour in reversed(range(hours)):
        rate = rate_ref[pl.ds(hour, 1), :]
        state = rate * state + (1.0 - rate * rate) * out_ref[hour]
        out_ref[hour] = state


def vmem_call(kernel, out_shape, count, cost, scalars=0):
    return pl.pallas_call(
        kernel,
        out_shape=out_shape,
        in_specs=[pl.BlockSpec(memory_space=pltpu.SMEM)] * scalars
        + [pl.BlockSpec(memory_space=pltpu.VMEM)] * count,
        out_specs=jax.tree.map(lambda _: pl.BlockSpec(memory_space=pltpu.VMEM), out_shape),
        cost_estimate=cost,
    )


def local(obs, mask, loadings, decay):
    tm_count = lax.axis_size("tm")
    state_count = lax.axis_size("state")
    levels = state_count.bit_length() - 1
    stations_local, hours, members = obs.shape
    members_here = members // tm_count
    chunk_members = members_here // CHUNKS
    masked = obs * mask[:, :, None].astype(obs.dtype)
    outgoing = jnp.transpose(
        masked.reshape(stations_local, hours, CHUNKS, tm_count, chunk_members),
        (3, 0, 1, 2, 4),
    ).reshape(tm_count, stations_local, hours * members_here)
    high = lax.reduce_precision(decay, exponent_bits=8, mantissa_bits=7)
    middle = lax.reduce_precision(decay - high, exponent_bits=8, mantissa_bits=7)
    low = decay - high - middle
    pieces = jnp.stack([high, middle, low]).astype(obs.dtype).reshape(-1, hours * members_here)
    spare = (-(stations_local + pieces.shape[0])) % 8
    pieces = jnp.pad(pieces, ((0, spare), (0, 0)))
    pieces = jnp.broadcast_to(pieces[None], (tm_count,) + pieces.shape)
    outgoing = jnp.concatenate([outgoing, pieces], axis=1)
    by_member = lax.all_to_all(outgoing, "tm", split_axis=0, concat_axis=0, tiled=True)
    stations_here = tm_count * stations_local
    slab_hours, comps_here = decay.shape
    arrived = by_member[:, stations_local:stations_local + 3 * slab_hours * comps_here // (hours * members_here)]
    arrived = arrived.reshape(tm_count, 3, slab_hours, comps_here).astype(jnp.float32)
    decay_all = (arrived[:, 0] + arrived[:, 1] + arrived[:, 2]).reshape(hours, comps_here)
    masked_later, by_member = lax.optimization_barrier((masked, by_member))
    by_hour = lax.all_to_all(masked_later, "tm", split_axis=1, concat_axis=0, tiled=True)
    all_comps = loadings.shape[1]
    comps = all_comps // state_count
    rows = hours * chunk_members
    half = jax.ShapeDtypeStruct((2,) * (levels - 1) + (rows, comps), jnp.float32)
    halves = vmem_call(
        functools.partial(information_kernel, hours, stations_local),
        (half,) * (2 * CHUNKS),
        2,
        pl.CostEstimate(
            flops=2 * stations_here * hours * members_here * all_comps,
            bytes_accessed=2 * stations_here * (hours * members_here + all_comps)
            + 4 * hours * members_here * all_comps,
            transcendentals=0,
        ),
        scalars=1,
    )(lax.axis_index("state").reshape(1).astype(jnp.int32), by_member, loadings)
    smoothed_parts = []
    residual_parts = []
    fitted_parts = []
    last = [halving_stages(halves[2 * c], halves[2 * c + 1], "state") for c in range(CHUNKS)]
    kept, outgoing, pairs = last[0]
    received = lax.ppermute(outgoing, "state", pairs)
    later = [(k, o) for k, o, _ in last[1:]]
    by_hour, kept, received, later = lax.optimization_barrier((by_hour, kept, received, later))
    addends = [(kept, received)] + [
        (k, lax.ppermute(o, "state", last[c + 1][2])) for c, (k, o) in enumerate(later)
    ]
    for chunk in range(CHUNKS):
        kept, received = addends[chunk]
        kept = kept.reshape(hours, chunk_members, comps)
        received = received.reshape(hours, chunk_members, comps)
        smoothed_here = vmem_call(
            recurrence_kernel,
            jax.ShapeDtypeStruct(kept.shape, jnp.float32),
            3,
            pl.CostEstimate(
                flops=6 * hours * chunk_members * comps,
                bytes_accessed=12 * hours * chunk_members * comps,
                transcendentals=0,
            ),
        )(decay_all, kept, received)
        gathered = lax.all_to_all(smoothed_here, "tm", split_axis=0, concat_axis=1, tiled=True)
        rounded = gathered.astype(jnp.bfloat16)
        pieces, earlier = doubling_gather(rounded, "state", fitted_parts[-1:])
        fitted_parts[-1:] = earlier
        slab_hours, width, _ = rounded.shape
        fitted = vmem_call(
            fitted_kernel,
            jax.ShapeDtypeStruct((slab_hours, stations_here, width), jnp.float32),
            1 + len(pieces),
            pl.CostEstimate(
                flops=2 * stations_here * slab_hours * width * all_comps,
                bytes_accessed=2 * stations_here * all_comps
                + 2 * slab_hours * width * all_comps
                + 4 * slab_hours * stations_here * width,
                transcendentals=0,
            ),
            scalars=1,
        )(lax.axis_index("state").reshape(1).astype(jnp.int32), loadings, *pieces)
        fitted_parts.append(fitted)
        smoothed_parts.append(jnp.transpose(gathered, (2, 0, 1)))
    for chunk, fitted in enumerate(fitted_parts):
        low = chunk * members // CHUNKS
        picked = by_hour[:, :, low:low + members // CHUNKS]
        residual_parts.append(picked.astype(jnp.float32) - jnp.transpose(fitted, (1, 0, 2)))
    return (
        jnp.concatenate(smoothed_parts, axis=2),
        jnp.concatenate(residual_parts, axis=2),
    )


def solution(mesh):
    return jax.shard_map(
        local,
        mesh=mesh,
        in_specs=(
            P(("state", "tm"), None, None),
            P(("state", "tm"), None),
            P("state", None),
            P("tm", "state"),
        ),
        out_specs=(P("state", "tm", None), P("state", "tm", None)),
        check_vma=False,
    )
```

```python
import functools

import jax
import jax.numpy as jnp
from jax import lax
from jax.experimental import pallas as pl
from jax.experimental.pallas import tpu as pltpu
from jax.sharding import PartitionSpec as P

CHUNKS = 2


def information_kernel(hours, stations, me_ref, x_ref, l_ref, *out_refs):
    me = me_ref[0]
    chunks = len(out_refs) // 2
    levels = out_refs[0].ndim - 1
    rows, width = out_refs[0].shape[-2:]
    senders = x_ref.shape[0]
    flipped = x_ref[:, :stations, :].reshape(senders * stations, x_ref.shape[2]).T
    for slot in range(2 ** levels):
        relative = tuple((slot >> level) & 1 for level in range(levels))
        block = 0
        for level in range(levels):
            block = block + ((relative[level] ^ ((me >> level) & 1) ^ 1) << level)
        columns = l_ref[:, pl.ds(pl.multiple_of(block * width, width), width)]
        total = jnp.dot(flipped, columns, preferred_element_type=jnp.float32)
        total = total.reshape(hours, chunks, rows // hours, width)
        for chunk in range(chunks):
            target = out_refs[2 * chunk + relative[0]]
            target[relative[1:]] = total[:, chunk].reshape(rows, width)


def halving_stages(outgoing, keep, axis):
    count = lax.axis_size(axis)
    level = 0
    pairs = [(i, i ^ 1) for i in range(count)]
    while keep.ndim > 2:
        received = lax.ppermute(outgoing, axis, pairs)
        level += 1
        outgoing = keep[0] + received[0]
        keep = keep[1] + received[1]
        pairs = [(i, i ^ (1 << level)) for i in range(count)]
    return keep, outgoing, pairs


def doubling_gather(block, axis, companion):
    count = lax.axis_size(axis)
    levels = count.bit_length() - 1
    pieces = [block]
    for level in reversed(range(levels)):
        pairs = [(i, i ^ (1 << level)) for i in range(count)]
        pieces = pieces + [lax.ppermute(piece, axis, pairs) for piece in pieces]
        if level == levels - 1:
            pieces, companion = lax.optimization_barrier((pieces, companion))
    return pieces, companion


def fitted_kernel(me_ref, l_ref, *refs):
    *piece_refs, out_ref = refs
    me = me_ref[0]
    levels = len(piece_refs).bit_length() - 1
    width = piece_refs[0].shape[-1]
    hours, members, _ = piece_refs[0].shape
    total = None
    for position, piece_ref in enumerate(piece_refs):
        flipped = 0
        for level in range(levels):
            flipped |= ((position >> level) & 1) << (levels - 1 - level)
        block = me ^ flipped
        columns = l_ref[:, pl.ds(pl.multiple_of(block * width, width), width)]
        piece = piece_ref[...].reshape(hours * members, width)
        part = lax.dot_general(
            columns, piece, (((1,), (1,)), ((), ())),
            preferred_element_type=jnp.float32,
        )
        total = part if total is None else total + part
    for hour in range(hours):
        out_ref[hour] = total[:, hour * members:(hour + 1) * members]


def recurrence_kernel(rate_ref, keep_ref, received_ref, out_ref):
    hours = out_ref.shape[0]
    state = jnp.zeros(out_ref.shape[1:], jnp.float32)
    for hour in range(hours):
        state = rate_ref[pl.ds(hour, 1), :] * state + (keep_ref[hour] + received_ref[hour])
        out_ref[hour] = state
    state = jnp.zeros(out_ref.shape[1:], jnp.float32)
    for hour in reversed(range(hours)):
        rate = rate_ref[pl.ds(hour, 1), :]
        state = rate * state + (1.0 - rate * rate) * out_ref[hour]
        out_ref[hour] = state


def vmem_call(kernel, out_shape, count, cost, scalars=0):
    return pl.pallas_call(
        kernel,
        out_shape=out_shape,
        in_specs=[pl.BlockSpec(memory_space=pltpu.SMEM)] * scalars
        + [pl.BlockSpec(memory_space=pltpu.VMEM)] * count,
        out_specs=jax.tree.map(lambda _: pl.BlockSpec(memory_space=pltpu.VMEM), out_shape),
        cost_estimate=cost,
    )


def local(obs, mask, loadings, decay):
    tm_count = lax.axis_size("tm")
    state_count = lax.axis_size("state")
    levels = state_count.bit_length() - 1
    stations_local, hours, members = obs.shape
    members_here = members // tm_count
    chunk_members = members_here // CHUNKS
    masked = obs * mask[:, :, None].astype(obs.dtype)
    outgoing = jnp.transpose(
        masked.reshape(stations_local, hours, CHUNKS, tm_count, chunk_members),
        (3, 0, 1, 2, 4),
    ).reshape(tm_count, stations_local, hours * members_here)
    high = lax.reduce_precision(decay, exponent_bits=8, mantissa_bits=7)
    middle = lax.reduce_precision(decay - high, exponent_bits=8, mantissa_bits=7)
    low = decay - high - middle
    pieces = jnp.stack([high, middle, low]).astype(obs.dtype).reshape(-1, hours * members_here)
    spare = (-(stations_local + pieces.shape[0])) % 8
    pieces = jnp.pad(pieces, ((0, spare), (0, 0)))
    pieces = jnp.broadcast_to(pieces[None], (tm_count,) + pieces.shape)
    outgoing = jnp.concatenate([outgoing, pieces], axis=1)
    by_member = lax.all_to_all(outgoing, "tm", split_axis=0, concat_axis=0, tiled=True)
    stations_here = tm_count * stations_local
    slab_hours, comps_here = decay.shape
    arrived = by_member[:, stations_local:stations_local + 3 * slab_hours * comps_here // (hours * members_here)]
    arrived = arrived.reshape(tm_count, 3, slab_hours, comps_here).astype(jnp.float32)
    decay_all = (arrived[:, 0] + arrived[:, 1] + arrived[:, 2]).reshape(hours, comps_here)
    masked_later, by_member = lax.optimization_barrier((masked, by_member))
    by_hour = lax.all_to_all(masked_later, "tm", split_axis=1, concat_axis=0, tiled=True)
    all_comps = loadings.shape[1]
    comps = all_comps // state_count
    rows = hours * chunk_members
    half = jax.ShapeDtypeStruct((2,) * (levels - 1) + (rows, comps), jnp.float32)
    halves = vmem_call(
        functools.partial(information_kernel, hours, stations_local),
        (half,) * (2 * CHUNKS),
        2,
        pl.CostEstimate(
            flops=2 * stations_here * hours * members_here * all_comps,
            bytes_accessed=2 * stations_here * (hours * members_here + all_comps)
            + 4 * hours * members_here * all_comps,
            transcendentals=0,
        ),
        scalars=1,
    )(lax.axis_index("state").reshape(1).astype(jnp.int32), by_member, loadings)
    smoothed_parts = []
    residual_parts = []
    fitted_parts = []
    last = [halving_stages(halves[2 * c], halves[2 * c + 1], "state") for c in range(CHUNKS)]
    kept, outgoing, pairs = last[0]
    received = lax.ppermute(outgoing, "state", pairs)
    later = [(k, o) for k, o, _ in last[1:]]
    by_hour, kept, received, later = lax.optimization_barrier((by_hour, kept, received, later))
    addends = [(kept, received)] + [
        (k, lax.ppermute(o, "state", last[c + 1][2])) for c, (k, o) in enumerate(later)
    ]
    for chunk in range(CHUNKS):
        kept, received = addends[chunk]
        kept = kept.reshape(hours, chunk_members, comps)
        received = received.reshape(hours, chunk_members, comps)
        smoothed_here = vmem_call(
            recurrence_kernel,
            jax.ShapeDtypeStruct(kept.shape, jnp.float32),
            3,
            pl.CostEstimate(
                flops=6 * hours * chunk_members * comps,
                bytes_accessed=12 * hours * chunk_members * comps,
                transcendentals=0,
            ),
        )(decay_all, kept, received)
        gathered = lax.all_to_all(smoothed_here, "tm", split_axis=0, concat_axis=1, tiled=True)
        rounded = gathered.astype(jnp.bfloat16)
        pieces, earlier = doubling_gather(rounded, "state", fitted_parts[-1:])
        fitted_parts[-1:] = earlier
        slab_hours, width, _ = rounded.shape
        fitted = vmem_call(
            fitted_kernel,
            jax.ShapeDtypeStruct((slab_hours, stations_here, width), jnp.float32),
            1 + len(pieces),
            pl.CostEstimate(
                flops=2 * stations_here * slab_hours * width * all_comps,
                bytes_accessed=2 * stations_here * all_comps
                + 2 * slab_hours * width * all_comps
                + 4 * slab_hours * stations_here * width,
                transcendentals=0,
            ),
            scalars=1,
        )(lax.axis_index("state").reshape(1).astype(jnp.int32), loadings, *pieces)
        fitted_parts.append(fitted)
        smoothed_parts.append(jnp.transpose(gathered, (2, 0, 1)))
    for chunk, fitted in enumerate(fitted_parts):
        low = chunk * members // CHUNKS
        picked = by_hour[:, :, low:low + members // CHUNKS]
        residual_parts.append(picked.astype(jnp.float32) - jnp.transpose(fitted, (1, 0, 2)))
    return (
        jnp.concatenate(smoothed_parts, axis=2),
        jnp.concatenate(residual_parts, axis=2),
    )


def solution(mesh):
    return jax.shard_map(
        local,
        mesh=mesh,
        in_specs=(
            P(("state", "tm"), None, None),
            P(("state", "tm"), None),
            P("state", None),
            P("tm", "state"),
        ),
        out_specs=(P("state", "tm", None), P("state", "tm", None)),
        check_vma=False,
    )
```

```python
import functools

import jax
import jax.numpy as jnp
from jax import lax
from jax.experimental import pallas as pl
from jax.experimental.pallas import tpu as pltpu
from jax.sharding import PartitionSpec as P

CHUNKS = 2


def information_kernel(hours, stations, me_ref, x_ref, l_ref, *out_refs):
    me = me_ref[0]
    chunks = len(out_refs) // 2
    levels = out_refs[0].ndim - 1
    rows, width = out_refs[0].shape[-2:]
    senders = x_ref.shape[0]
    flipped = x_ref[:, :stations, :].reshape(senders * stations, x_ref.shape[2]).T
    for slot in range(2 ** levels):
        relative = tuple((slot >> level) & 1 for level in range(levels))
        block = 0
        for level in range(levels):
            block = block + ((relative[level] ^ ((me >> level) & 1) ^ 1) << level)
        columns = l_ref[:, pl.ds(pl.multiple_of(block * width, width), width)]
        total = jnp.dot(flipped, columns, preferred_element_type=jnp.float32)
        total = total.reshape(hours, chunks, rows // hours, width)
        for chunk in range(chunks):
            target = out_refs[2 * chunk + relative[0]]
            target[relative[1:]] = total[:, chunk].reshape(rows, width)


def halving_stages(outgoing, keep, axis):
    count = lax.axis_size(axis)
    level = 0
    pairs = [(i, i ^ 1) for i in range(count)]
    parts = (keep,)
    while keep.ndim > 2:
        received = lax.ppermute(outgoing, axis, pairs)
        level += 1
        outgoing = keep[0] + received[0]
        if keep.ndim == 3:
            parts = (keep[1], received[1])
            keep = keep[1]
        else:
            keep = keep[1] + received[1]
            parts = (keep,)
        pairs = [(i, i ^ (1 << level)) for i in range(count)]
    return parts, outgoing, pairs


def doubling_gather(block, axis, companion):
    count = lax.axis_size(axis)
    levels = count.bit_length() - 1
    pieces = [block]
    for level in reversed(range(levels)):
        pairs = [(i, i ^ (1 << level)) for i in range(count)]
        pieces = pieces + [lax.ppermute(piece, axis, pairs) for piece in pieces]
        if level == levels - 1:
            pieces, companion = lax.optimization_barrier((pieces, companion))
    return pieces, companion


def fitted_kernel(me_ref, l_ref, *refs):
    *piece_refs, out_ref = refs
    me = me_ref[0]
    levels = len(piece_refs).bit_length() - 1
    width = piece_refs[0].shape[-1]
    hours, members, _ = piece_refs[0].shape
    total = None
    for position, piece_ref in enumerate(piece_refs):
        flipped = 0
        for level in range(levels):
            flipped |= ((position >> level) & 1) << (levels - 1 - level)
        block = me ^ flipped
        columns = l_ref[:, pl.ds(pl.multiple_of(block * width, width), width)]
        piece = piece_ref[...].reshape(hours * members, width)
        part = lax.dot_general(
            columns, piece, (((1,), (1,)), ((), ())),
            preferred_element_type=jnp.float32,
        )
        total = part if total is None else total + part
    for hour in range(hours):
        out_ref[hour] = total[:, hour * members:(hour + 1) * members]


def recurrence_kernel(rate_ref, *refs):
    *addend_refs, out_ref = refs
    hours = out_ref.shape[0]
    state = jnp.zeros(out_ref.shape[1:], jnp.float32)
    for hour in range(hours):
        information = addend_refs[0][hour]
        for addend_ref in addend_refs[1:]:
            information = information + addend_ref[hour]
        state = rate_ref[pl.ds(hour, 1), :] * state + information
        out_ref[hour] = state
    state = jnp.zeros(out_ref.shape[1:], jnp.float32)
    for hour in reversed(range(hours)):
        rate = rate_ref[pl.ds(hour, 1), :]
        state = rate * state + (1.0 - rate * rate) * out_ref[hour]
        out_ref[hour] = state


def vmem_call(kernel, out_shape, count, cost, scalars=0):
    return pl.pallas_call(
        kernel,
        out_shape=out_shape,
        in_specs=[pl.BlockSpec(memory_space=pltpu.SMEM)] * scalars
        + [pl.BlockSpec(memory_space=pltpu.VMEM)] * count,
        out_specs=jax.tree.map(lambda _: pl.BlockSpec(memory_space=pltpu.VMEM), out_shape),
        cost_estimate=cost,
    )


def local(obs, mask, loadings, decay):
    tm_count = lax.axis_size("tm")
    state_count = lax.axis_size("state")
    levels = state_count.bit_length() - 1
    stations_local, hours, members = obs.shape
    members_here = members // tm_count
    chunk_members = members_here // CHUNKS
    masked = obs * mask[:, :, None].astype(obs.dtype)
    outgoing = jnp.transpose(
        masked.reshape(stations_local, hours, CHUNKS, tm_count, chunk_members),
        (3, 0, 1, 2, 4),
    ).reshape(tm_count, stations_local, hours * members_here)
    high = lax.reduce_precision(decay, exponent_bits=8, mantissa_bits=7)
    middle = lax.reduce_precision(decay - high, exponent_bits=8, mantissa_bits=7)
    low = decay - high - middle
    pieces = jnp.stack([high, middle, low]).astype(obs.dtype).reshape(-1, hours * members_here)
    spare = (-(stations_local + pieces.shape[0])) % 8
    pieces = jnp.pad(pieces, ((0, spare), (0, 0)))
    pieces = jnp.broadcast_to(pieces[None], (tm_count,) + pieces.shape)
    outgoing = jnp.concatenate([outgoing, pieces], axis=1)
    by_member = lax.all_to_all(outgoing, "tm", split_axis=0, concat_axis=0, tiled=True)
    stations_here = tm_count * stations_local
    slab_hours, comps_here = decay.shape
    arrived = by_member[:, stations_local:stations_local + 3 * slab_hours * comps_here // (hours * members_here)]
    arrived = arrived.reshape(tm_count, 3, slab_hours, comps_here).astype(jnp.float32)
    decay_all = (arrived[:, 0] + arrived[:, 1] + arrived[:, 2]).reshape(hours, comps_here)
    masked_later, by_member = lax.optimization_barrier((masked, by_member))
    by_hour = lax.all_to_all(masked_later, "tm", split_axis=1, concat_axis=0, tiled=True)
    all_comps = loadings.shape[1]
    comps = all_comps // state_count
    rows = hours * chunk_members
    half = jax.ShapeDtypeStruct((2,) * (levels - 1) + (rows, comps), jnp.float32)
    halves = vmem_call(
        functools.partial(information_kernel, hours, stations_local),
        (half,) * (2 * CHUNKS),
        2,
        pl.CostEstimate(
            flops=2 * stations_here * hours * members_here * all_comps,
            bytes_accessed=2 * stations_here * (hours * members_here + all_comps)
            + 4 * hours * members_here * all_comps,
            transcendentals=0,
        ),
        scalars=1,
    )(lax.axis_index("state").reshape(1).astype(jnp.int32), by_member, loadings)
    smoothed_parts = []
    residual_parts = []
    fitted_parts = []
    last = [halving_stages(halves[2 * c], halves[2 * c + 1], "state") for c in range(CHUNKS)]
    kept, outgoing, pairs = last[0]
    received = lax.ppermute(outgoing, "state", pairs)
    later = [(k, o) for k, o, _ in last[1:]]
    by_hour, kept, received, later = lax.optimization_barrier((by_hour, kept, received, later))
    addends = [(kept, received)] + [
        (k, lax.ppermute(o, "state", last[c + 1][2])) for c, (k, o) in enumerate(later)
    ]
    for chunk in range(CHUNKS):
        kept, received = addends[chunk]
        parts = [a.reshape(hours, chunk_members, comps) for a in kept + (received,)]
        smoothed_here = vmem_call(
            recurrence_kernel,
            jax.ShapeDtypeStruct(parts[0].shape, jnp.float32),
            1 + len(parts),
            pl.CostEstimate(
                flops=6 * hours * chunk_members * comps,
                bytes_accessed=12 * hours * chunk_members * comps,
                transcendentals=0,
            ),
        )(decay_all, *parts)
        gathered = lax.all_to_all(smoothed_here, "tm", split_axis=0, concat_axis=1, tiled=True)
        rounded = gathered.astype(jnp.bfloat16)
        pieces, earlier = doubling_gather(rounded, "state", fitted_parts[-1:])
        fitted_parts[-1:] = earlier
        slab_hours, width, _ = rounded.shape
        fitted = vmem_call(
            fitted_kernel,
            jax.ShapeDtypeStruct((slab_hours, stations_here, width), jnp.float32),
            1 + len(pieces),
            pl.CostEstimate(
                flops=2 * stations_here * slab_hours * width * all_comps,
                bytes_accessed=2 * stations_here * all_comps
                + 2 * slab_hours * width * all_comps
                + 4 * slab_hours * stations_here * width,
                transcendentals=0,
            ),
            scalars=1,
        )(lax.axis_index("state").reshape(1).astype(jnp.int32), loadings, *pieces)
        fitted_parts.append(fitted)
        smoothed_parts.append(jnp.transpose(gathered, (2, 0, 1)))
    for chunk, fitted in enumerate(fitted_parts):
        low = chunk * members // CHUNKS
        picked = by_hour[:, :, low:low + members // CHUNKS]
        residual_parts.append(picked.astype(jnp.float32) - jnp.transpose(fitted, (1, 0, 2)))
    return (
        jnp.concatenate(smoothed_parts, axis=2),
        jnp.concatenate(residual_parts, axis=2),
    )


def solution(mesh):
    return jax.shard_map(
        local,
        mesh=mesh,
        in_specs=(
            P(("state", "tm"), None, None),
            P(("state", "tm"), None),
            P("state", None),
            P("tm", "state"),
        ),
        out_specs=(P("state", "tm", None), P("state", "tm", None)),
        check_vma=False,
    )
```

```python
import functools

import jax
import jax.numpy as jnp
from jax import lax
from jax.experimental import pallas as pl
from jax.experimental.pallas import tpu as pltpu
from jax.sharding import PartitionSpec as P

CHUNKS = 2


def information_kernel(hours, stations, me_ref, x_ref, l_ref, *out_refs):
    me = me_ref[0]
    chunks = len(out_refs) // 2
    levels = out_refs[0].ndim - 1
    rows, width = out_refs[0].shape[-2:]
    senders = x_ref.shape[0]
    flipped = x_ref[:, :stations, :].reshape(senders * stations, x_ref.shape[2]).T
    for slot in range(2 ** levels):
        relative = tuple((slot >> level) & 1 for level in range(levels))
        block = 0
        for level in range(levels):
            block = block + ((relative[level] ^ ((me >> level) & 1) ^ 1) << level)
        columns = l_ref[:, pl.ds(pl.multiple_of(block * width, width), width)]
        total = jnp.dot(flipped, columns, preferred_element_type=jnp.float32)
        total = total.reshape(hours, chunks, rows // hours, width)
        for chunk in range(chunks):
            target = out_refs[2 * chunk + relative[0]]
            target[relative[1:]] = total[:, chunk].reshape(rows, width)


def halving_stages(outgoing, keep, axis):
    count = lax.axis_size(axis)
    level = 0
    pairs = [(i, i ^ 1) for i in range(count)]
    while keep.ndim > 2:
        received = lax.ppermute(outgoing, axis, pairs)
        level += 1
        outgoing = keep[0] + received[0]
        keep = keep[1] + received[1]
        pairs = [(i, i ^ (1 << level)) for i in range(count)]
    return keep, outgoing, pairs


def doubling_gather(block, axis, companion):
    count = lax.axis_size(axis)
    levels = count.bit_length() - 1
    pieces = [block]
    for level in reversed(range(levels)):
        pairs = [(i, i ^ (1 << level)) for i in range(count)]
        pieces = pieces + [lax.ppermute(piece, axis, pairs) for piece in pieces]
        if level == levels - 1:
            pieces, companion = lax.optimization_barrier((pieces, companion))
    return pieces, companion


def fitted_kernel(me_ref, l_ref, *refs):
    *piece_refs, out_ref = refs
    me = me_ref[0]
    levels = len(piece_refs).bit_length() - 1
    width = piece_refs[0].shape[-1]
    hours, members, _ = piece_refs[0].shape
    total = None
    for position, piece_ref in enumerate(piece_refs):
        flipped = 0
        for level in range(levels):
            flipped |= ((position >> level) & 1) << (levels - 1 - level)
        block = me ^ flipped
        columns = l_ref[:, pl.ds(pl.multiple_of(block * width, width), width)]
        piece = piece_ref[...].reshape(hours * members, width)
        part = lax.dot_general(
            columns, piece, (((1,), (1,)), ((), ())),
            preferred_element_type=jnp.float32,
        )
        total = part if total is None else total + part
    for hour in range(hours):
        out_ref[:, hour, :] = total[:, hour * members:(hour + 1) * members]


def recurrence_kernel(rate_ref, keep_ref, received_ref, out_ref):
    hours = out_ref.shape[0]
    state = jnp.zeros(out_ref.shape[1:], jnp.float32)
    for hour in range(hours):
        state = rate_ref[pl.ds(hour, 1), :] * state + (keep_ref[hour] + received_ref[hour])
        out_ref[hour] = state
    state = jnp.zeros(out_ref.shape[1:], jnp.float32)
    for hour in reversed(range(hours)):
        rate = rate_ref[pl.ds(hour, 1), :]
        state = rate * state + (1.0 - rate * rate) * out_ref[hour]
        out_ref[hour] = state


def vmem_call(kernel, out_shape, count, cost, scalars=0):
    return pl.pallas_call(
        kernel,
        out_shape=out_shape,
        in_specs=[pl.BlockSpec(memory_space=pltpu.SMEM)] * scalars
        + [pl.BlockSpec(memory_space=pltpu.VMEM)] * count,
        out_specs=jax.tree.map(lambda _: pl.BlockSpec(memory_space=pltpu.VMEM), out_shape),
        cost_estimate=cost,
    )


def local(obs, mask, loadings, decay):
    tm_count = lax.axis_size("tm")
    state_count = lax.axis_size("state")
    levels = state_count.bit_length() - 1
    stations_local, hours, members = obs.shape
    members_here = members // tm_count
    chunk_members = members_here // CHUNKS
    masked = obs * mask[:, :, None].astype(obs.dtype)
    outgoing = jnp.transpose(
        masked.reshape(stations_local, hours, CHUNKS, tm_count, chunk_members),
        (3, 0, 1, 2, 4),
    ).reshape(tm_count, stations_local, hours * members_here)
    high = lax.reduce_precision(decay, exponent_bits=8, mantissa_bits=7)
    middle = lax.reduce_precision(decay - high, exponent_bits=8, mantissa_bits=7)
    low = decay - high - middle
    pieces = jnp.stack([high, middle, low]).astype(obs.dtype).reshape(-1, hours * members_here)
    spare = (-(stations_local + pieces.shape[0])) % 8
    pieces = jnp.pad(pieces, ((0, spare), (0, 0)))
    pieces = jnp.broadcast_to(pieces[None], (tm_count,) + pieces.shape)
    outgoing = jnp.concatenate([outgoing, pieces], axis=1)
    by_member = lax.all_to_all(outgoing, "tm", split_axis=0, concat_axis=0, tiled=True)
    stations_here = tm_count * stations_local
    slab_hours, comps_here = decay.shape
    arrived = by_member[:, stations_local:stations_local + 3 * slab_hours * comps_here // (hours * members_here)]
    arrived = arrived.reshape(tm_count, 3, slab_hours, comps_here).astype(jnp.float32)
    decay_all = (arrived[:, 0] + arrived[:, 1] + arrived[:, 2]).reshape(hours, comps_here)
    masked_later, by_member = lax.optimization_barrier((masked, by_member))
    by_hour = lax.all_to_all(masked_later, "tm", split_axis=1, concat_axis=0, tiled=True)
    all_comps = loadings.shape[1]
    comps = all_comps // state_count
    rows = hours * chunk_members
    half = jax.ShapeDtypeStruct((2,) * (levels - 1) + (rows, comps), jnp.float32)
    halves = vmem_call(
        functools.partial(information_kernel, hours, stations_local),
        (half,) * (2 * CHUNKS),
        2,
        pl.CostEstimate(
            flops=2 * stations_here * hours * members_here * all_comps,
            bytes_accessed=2 * stations_here * (hours * members_here + all_comps)
            + 4 * hours * members_here * all_comps,
            transcendentals=0,
        ),
        scalars=1,
    )(lax.axis_index("state").reshape(1).astype(jnp.int32), by_member, loadings)
    smoothed_parts = []
    residual_parts = []
    fitted_parts = []
    last = [halving_stages(halves[2 * c], halves[2 * c + 1], "state") for c in range(CHUNKS)]
    kept, outgoing, pairs = last[0]
    received = lax.ppermute(outgoing, "state", pairs)
    later = [(k, o) for k, o, _ in last[1:]]
    by_hour, kept, received, later = lax.optimization_barrier((by_hour, kept, received, later))
    addends = [(kept, received)] + [
        (k, lax.ppermute(o, "state", last[c + 1][2])) for c, (k, o) in enumerate(later)
    ]
    for chunk in range(CHUNKS):
        kept, received = addends[chunk]
        kept = kept.reshape(hours, chunk_members, comps)
        received = received.reshape(hours, chunk_members, comps)
        smoothed_here = vmem_call(
            recurrence_kernel,
            jax.ShapeDtypeStruct(kept.shape, jnp.float32),
            3,
            pl.CostEstimate(
                flops=6 * hours * chunk_members * comps,
                bytes_accessed=12 * hours * chunk_members * comps,
                transcendentals=0,
            ),
        )(decay_all, kept, received)
        gathered = lax.all_to_all(smoothed_here, "tm", split_axis=0, concat_axis=1, tiled=True)
        rounded = gathered.astype(jnp.bfloat16)
        pieces, earlier = doubling_gather(rounded, "state", fitted_parts[-1:])
        fitted_parts[-1:] = earlier
        slab_hours, width, _ = rounded.shape
        fitted = vmem_call(
            fitted_kernel,
            jax.ShapeDtypeStruct((stations_here, slab_hours, width), jnp.float32),
            1 + len(pieces),
            pl.CostEstimate(
                flops=2 * stations_here * slab_hours * width * all_comps,
                bytes_accessed=2 * stations_here * all_comps
                + 2 * slab_hours * width * all_comps
                + 4 * slab_hours * stations_here * width,
                transcendentals=0,
            ),
            scalars=1,
        )(lax.axis_index("state").reshape(1).astype(jnp.int32), loadings, *pieces)
        fitted_parts.append(fitted)
        smoothed_parts.append(jnp.transpose(gathered, (2, 0, 1)))
    for chunk, fitted in enumerate(fitted_parts):
        low = chunk * members // CHUNKS
        picked = by_hour[:, :, low:low + members // CHUNKS]
        residual_parts.append(picked.astype(jnp.float32) - fitted)
    return (
        jnp.concatenate(smoothed_parts, axis=2),
        jnp.concatenate(residual_parts, axis=2),
    )


def solution(mesh):
    return jax.shard_map(
        local,
        mesh=mesh,
        in_specs=(
            P(("state", "tm"), None, None),
            P(("state", "tm"), None),
            P("state", None),
            P("tm", "state"),
        ),
        out_specs=(P("state", "tm", None), P("state", "tm", None)),
        check_vma=False,
    )
```

```python
import functools

import jax
import jax.numpy as jnp
from jax import lax
from jax.experimental import pallas as pl
from jax.experimental.pallas import tpu as pltpu
from jax.sharding import PartitionSpec as P

CHUNKS = 2


def information_kernel(hours, stations, me_ref, x_ref, l_ref, *out_refs):
    me = me_ref[0]
    chunks = len(out_refs) // 2
    levels = out_refs[0].ndim - 1
    rows, width = out_refs[0].shape[-2:]
    senders = x_ref.shape[0]
    flipped = x_ref[:, :stations, :].reshape(senders * stations, x_ref.shape[2]).T
    for slot in range(2 ** levels):
        relative = tuple((slot >> level) & 1 for level in range(levels))
        block = 0
        for level in range(levels):
            block = block + ((relative[level] ^ ((me >> level) & 1) ^ 1) << level)
        columns = l_ref[:, pl.ds(pl.multiple_of(block * width, width), width)]
        total = jnp.dot(flipped, columns, preferred_element_type=jnp.float32)
        total = total.reshape(hours, chunks, rows // hours, width)
        for chunk in range(chunks):
            target = out_refs[2 * chunk + relative[0]]
            target[relative[1:]] = total[:, chunk].reshape(rows, width)


def halving_stages(outgoing, keep, axis):
    count = lax.axis_size(axis)
    level = 0
    pairs = [(i, i ^ 1) for i in range(count)]
    while keep.ndim > 2:
        received = lax.ppermute(outgoing, axis, pairs)
        level += 1
        outgoing = keep[0] + received[0]
        keep = keep[1] + received[1]
        pairs = [(i, i ^ (1 << level)) for i in range(count)]
    return keep, outgoing, pairs


def doubling_gather(block, axis, companion):
    count = lax.axis_size(axis)
    levels = count.bit_length() - 1
    pieces = [block]
    for level in reversed(range(levels)):
        pairs = [(i, i ^ (1 << level)) for i in range(count)]
        pieces = pieces + [lax.ppermute(piece, axis, pairs) for piece in pieces]
        if level == levels - 1:
            pieces, companion = lax.optimization_barrier((pieces, companion))
    return pieces, companion


def fitted_kernel(chunk, count, me_ref, l_ref, *refs):
    piece_refs = refs[:count]
    observed_ref = refs[count]
    earlier_ref = refs[count + 1] if chunk else None
    out_ref = refs[-1]
    me = me_ref[0]
    levels = len(piece_refs).bit_length() - 1
    hours, members, width = piece_refs[0].shape
    total = None
    for position, piece_ref in enumerate(piece_refs):
        flipped = 0
        for level in range(levels):
            flipped |= ((position >> level) & 1) << (levels - 1 - level)
        block = me ^ flipped
        columns = l_ref[:, pl.ds(pl.multiple_of(block * width, width), width)]
        piece = piece_ref[...].reshape(hours * members, width)
        part = lax.dot_general(
            columns, piece, (((1,), (1,)), ((), ())),
            preferred_element_type=jnp.float32,
        )
        total = part if total is None else total + part
    low = chunk * members
    if chunk:
        out_ref[:, :, :low] = earlier_ref[:, :, :low]
    for hour in range(hours):
        observed = observed_ref[:, hour, low:low + members].astype(jnp.float32)
        out_ref[:, hour, low:low + members] = (
            observed - total[:, hour * members:(hour + 1) * members]
        )


def recurrence_kernel(rate_ref, keep_ref, received_ref, out_ref):
    hours = out_ref.shape[0]
    state = jnp.zeros(out_ref.shape[1:], jnp.float32)
    for hour in range(hours):
        state = rate_ref[pl.ds(hour, 1), :] * state + (keep_ref[hour] + received_ref[hour])
        out_ref[hour] = state
    state = jnp.zeros(out_ref.shape[1:], jnp.float32)
    for hour in reversed(range(hours)):
        rate = rate_ref[pl.ds(hour, 1), :]
        state = rate * state + (1.0 - rate * rate) * out_ref[hour]
        out_ref[hour] = state


def vmem_call(kernel, out_shape, count, cost, scalars=0):
    return pl.pallas_call(
        kernel,
        out_shape=out_shape,
        in_specs=[pl.BlockSpec(memory_space=pltpu.SMEM)] * scalars
        + [pl.BlockSpec(memory_space=pltpu.VMEM)] * count,
        out_specs=jax.tree.map(lambda _: pl.BlockSpec(memory_space=pltpu.VMEM), out_shape),
        cost_estimate=cost,
    )


def local(obs, mask, loadings, decay):
    tm_count = lax.axis_size("tm")
    state_count = lax.axis_size("state")
    levels = state_count.bit_length() - 1
    stations_local, hours, members = obs.shape
    members_here = members // tm_count
    chunk_members = members_here // CHUNKS
    masked = obs * mask[:, :, None].astype(obs.dtype)
    outgoing = jnp.transpose(
        masked.reshape(stations_local, hours, CHUNKS, tm_count, chunk_members),
        (3, 0, 1, 2, 4),
    ).reshape(tm_count, stations_local, hours * members_here)
    high = lax.reduce_precision(decay, exponent_bits=8, mantissa_bits=7)
    middle = lax.reduce_precision(decay - high, exponent_bits=8, mantissa_bits=7)
    low = decay - high - middle
    pieces = jnp.stack([high, middle, low]).astype(obs.dtype).reshape(-1, hours * members_here)
    spare = (-(stations_local + pieces.shape[0])) % 8
    pieces = jnp.pad(pieces, ((0, spare), (0, 0)))
    pieces = jnp.broadcast_to(pieces[None], (tm_count,) + pieces.shape)
    outgoing = jnp.concatenate([outgoing, pieces], axis=1)
    by_member = lax.all_to_all(outgoing, "tm", split_axis=0, concat_axis=0, tiled=True)
    stations_here = tm_count * stations_local
    slab_hours, comps_here = decay.shape
    arrived = by_member[:, stations_local:stations_local + 3 * slab_hours * comps_here // (hours * members_here)]
    arrived = arrived.reshape(tm_count, 3, slab_hours, comps_here).astype(jnp.float32)
    decay_all = (arrived[:, 0] + arrived[:, 1] + arrived[:, 2]).reshape(hours, comps_here)
    masked_later, by_member = lax.optimization_barrier((masked, by_member))
    by_hour = lax.all_to_all(masked_later, "tm", split_axis=1, concat_axis=0, tiled=True)
    all_comps = loadings.shape[1]
    comps = all_comps // state_count
    rows = hours * chunk_members
    half = jax.ShapeDtypeStruct((2,) * (levels - 1) + (rows, comps), jnp.float32)
    halves = vmem_call(
        functools.partial(information_kernel, hours, stations_local),
        (half,) * (2 * CHUNKS),
        2,
        pl.CostEstimate(
            flops=2 * stations_here * hours * members_here * all_comps,
            bytes_accessed=2 * stations_here * (hours * members_here + all_comps)
            + 4 * hours * members_here * all_comps,
            transcendentals=0,
        ),
        scalars=1,
    )(lax.axis_index("state").reshape(1).astype(jnp.int32), by_member, loadings)
    smoothed_parts = []
    residual_parts = []
    fitted_parts = []
    last = [halving_stages(halves[2 * c], halves[2 * c + 1], "state") for c in range(CHUNKS)]
    kept, outgoing, pairs = last[0]
    received = lax.ppermute(outgoing, "state", pairs)
    later = [(k, o) for k, o, _ in last[1:]]
    by_hour, kept, received, later = lax.optimization_barrier((by_hour, kept, received, later))
    addends = [(kept, received)] + [
        (k, lax.ppermute(o, "state", last[c + 1][2])) for c, (k, o) in enumerate(later)
    ]
    for chunk in range(CHUNKS):
        kept, received = addends[chunk]
        kept = kept.reshape(hours, chunk_members, comps)
        received = received.reshape(hours, chunk_members, comps)
        smoothed_here = vmem_call(
            recurrence_kernel,
            jax.ShapeDtypeStruct(kept.shape, jnp.float32),
            3,
            pl.CostEstimate(
                flops=6 * hours * chunk_members * comps,
                bytes_accessed=12 * hours * chunk_members * comps,
                transcendentals=0,
            ),
        )(decay_all, kept, received)
        gathered = lax.all_to_all(smoothed_here, "tm", split_axis=0, concat_axis=1, tiled=True)
        rounded = gathered.astype(jnp.bfloat16)
        pieces, earlier = doubling_gather(rounded, "state", fitted_parts[-1:])
        fitted_parts[-1:] = earlier
        slab_hours, width, _ = rounded.shape
        extra = [fitted_parts[-1]] if fitted_parts else []
        fitted = pl.pallas_call(
            functools.partial(fitted_kernel, chunk, len(pieces)),
            out_shape=jax.ShapeDtypeStruct(by_hour.shape, jnp.float32),
            in_specs=[pl.BlockSpec(memory_space=pltpu.SMEM)]
            + [pl.BlockSpec(memory_space=pltpu.VMEM)] * (2 + len(pieces) + len(extra)),
            out_specs=pl.BlockSpec(memory_space=pltpu.VMEM),
            input_output_aliases={3 + len(pieces): 0} if extra else {},
            cost_estimate=pl.CostEstimate(
                flops=2 * stations_here * slab_hours * width * all_comps,
                bytes_accessed=2 * stations_here * all_comps
                + 2 * slab_hours * width * all_comps
                + 4 * slab_hours * stations_here * width,
                transcendentals=0,
            ),
        )(lax.axis_index("state").reshape(1).astype(jnp.int32), loadings, *pieces, by_hour, *extra)
        fitted_parts.append(fitted)
        smoothed_parts.append(jnp.transpose(gathered, (2, 0, 1)))

    return (
        jnp.concatenate(smoothed_parts, axis=2),
        fitted_parts[-1],
    )


def solution(mesh):
    return jax.shard_map(
        local,
        mesh=mesh,
        in_specs=(
            P(("state", "tm"), None, None),
            P(("state", "tm"), None),
            P("state", None),
            P("tm", "state"),
        ),
        out_specs=(P("state", "tm", None), P("state", "tm", None)),
        check_vma=False,
    )
```
